32 devices in a mesh: groups: 2 (over y), seq: 16 (over z, x, core).
Axes of the slice: x: 2, y: 2, z: 4, core: 2. Of those that a mesh axis runs over, the one named last changes fastest.
Arguments:
- query_rows: bfloat16 [4096, 768], P(('groups', 'seq')), parts along dimension 0, may hold values from -10 to 10
- key_rows: bfloat16 [4096, 768], P(('groups', 'seq')), parts along dimension 0, may hold values from -10 to 10
- value_rows: bfloat16 [4096, 768], P(('groups', 'seq')), parts along dimension 0, may hold values from -6 to 6
- output_grad: bfloat16 [4096, 768], P(('groups', 'seq')), parts along dimension 0, may hold values from -6 to 6
- head_offsets: int32 [3, 12], replicated, may hold values from 0 to 15, as said below
Outputs:
- attended: bfloat16 [4096, 768], P(('groups', 'seq')), parts along dimension 0
- query_grad: bfloat16 [4096, 768], P(('groups', 'seq')), parts along dimension 0
- key_grad: bfloat16 [4096, 768], P(('groups', 'seq')), parts along dimension 0
- value_grad: bfloat16 [4096, 768], P(('groups', 'seq')), parts along dimension 0
The draws below stay inside these ranges and needn't reach their ends.
There are 2 independent parts, one for each index of `groups`. The reference program is written for one: setup_inputs(seed, part) draws one part's arguments, and reference() takes and returns one part's arrays. A program takes and returns all parts, laid end to end along the dimension named above; an argument that names none is the same for every part. Nothing has to cross between parts.
Inputs may be any that keep to these rules, and one draw needn't show every extreme that they name: `head_offsets`: row 0 is all zeros; the entries of row 1 lie below 4, those of row 2 below 16.
All inputs are finite; a program needn't handle non-finite values.
Results may differ from the reference program's by a relative error of at most 0.0084.
Values may be sent and summed in bfloat16 or wider, within the bound.
No kernel may reach another device: no remote copies, remote signals or barrier semaphores. Data moves between devices by JAX's collectives and lax.ppermute only.
A program may use at most 128 MiB of HBM per device.

```python
import math
from functools import reduce
import jax
import jax.numpy as jnp
from jax import lax

HEAD_NUMBER = 12
HEAD_DIM = 64
WIDTH = 768
TOKENS = 2048
DILATION_FIRST = 1
DILATION_SECOND = 4
DILATION_THIRD = 16
SEGMENT_FIRST = 1024
SEGMENT_SECOND = 2048
SEGMENT_THIRD = 2048


def anchored_pair(key):
    query_key, keyrow_key = jax.random.split(key, 2)
    query_out = jnp.clip(jax.random.normal(query_key, (TOKENS, WIDTH), jnp.float32) * 1.5, -7.0, 7.0)
    keyrow_out = jnp.clip(jax.random.normal(keyrow_key, (TOKENS, WIDTH), jnp.float32) * 1.5, -7.0, 7.0)
    return (query_out.astype(jnp.bfloat16), keyrow_out.astype(jnp.bfloat16))


def draw_query_rows(key, part):
    return anchored_pair(jax.random.fold_in(key, 11))[0]


def draw_key_rows(key, part):
    return anchored_pair(jax.random.fold_in(key, 11))[1]


def draw_head_offsets(key, part):
    middle_key, distant_key, pick_key = jax.random.split(jax.random.fold_in(key, 23), 3)
    near_row = jnp.zeros((HEAD_NUMBER,), jnp.int32)
    middle_row = jax.random.randint(middle_key, (HEAD_NUMBER,), 0, DILATION_SECOND, dtype=jnp.int32)
    distant_row = jax.random.randint(distant_key, (HEAD_NUMBER,), 0, DILATION_THIRD, dtype=jnp.int32)
    selected_head = jax.random.randint(pick_key, (), 0, HEAD_NUMBER, dtype=jnp.int32)
    distant_row = jnp.where(jnp.arange(HEAD_NUMBER, dtype=jnp.int32) == selected_head, DILATION_THIRD - 1, distant_row)
    return jnp.stack([near_row, middle_row, distant_row])


def level_of(rng, shape, shards, least, high):
    factor_of = 1.0
    for dim, blocks in shards:
        draws = jax.random.uniform(jax.random.fold_in(jax.random.fold_in(rng, 6), dim), (blocks,), jnp.float32, least / len(shards), high / len(shards))
        factor_of = factor_of * jnp.repeat(jnp.exp(draws), shape[dim] // blocks).reshape((-1,) + (1,) * (len(shape) - 1 - dim))
    return factor_of


def bell_draw(rng, extent, width, most, shards=(), kind=jnp.bfloat16):
    result = jax.random.normal(rng, extent, jnp.float32) * width
    if len(shards) > 0:
        result = level_of(rng, extent, shards, -0.22, 0.18) * result
    return jnp.clip(result, min=-most, max=most).astype(kind)


def setup_inputs(seed: int = 0, part: int = 0) -> dict:
    seeds = jax.random.split(jax.random.key(seed), 6)
    part_keys = jax.random.split(jax.random.fold_in(seeds[5], part), 6)
    query_rows = draw_query_rows(jax.random.fold_in(jax.random.fold_in(seeds[5], part), 71), part)
    key_rows = draw_key_rows(jax.random.fold_in(jax.random.fold_in(seeds[5], part), 71), part)
    value_rows = bell_draw(part_keys[2], (TOKENS, WIDTH), 1.0, 6.0, ((0, 16),))
    output_grad = bell_draw(part_keys[3], (TOKENS, WIDTH), 1.0, 6.0, ((0, 16),))
    head_offsets = draw_head_offsets(jax.random.fold_in(seeds[5], 71), part)
    return dict(query_rows=query_rows, key_rows=key_rows, value_rows=value_rows, output_grad=output_grad, head_offsets=head_offsets)


NEG_FILL = -1e+30

def pick_rows(full_rows, stride, offset):
    grouped = full_rows.reshape(full_rows.shape[0] // stride, stride, full_rows.shape[1])
    chosen = (jnp.arange(stride, dtype=jnp.int32) == offset)[None, :, None]
    return lax.optimization_barrier(jnp.sum(jnp.where(chosen, grouped, jnp.zeros((), full_rows.dtype)), axis=1))

def spread_rows(picked, stride, offset, filler):
    chosen = (jnp.arange(stride, dtype=jnp.int32) == offset)[None, :, None]
    widened = jnp.where(chosen, picked[:, None, :], jnp.asarray(filler, picked.dtype))
    return widened.reshape(picked.shape[0] * stride, picked.shape[1])

def reference(query_rows, key_rows, value_rows, output_grad, head_offsets):
    tokens_all = query_rows.shape[0]
    score_scale = 1.0 / math.sqrt(HEAD_DIM)
    branch_settings = ((SEGMENT_FIRST, DILATION_FIRST), (SEGMENT_SECOND, DILATION_SECOND), (SEGMENT_THIRD, DILATION_THIRD))
    highest = lax.Precision.HIGHEST

    def one_head(head_index):

        def column(array):
            return lax.dynamic_slice_in_dim(array, head_index * HEAD_DIM, HEAD_DIM, 1)
        query_one = column(query_rows)
        key_one = column(key_rows)
        value_one = column(value_rows)
        grad_one = column(output_grad)
        offsets_now = [head_offsets[branch, head_index] for branch in range(3)]

        def grab(array, branch):
            seg_length, stride = branch_settings[branch]
            picked = pick_rows(array, stride, offsets_now[branch]).astype(jnp.float32)
            return picked.reshape(tokens_all // seg_length, seg_length // stride, array.shape[1])

        def place(block, branch, filler):
            flat_block = block.reshape(-1, block.shape[-1])
            return spread_rows(flat_block, branch_settings[branch][1], offsets_now[branch], filler)
        branches = range(3)
        queries = [grab(query_one, branch) for branch in branches]
        keys_sel = [grab(key_one, branch) for branch in branches]
        values_sel = [grab(value_one, branch) for branch in branches]
        grads_sel = [grab(grad_one, branch) for branch in branches]
        scores = [jnp.einsum('sie,sje->sij', queries[branch], keys_sel[branch], precision=highest) * score_scale for branch in branches]
        peak = reduce(jnp.maximum, [place(lax.optimization_barrier(jnp.max(scores[branch], axis=2, keepdims=True)), branch, NEG_FILL) for branch in branches])
        expos = [jnp.exp(scores[branch] - grab(peak, branch)) for branch in branches]
        total = reduce(jnp.add, [place(lax.optimization_barrier(jnp.sum(expos[branch], axis=2, keepdims=True)), branch, 0.0) for branch in branches])
        probs = [expos[branch] / grab(total, branch) for branch in branches]
        weights = [probs[branch].astype(jnp.bfloat16) for branch in branches]
        mixed = reduce(jnp.add, [place(jnp.einsum('sij,sje->sie', weights[branch].astype(jnp.float32), values_sel[branch], precision=highest), branch, 0.0) for branch in branches])
        balance = lax.optimization_barrier(jnp.sum(grad_one.astype(jnp.float32) * mixed, axis=1, keepdims=True))
        flows = [jnp.einsum('sie,sje->sij', grads_sel[branch], values_sel[branch], precision=highest) for branch in branches]
        score_grads = [(probs[branch] * (flows[branch] - grab(balance, branch))).astype(jnp.bfloat16) for branch in branches]
        query_grad = reduce(jnp.add, [place(jnp.einsum('sij,sje->sie', score_grads[branch].astype(jnp.float32), keys_sel[branch], precision=highest), branch, 0.0) for branch in branches]) * score_scale
        key_grad = reduce(jnp.add, [place(jnp.einsum('sij,sie->sje', score_grads[branch].astype(jnp.float32), queries[branch], precision=highest) * score_scale, branch, 0.0) for branch in branches])
        value_grad = reduce(jnp.add, [place(jnp.einsum('sij,sie->sje', weights[branch].astype(jnp.float32), grads_sel[branch], precision=highest), branch, 0.0) for branch in branches])
        return (mixed.astype(jnp.bfloat16), query_grad.astype(jnp.bfloat16), key_grad.astype(jnp.bfloat16), value_grad.astype(jnp.bfloat16))
    stacked = lax.map(one_head, jnp.arange(HEAD_NUMBER, dtype=jnp.int32))

    def merge_heads(array):
        return jnp.transpose(array, (1, 0, 2)).reshape(tokens_all, HEAD_NUMBER * HEAD_DIM)
    return (merge_heads(stacked[0]), merge_heads(stacked[1]), merge_heads(stacked[2]), merge_heads(stacked[3]))
```

```python
import math

import numpy as np
import jax
import jax.numpy as jnp
from jax import lax
from jax.sharding import Mesh, NamedSharding, PartitionSpec as P

LEN_NEAR = 1024
LEN_MID = 4096
LEN_FAR = 16384
DILATION_FIRST = 1
DILATION_SECOND = 4
DILATION_THIRD = 16

NEG_FILL = -1e30


def segment_plan(seq_devices, local_rows):
    tokens_all = seq_devices * local_rows
    seg_lengths = [min(LEN_NEAR, tokens_all), min(LEN_MID, tokens_all), min(LEN_FAR, tokens_all)]
    spans = [seg_length // local_rows for seg_length in seg_lengths]
    distinct = sorted(set(spans))
    factors = []
    previous = 1
    for span in distinct:
        factors.append(span // previous)
        previous = span
    outer = seq_devices // previous
    names = ["q%d" % k for k in range(len(distinct), -1, -1)]
    sizes = [outer] + factors[::-1]
    branch_axes = []
    for span in spans:
        level = distinct.index(span)
        branch_axes.append(tuple(names[len(names) - 1 - level :]))
    return names, sizes, branch_axes


def pick_rows(rows, stride, offsets_row):
    count, heads, dim = rows.shape
    grouped = rows.reshape(count // stride, stride, heads, dim)
    chosen = (jnp.arange(stride, dtype=jnp.int32)[:, None] == offsets_row[None, :])[None, :, :, None]
    return jnp.sum(jnp.where(chosen, grouped, jnp.zeros((), rows.dtype)), axis=1)


def spread_rows(picked, stride, offsets_row):
    count, heads, dim = picked.shape
    chosen = (jnp.arange(stride, dtype=jnp.int32)[:, None] == offsets_row[None, :])[None, :, :, None]
    widened = jnp.where(chosen, picked[:, None], jnp.zeros((), picked.dtype))
    return widened.reshape(count * stride, heads, dim)


def make_per_device(branch_axes):
    strides = [DILATION_FIRST, DILATION_SECOND, DILATION_THIRD]
    groups = []
    for branch, axes in enumerate(branch_axes):
        for entry in groups:
            if entry[0] == axes:
                entry[1].append(branch)
                break
        else:
            groups.append((axes, [branch]))

    def per_device(query_rows, key_rows, value_rows, output_grad, head_offsets):
        local_rows, model_width = query_rows.shape
        head_count = head_offsets.shape[1]
        head_dim = model_width // head_count
        score_scale = 1.0 / math.sqrt(head_dim)
        shape3 = (local_rows, head_count, head_dim)
        query3 = query_rows.reshape(shape3)
        key3 = key_rows.reshape(shape3)
        value3 = value_rows.reshape(shape3)
        grad3 = output_grad.reshape(shape3)
        kv3 = jnp.stack([key3, value3])

        gathered = [None] * 3
        for axes, members in groups:
            parts = [
                jax.vmap(lambda block, b=branch: pick_rows(block, strides[b], head_offsets[b]))(kv3)
                for branch in members
            ]
            counts = [part.shape[1] for part in parts]
            joined = jnp.concatenate(parts, axis=1)
            full = lax.all_gather(joined, axes, axis=1, tiled=False)
            cursor = 0
            for branch, count in zip(members, counts):
                block = full[:, :, cursor : cursor + count]
                gathered[branch] = block.reshape(2, -1, head_count, head_dim)
                cursor += count
        key_counts = [block.shape[1] for block in gathered]
        kv_all = jnp.concatenate(gathered, axis=1)
        key_all = kv_all[0]
        value_all = kv_all[1]

        local_index = jnp.arange(local_rows, dtype=jnp.int32)
        member = [
            (local_index[None, :] % strides[branch]) == head_offsets[branch][:, None]
            for branch in range(3)
        ]
        key_branch = np.concatenate(
            [np.full((count,), branch, np.int32) for branch, count in enumerate(key_counts)]
        )
        valid = None
        for branch in range(3):
            term = member[branch][:, :, None] & jnp.asarray(key_branch == branch)[None, None, :]
            valid = term if valid is None else valid | term

        scores = (
            jnp.einsum("qhe,khe->hqk", query3, key_all, preferred_element_type=jnp.float32)
            * score_scale
        )
        scores = jnp.where(valid, scores, NEG_FILL)
        peak = jnp.max(scores, axis=2, keepdims=True)
        expo = jnp.where(valid, jnp.exp(scores - peak), 0.0)
        total = jnp.sum(expo, axis=2, keepdims=True)
        prob = expo / total
        weight = prob.astype(jnp.bfloat16)
        mixed = jnp.einsum("hqk,khe->qhe", weight, value_all, preferred_element_type=jnp.float32)
        balance = jnp.sum(grad3.astype(jnp.float32) * mixed, axis=2)
        flow = jnp.einsum("qhe,khe->hqk", grad3, value_all, preferred_element_type=jnp.float32)
        score_grad = (prob * (flow - jnp.transpose(balance)[:, :, None])).astype(jnp.bfloat16)
        query_grad = (
            jnp.einsum("hqk,khe->qhe", score_grad, key_all, preferred_element_type=jnp.float32)
            * score_scale
        )
        key_terms = (
            jnp.einsum("hqk,qhe->khe", score_grad, query3, preferred_element_type=jnp.float32)
            * score_scale
        )
        value_terms = jnp.einsum("hqk,qhe->khe", weight, grad3, preferred_element_type=jnp.float32)
        terms = jnp.stack([key_terms, value_terms])

        starts = np.cumsum([0] + key_counts)
        total_grad = None
        for axes, members in groups:
            blocks = [terms[:, starts[branch] : starts[branch + 1]] for branch in members]
            dev_count = 1
            for name in axes:
                dev_count *= lax.axis_size(name)
            shaped = [
                block.reshape(2, dev_count, -1, head_count, head_dim) for block in blocks
            ]
            row_counts = [block.shape[2] for block in shaped]
            joined = jnp.concatenate(shaped, axis=2)
            reduced = lax.psum_scatter(joined, axes, scatter_dimension=1, tiled=False)
            cursor = 0
            for branch, count in zip(members, row_counts):
                part = reduced[:, cursor : cursor + count]
                cursor += count
                spread = jax.vmap(lambda block, b=branch: spread_rows(block, strides[b], head_offsets[b]))(
                    part
                )
                total_grad = spread if total_grad is None else total_grad + spread

        return (
            mixed.astype(jnp.bfloat16).reshape(local_rows, model_width),
            query_grad.astype(jnp.bfloat16).reshape(local_rows, model_width),
            total_grad[0].astype(jnp.bfloat16).reshape(local_rows, model_width),
            total_grad[1].astype(jnp.bfloat16).reshape(local_rows, model_width),
        )

    return per_device


def solution(mesh):
    group_count = mesh.shape["groups"]
    seq_devices = mesh.shape["seq"]

    def run(query_rows, key_rows, value_rows, output_grad, head_offsets):
        local_rows = query_rows.shape[0] // (group_count * seq_devices)
        names, sizes, branch_axes = segment_plan(seq_devices, local_rows)
        split_mesh = Mesh(
            mesh.devices.reshape((group_count,) + tuple(sizes)), ("groups",) + tuple(names)
        )
        row_spec = P(("groups",) + tuple(names), None)
        outs = jax.shard_map(
            make_per_device(branch_axes),
            mesh=split_mesh,
            in_specs=(row_spec, row_spec, row_spec, row_spec, P()),
            out_specs=(row_spec, row_spec, row_spec, row_spec),
            check_vma=False,
        )(query_rows, key_rows, value_rows, output_grad, head_offsets)
        placed = NamedSharding(mesh, P(("groups", "seq"), None))
        return tuple(lax.with_sharding_constraint(out, placed) for out in outs)

    return run
```

```python
import math

import numpy as np
import jax
import jax.numpy as jnp
from jax import lax
from jax.sharding import PartitionSpec as P

LEN_NEAR = 1024
LEN_MID = 4096
LEN_FAR = 16384
DILATION_FIRST = 1
DILATION_SECOND = 4
DILATION_THIRD = 16

NEG_FILL = -1e30


def exchange(block, bit):
    count = lax.axis_size("seq")
    route = [(index, index ^ (1 << bit)) for index in range(count)]
    return lax.ppermute(block, "seq", route)


def pick_rows(rows, stride, offsets_row):
    count = rows.shape[0]
    grouped = rows.reshape((count // stride, stride) + rows.shape[1:])
    chosen = (jnp.arange(stride, dtype=jnp.int32)[:, None] == offsets_row[None, :])[
        None, :, None, :, None
    ]
    return jnp.sum(jnp.where(chosen, grouped, jnp.zeros((), rows.dtype)), axis=1)


def spread_rows(picked, stride, offsets_row):
    count = picked.shape[0]
    chosen = (jnp.arange(stride, dtype=jnp.int32)[:, None] == offsets_row[None, :])[
        None, :, None, :, None
    ]
    widened = jnp.where(chosen, picked[:, None], jnp.zeros((), picked.dtype))
    return widened.reshape((count * stride,) + picked.shape[1:])


def make_per_device(branch_bits):
    strides = [DILATION_FIRST, DILATION_SECOND, DILATION_THIRD]
    top_bits = max(branch_bits)

    def per_device(query_rows, key_rows, value_rows, output_grad, head_offsets):
        local_rows, model_width = query_rows.shape
        head_count = head_offsets.shape[1]
        head_dim = model_width // head_count
        score_scale = 1.0 / math.sqrt(head_dim)
        shape3 = (local_rows, head_count, head_dim)
        query3 = query_rows.reshape(shape3)
        key3 = key_rows.reshape(shape3)
        value3 = value_rows.reshape(shape3)
        grad3 = output_grad.reshape(shape3)
        kv3 = jnp.stack([key3, value3], axis=1)

        buffers = [
            pick_rows(kv3, strides[branch], head_offsets[branch]) for branch in range(3)
        ]
        for bit in reversed(range(top_bits)):
            active = [branch for branch in range(3) if branch_bits[branch] > bit]
            outgoing = jnp.concatenate([buffers[branch].reshape(-1) for branch in active])
            incoming = exchange(outgoing, bit)
            cursor = 0
            for branch in active:
                size = buffers[branch].size
                arrived = incoming[cursor : cursor + size].reshape(buffers[branch].shape)
                cursor += size
                buffers[branch] = jnp.stack([buffers[branch], arrived])
        gathered = [
            buffers[branch].reshape((-1,) + kv3.shape[1:]) for branch in range(3)
        ]
        key_counts = [block.shape[0] for block in gathered]
        kv_all = jnp.concatenate(gathered, axis=0)
        key_all = kv_all[:, 0]
        value_all = kv_all[:, 1]

        local_index = jnp.arange(local_rows, dtype=jnp.int32)
        member = [
            (local_index[None, :] % strides[branch]) == head_offsets[branch][:, None]
            for branch in range(3)
        ]
        key_branch = np.concatenate(
            [np.full((count,), branch, np.int32) for branch, count in enumerate(key_counts)]
        )
        valid = None
        for branch in range(3):
            term = member[branch][:, :, None] & jnp.asarray(key_branch == branch)[None, None, :]
            valid = term if valid is None else valid | term

        scores = (
            jnp.einsum("qhe,khe->hqk", query3, key_all, preferred_element_type=jnp.float32)
            * score_scale
        )
        scores = jnp.where(valid, scores, NEG_FILL)
        peak = jnp.max(scores, axis=2, keepdims=True)
        expo = jnp.where(valid, jnp.exp(scores - peak), 0.0)
        total = jnp.sum(expo, axis=2, keepdims=True)
        prob = expo / total
        weight = prob.astype(jnp.bfloat16)
        mixed = jnp.einsum("hqk,khe->qhe", weight, value_all, preferred_element_type=jnp.float32)
        balance = jnp.sum(grad3.astype(jnp.float32) * mixed, axis=2)
        flow = jnp.einsum("qhe,khe->hqk", grad3, value_all, preferred_element_type=jnp.float32)
        score_grad = (prob * (flow - jnp.transpose(balance)[:, :, None])).astype(jnp.bfloat16)
        query_grad = (
            jnp.einsum("hqk,khe->qhe", score_grad, key_all, preferred_element_type=jnp.float32)
            * score_scale
        )
        key_terms = (
            jnp.einsum("hqk,qhe->khe", score_grad, query3, preferred_element_type=jnp.float32)
            * score_scale
        )
        value_terms = jnp.einsum("hqk,qhe->khe", weight, grad3, preferred_element_type=jnp.float32)
        terms = jnp.stack([key_terms, value_terms], axis=1)

        starts = np.cumsum([0] + key_counts)
        partial = []
        for branch in range(3):
            block = terms[starts[branch] : starts[branch + 1]]
            partial.append(block.reshape((2,) * branch_bits[branch] + (-1,) + terms.shape[1:]))
        for bit in range(top_bits):
            active = [branch for branch in range(3) if branch_bits[branch] > bit]
            outgoing = jnp.concatenate([partial[branch][1].reshape(-1) for branch in active])
            incoming = exchange(outgoing, bit)
            cursor = 0
            for branch in active:
                kept = partial[branch][0]
                size = kept.size
                partial[branch] = kept + incoming[cursor : cursor + size].reshape(kept.shape)
                cursor += size
        total_grad = None
        for branch in range(3):
            spread = spread_rows(partial[branch], strides[branch], head_offsets[branch])
            total_grad = spread if total_grad is None else total_grad + spread

        return (
            mixed.astype(jnp.bfloat16).reshape(local_rows, model_width),
            query_grad.astype(jnp.bfloat16).reshape(local_rows, model_width),
            total_grad[:, 0].astype(jnp.bfloat16).reshape(local_rows, model_width),
            total_grad[:, 1].astype(jnp.bfloat16).reshape(local_rows, model_width),
        )

    return per_device


def solution(mesh):
    group_count = mesh.shape["groups"]
    seq_devices = mesh.shape["seq"]

    def run(query_rows, key_rows, value_rows, output_grad, head_offsets):
        local_rows = query_rows.shape[0] // (group_count * seq_devices)
        tokens_all = seq_devices * local_rows
        seg_lengths = [min(LEN_NEAR, tokens_all), min(LEN_MID, tokens_all), min(LEN_FAR, tokens_all)]
        branch_bits = [(seg_length // local_rows).bit_length() - 1 for seg_length in seg_lengths]
        row_spec = P(("groups", "seq"), None)
        return jax.shard_map(
            make_per_device(branch_bits),
            mesh=mesh,
            in_specs=(row_spec, row_spec, row_spec, row_spec, P()),
            out_specs=(row_spec, row_spec, row_spec, row_spec),
            check_vma=False,
        )(query_rows, key_rows, value_rows, output_grad, head_offsets)

    return run
```

```python
import math

import jax
import jax.numpy as jnp
from jax import lax
from jax.experimental import pallas as pl
from jax.experimental.pallas import tpu as pltpu
from jax.sharding import PartitionSpec as P

LEN_NEAR = 1024
LEN_MID = 4096
LEN_FAR = 16384
DILATION_FIRST = 1
DILATION_SECOND = 4
DILATION_THIRD = 16

NEG_FILL = -1e30
STRIDES = (DILATION_FIRST, DILATION_SECOND, DILATION_THIRD)


def exchange(block, bit):
    count = lax.axis_size("seq")
    route = [(index, index ^ (1 << bit)) for index in range(count)]
    return lax.ppermute(block, "seq", route)


def pick_rows(rows, stride, offsets_row):
    if stride == 1:
        return rows
    pair, count, width = rows.shape
    heads = offsets_row.shape[0]
    grouped = rows.reshape(pair, count // stride, stride, heads, width // heads)
    chosen = (jnp.arange(stride, dtype=jnp.int32)[:, None] == offsets_row[None, :])[
        None, None, :, :, None
    ]
    picked = jnp.sum(jnp.where(chosen, grouped, jnp.zeros((), rows.dtype)), axis=2)
    return picked.reshape(pair, count // stride, width)


def spread_rows(picked, stride, offsets_row):
    if stride == 1:
        return picked
    pair, count, width = picked.shape
    heads = offsets_row.shape[0]
    grouped = picked.reshape(pair, count, 1, heads, width // heads)
    chosen = (jnp.arange(stride, dtype=jnp.int32)[:, None] == offsets_row[None, :])[
        None, None, :, :, None
    ]
    widened = jnp.where(chosen, grouped, jnp.zeros((), picked.dtype))
    return widened.reshape(pair, count * stride, width)


def attention_kernel(key_counts, head_dim, score_scale):
    first_end = key_counts[0]
    second_end = key_counts[0] + key_counts[1]

    def kernel(offsets_ref, query_ref, key_ref, value_ref, grad_ref, out_ref, qgrad_ref, terms_ref):
        pair = pl.program_id(0)
        rows = query_ref.shape[0]
        keys = key_ref.shape[0]
        row_index = lax.broadcasted_iota(jnp.int32, (rows, keys), 0)
        col_index = lax.broadcasted_iota(jnp.int32, (rows, keys), 1)
        heads_per_block = query_ref.shape[1] // head_dim
        for sub in range(heads_per_block):
            head = pair * heads_per_block + sub
            cols = slice(sub * head_dim, (sub + 1) * head_dim)
            query = query_ref[:, cols]
            key = key_ref[:, cols]
            value = value_ref[:, cols]
            grad = grad_ref[:, cols]
            member = [
                (row_index % STRIDES[branch]) == offsets_ref[branch, head] for branch in range(3)
            ]
            in_first = col_index < first_end
            in_third = col_index >= second_end
            in_second = jnp.logical_not(in_first | in_third)
            valid = (in_first & member[0]) | (in_second & member[1]) | (in_third & member[2])
            scores = (
                lax.dot_general(
                    query, key, (((1,), (1,)), ((), ())), preferred_element_type=jnp.float32
                )
                * score_scale
            )
            scores = jnp.where(valid, scores, NEG_FILL)
            peak = jnp.max(scores, axis=1, keepdims=True)
            expo = jnp.where(valid, jnp.exp(scores - peak), 0.0)
            total = jnp.sum(expo, axis=1, keepdims=True)
            prob = expo / total
            weight = prob.astype(jnp.bfloat16)
            mixed = jnp.dot(weight, value, preferred_element_type=jnp.float32)
            out_ref[:, cols] = mixed.astype(out_ref.dtype)
            balance = jnp.sum(grad.astype(jnp.float32) * mixed, axis=1, keepdims=True)
            flow = lax.dot_general(
                grad, value, (((1,), (1,)), ((), ())), preferred_element_type=jnp.float32
            )
            score_grad_wide = prob * (flow - balance)
            score_grad = score_grad_wide.astype(jnp.bfloat16)
            query_grad = jnp.dot(score_grad, key, preferred_element_type=jnp.float32) * score_scale
            qgrad_ref[:, cols] = query_grad.astype(qgrad_ref.dtype)
            key_terms = (
                jnp.dot(
                    jnp.transpose(score_grad_wide).astype(jnp.bfloat16),
                    query,
                    preferred_element_type=jnp.float32,
                )
                * score_scale
            )
            value_terms = jnp.dot(
                jnp.transpose(prob).astype(jnp.bfloat16), grad, preferred_element_type=jnp.float32
            )
            terms_ref[0, :, cols] = key_terms
            terms_ref[1, :, cols] = value_terms

    return kernel


def make_per_device(branch_bits):
    top_bits = max(branch_bits)

    def per_device(query_rows, key_rows, value_rows, output_grad, head_offsets):
        local_rows, model_width = query_rows.shape
        head_count = head_offsets.shape[1]
        head_dim = model_width // head_count
        score_scale = 1.0 / math.sqrt(head_dim)
        kv_rows = jnp.stack([key_rows, value_rows])

        buffers = [
            pick_rows(kv_rows, STRIDES[branch], head_offsets[branch]) for branch in range(3)
        ]
        for bit in reversed(range(top_bits)):
            active = [branch for branch in range(3) if branch_bits[branch] > bit]
            outgoing = jnp.concatenate([buffers[branch].reshape(-1) for branch in active])
            incoming = exchange(outgoing, bit)
            cursor = 0
            for branch in active:
                size = buffers[branch].size
                arrived = incoming[cursor : cursor + size].reshape(buffers[branch].shape)
                cursor += size
                buffers[branch] = jnp.stack([buffers[branch], arrived], axis=1)
        gathered = [
            buffers[branch].reshape(2, -1, model_width) for branch in range(3)
        ]
        key_counts = [block.shape[1] for block in gathered]
        kv_all = jnp.concatenate(gathered, axis=1)
        key_total = kv_all.shape[1]

        block_width = 128 if (128 % head_dim == 0 and model_width % 128 == 0) else model_width
        pairs = model_width // block_width
        row_block = pl.BlockSpec((local_rows, block_width), lambda p, offs: (0, p))
        key_block = pl.BlockSpec((key_total, block_width), lambda p, offs: (0, p))
        attended, query_grad, terms = pl.pallas_call(
            attention_kernel(key_counts, head_dim, score_scale),
            out_shape=(
                jax.ShapeDtypeStruct((local_rows, model_width), jnp.bfloat16),
                jax.ShapeDtypeStruct((local_rows, model_width), jnp.bfloat16),
                jax.ShapeDtypeStruct((2, key_total, model_width), jnp.float32),
            ),
            grid_spec=pltpu.PrefetchScalarGridSpec(
                num_scalar_prefetch=1,
                grid=(pairs,),
                in_specs=[row_block, key_block, key_block, row_block],
                out_specs=[
                    row_block,
                    row_block,
                    pl.BlockSpec((2, key_total, block_width), lambda p, offs: (0, 0, p)),
                ],
            ),
            compiler_params=pltpu.CompilerParams(vmem_limit_bytes=100 * 1024 * 1024),
        )(head_offsets, query_rows, kv_all[0], kv_all[1], output_grad)

        starts = [0, key_counts[0], key_counts[0] + key_counts[1], key_total]
        partial = []
        for branch in range(3):
            block = terms[:, starts[branch] : starts[branch + 1]]
            partial.append(block.reshape((2,) + (2,) * branch_bits[branch] + (-1, model_width)))
        for bit in range(top_bits):
            active = [branch for branch in range(3) if branch_bits[branch] > bit]
            outgoing = jnp.concatenate([partial[branch][:, 1].reshape(-1) for branch in active])
            incoming = exchange(outgoing, bit)
            cursor = 0
            for branch in active:
                kept = partial[branch][:, 0]
                size = kept.size
                partial[branch] = kept + incoming[cursor : cursor + size].reshape(kept.shape)
                cursor += size
        total_grad = None
        for branch in range(3):
            spread = spread_rows(partial[branch], STRIDES[branch], head_offsets[branch])
            total_grad = spread if total_grad is None else total_grad + spread

        return (
            attended,
            query_grad,
            total_grad[0].astype(jnp.bfloat16),
            total_grad[1].astype(jnp.bfloat16),
        )

    return per_device


def solution(mesh):
    group_count = mesh.shape["groups"]
    seq_devices = mesh.shape["seq"]

    def run(query_rows, key_rows, value_rows, output_grad, head_offsets):
        local_rows = query_rows.shape[0] // (group_count * seq_devices)
        tokens_all = seq_devices * local_rows
        seg_lengths = [min(LEN_NEAR, tokens_all), min(LEN_MID, tokens_all), min(LEN_FAR, tokens_all)]
        branch_bits = [(seg_length // local_rows).bit_length() - 1 for seg_length in seg_lengths]
        row_spec = P(("groups", "seq"), None)
        return jax.shard_map(
            make_per_device(branch_bits),
            mesh=mesh,
            in_specs=(row_spec, row_spec, row_spec, row_spec, P()),
            out_specs=(row_spec, row_spec, row_spec, row_spec),
            check_vma=False,
        )(query_rows, key_rows, value_rows, output_grad, head_offsets)

    return run
```

```python
import math

import jax
import jax.numpy as jnp
from jax import lax
from jax.experimental import pallas as pl
from jax.experimental.pallas import tpu as pltpu
from jax.sharding import PartitionSpec as P

LEN_NEAR = 1024
LEN_MID = 4096
LEN_FAR = 16384
DILATION_FIRST = 1
DILATION_SECOND = 4
DILATION_THIRD = 16

NEG_FILL = -1e30
STRIDES = (DILATION_FIRST, DILATION_SECOND, DILATION_THIRD)


def exchange(block, bit):
    count = lax.axis_size("seq")
    route = [(index, index ^ (1 << bit)) for index in range(count)]
    return lax.ppermute(block, "seq", route)


def pick_rows(rows, stride, offsets_row):
    if stride == 1:
        return rows
    pair, count, width = rows.shape
    heads = offsets_row.shape[0]
    grouped = rows.reshape(pair, count // stride, stride, heads, width // heads)
    chosen = (jnp.arange(stride, dtype=jnp.int32)[:, None] == offsets_row[None, :])[
        None, None, :, :, None
    ]
    picked = jnp.sum(jnp.where(chosen, grouped, jnp.zeros((), rows.dtype)), axis=2)
    return picked.reshape(pair, count // stride, width)


def spread_rows(picked, stride, offsets_row):
    if stride == 1:
        return picked
    pair, count, width = picked.shape
    heads = offsets_row.shape[0]
    grouped = picked.reshape(pair, count, 1, heads, width // heads)
    chosen = (jnp.arange(stride, dtype=jnp.int32)[:, None] == offsets_row[None, :])[
        None, None, :, :, None
    ]
    widened = jnp.where(chosen, grouped, jnp.zeros((), picked.dtype))
    return widened.reshape(pair, count * stride, width)


def attention_kernel(key_counts, head_dim, score_scale):
    first_end = key_counts[0]
    second_end = key_counts[0] + key_counts[1]

    def kernel(offsets_ref, query_ref, key_ref, value_ref, grad_ref, out_ref, qgrad_ref, terms_ref):
        pair = pl.program_id(0)
        rows = query_ref.shape[0]
        keys = key_ref.shape[0]
        row_index = lax.broadcasted_iota(jnp.int32, (rows, keys), 0)
        col_index = lax.broadcasted_iota(jnp.int32, (rows, keys), 1)
        heads_per_block = query_ref.shape[1] // head_dim
        for sub in range(heads_per_block):
            head = pair * heads_per_block + sub
            cols = slice(sub * head_dim, (sub + 1) * head_dim)
            query = query_ref[:, cols]
            key = key_ref[:, cols]
            value = value_ref[:, cols]
            grad = grad_ref[:, cols]
            member = [
                (row_index % STRIDES[branch]) == offsets_ref[branch, head] for branch in range(3)
            ]
            in_first = col_index < first_end
            in_third = col_index >= second_end
            in_second = jnp.logical_not(in_first | in_third)
            valid = (in_first & member[0]) | (in_second & member[1]) | (in_third & member[2])
            scores = (
                lax.dot_general(
                    query, key, (((1,), (1,)), ((), ())), preferred_element_type=jnp.float32
                )
                * score_scale
            )
            scores = jnp.where(valid, scores, NEG_FILL)
            peak = jnp.max(scores, axis=1, keepdims=True)
            expo = jnp.where(valid, jnp.exp(scores - peak), 0.0)
            total = jnp.sum(expo, axis=1, keepdims=True)
            prob = expo / total
            weight = prob.astype(jnp.bfloat16)
            mixed = jnp.dot(weight, value, preferred_element_type=jnp.float32)
            out_ref[:, cols] = mixed.astype(out_ref.dtype)
            balance = jnp.sum(grad.astype(jnp.float32) * mixed, axis=1, keepdims=True)
            flow = lax.dot_general(
                grad, value, (((1,), (1,)), ((), ())), preferred_element_type=jnp.float32
            )
            score_grad_wide = prob * (flow - balance)
            score_grad = score_grad_wide.astype(jnp.bfloat16)
            query_grad = jnp.dot(score_grad, key, preferred_element_type=jnp.float32) * score_scale
            qgrad_ref[:, cols] = query_grad.astype(qgrad_ref.dtype)
            key_terms = (
                jnp.dot(
                    jnp.transpose(score_grad_wide).astype(jnp.bfloat16),
                    query,
                    preferred_element_type=jnp.float32,
                )
                * score_scale
            )
            value_terms = jnp.dot(
                jnp.transpose(prob).astype(jnp.bfloat16), grad, preferred_element_type=jnp.float32
            )
            terms_ref[0, :, cols] = key_terms
            terms_ref[1, :, cols] = value_terms

    return kernel


def make_per_device(branch_bits):
    top_bits = max(branch_bits)

    def per_device(query_rows, key_rows, value_rows, output_grad, head_offsets):
        local_rows, model_width = query_rows.shape
        head_count = head_offsets.shape[1]
        head_dim = model_width // head_count
        score_scale = 1.0 / math.sqrt(head_dim)
        kv_rows = jnp.stack([key_rows, value_rows])

        buffers = [
            pick_rows(kv_rows, STRIDES[branch], head_offsets[branch]) for branch in range(3)
        ]
        for bit in reversed(range(top_bits)):
            active = [branch for branch in range(3) if branch_bits[branch] > bit]
            outgoing = jnp.concatenate([buffers[branch].reshape(-1) for branch in active])
            incoming = exchange(outgoing, bit)
            cursor = 0
            for branch in active:
                size = buffers[branch].size
                arrived = incoming[cursor : cursor + size].reshape(buffers[branch].shape)
                cursor += size
                buffers[branch] = jnp.stack([buffers[branch], arrived], axis=1)
        gathered = [
            buffers[branch].reshape(2, -1, model_width) for branch in range(3)
        ]
        key_counts = [block.shape[1] for block in gathered]
        kv_all = jnp.concatenate(gathered, axis=1)
        key_total = kv_all.shape[1]

        block_width = 128 if (128 % head_dim == 0 and model_width % 128 == 0) else model_width
        pairs = model_width // block_width
        row_block = pl.BlockSpec((local_rows, block_width), lambda p, offs: (0, p))
        key_block = pl.BlockSpec((key_total, block_width), lambda p, offs: (0, p))
        attended, query_grad, terms = pl.pallas_call(
            attention_kernel(key_counts, head_dim, score_scale),
            out_shape=(
                jax.ShapeDtypeStruct((local_rows, model_width), jnp.bfloat16),
                jax.ShapeDtypeStruct((local_rows, model_width), jnp.bfloat16),
                jax.ShapeDtypeStruct((2, key_total, model_width), jnp.float32),
            ),
            grid_spec=pltpu.PrefetchScalarGridSpec(
                num_scalar_prefetch=1,
                grid=(pairs,),
                in_specs=[row_block, key_block, key_block, row_block],
                out_specs=[
                    row_block,
                    row_block,
                    pl.BlockSpec((2, key_total, block_width), lambda p, offs: (0, 0, p)),
                ],
            ),
            compiler_params=pltpu.CompilerParams(vmem_limit_bytes=100 * 1024 * 1024),
        )(head_offsets, query_rows, kv_all[0], kv_all[1], output_grad)

        starts = [0, key_counts[0], key_counts[0] + key_counts[1], key_total]
        partial = []
        for branch in range(3):
            block = terms[:, starts[branch] : starts[branch + 1]]
            partial.append(block.reshape((2,) + (2,) * branch_bits[branch] + (-1, model_width)))
        for bit in range(top_bits):
            active = [branch for branch in range(3) if branch_bits[branch] > bit]
            outgoing = jnp.concatenate(
                [partial[branch][:, 1].reshape(-1).astype(jnp.bfloat16) for branch in active]
            )
            incoming = exchange(outgoing, bit).astype(jnp.float32)
            cursor = 0
            for branch in active:
                kept = partial[branch][:, 0]
                size = kept.size
                partial[branch] = kept + incoming[cursor : cursor + size].reshape(kept.shape)
                cursor += size
        total_grad = None
        for branch in range(3):
            spread = spread_rows(partial[branch], STRIDES[branch], head_offsets[branch])
            total_grad = spread if total_grad is None else total_grad + spread

        return (
            attended,
            query_grad,
            total_grad[0].astype(jnp.bfloat16),
            total_grad[1].astype(jnp.bfloat16),
        )

    return per_device


def solution(mesh):
    group_count = mesh.shape["groups"]
    seq_devices = mesh.shape["seq"]

    def run(query_rows, key_rows, value_rows, output_grad, head_offsets):
        local_rows = query_rows.shape[0] // (group_count * seq_devices)
        tokens_all = seq_devices * local_rows
        seg_lengths = [min(LEN_NEAR, tokens_all), min(LEN_MID, tokens_all), min(LEN_FAR, tokens_all)]
        branch_bits = [(seg_length // local_rows).bit_length() - 1 for seg_length in seg_lengths]
        row_spec = P(("groups", "seq"), None)
        return jax.shard_map(
            make_per_device(branch_bits),
            mesh=mesh,
            in_specs=(row_spec, row_spec, row_spec, row_spec, P()),
            out_specs=(row_spec, row_spec, row_spec, row_spec),
            check_vma=False,
        )(query_rows, key_rows, value_rows, output_grad, head_offsets)

    return run
```

```python
import math

import jax
import jax.numpy as jnp
from jax import lax
from jax.experimental import pallas as pl
from jax.experimental.pallas import tpu as pltpu
from jax.sharding import PartitionSpec as P

LEN_NEAR = 1024
LEN_MID = 4096
LEN_FAR = 16384
DILATION_FIRST = 1
DILATION_SECOND = 4
DILATION_THIRD = 16

NEG_FILL = -1e30
STRIDES = (DILATION_FIRST, DILATION_SECOND, DILATION_THIRD)


def exchange(block, bit):
    count = lax.axis_size("seq")
    route = [(index, index ^ (1 << bit)) for index in range(count)]
    return lax.ppermute(block, "seq", route)


def pick_rows(rows, stride, offsets_row):
    if stride == 1:
        return rows
    pair, count, width = rows.shape
    heads = offsets_row.shape[0]
    grouped = rows.reshape(pair, count // stride, stride, heads, width // heads)
    chosen = (jnp.arange(stride, dtype=jnp.int32)[:, None] == offsets_row[None, :])[
        None, None, :, :, None
    ]
    picked = jnp.sum(jnp.where(chosen, grouped, jnp.zeros((), rows.dtype)), axis=2)
    return picked.reshape(pair, count // stride, width)


def spread_rows(picked, stride, offsets_row):
    if stride == 1:
        return picked
    pair, count, width = picked.shape
    heads = offsets_row.shape[0]
    grouped = picked.reshape(pair, count, 1, heads, width // heads)
    chosen = (jnp.arange(stride, dtype=jnp.int32)[:, None] == offsets_row[None, :])[
        None, None, :, :, None
    ]
    widened = jnp.where(chosen, grouped, jnp.zeros((), picked.dtype))
    return widened.reshape(pair, count * stride, width)


def attention_kernel(head_dim, score_scale):
    def kernel(offsets_ref, query_ref, grad_ref, *refs):
        kv_refs = refs[:3]
        out_ref, qgrad_ref = refs[3:5]
        term_refs = refs[5:]
        pair = pl.program_id(0)
        rows = query_ref.shape[0]
        heads_per_block = query_ref.shape[1] // head_dim
        for sub in range(heads_per_block):
            head = pair * heads_per_block + sub
            cols = slice(sub * head_dim, (sub + 1) * head_dim)
            query = query_ref[:, cols]
            grad = grad_ref[:, cols]
            keys = [kv_ref[0, :, cols] for kv_ref in kv_refs]
            values = [kv_ref[1, :, cols] for kv_ref in kv_refs]
            members = []
            scores = []
            for branch in range(3):
                block = (
                    lax.dot_general(
                        query, keys[branch], (((1,), (1,)), ((), ())),
                        preferred_element_type=jnp.float32,
                    )
                    * score_scale
                )
                if STRIDES[branch] == 1:
                    member = None
                else:
                    row_index = lax.broadcasted_iota(jnp.int32, block.shape, 0)
                    member = (row_index % STRIDES[branch]) == offsets_ref[branch, head]
                    block = jnp.where(member, block, NEG_FILL)
                members.append(member)
                scores.append(block)
            peak = jnp.max(scores[0], axis=1, keepdims=True)
            for branch in range(1, 3):
                peak = jnp.maximum(peak, jnp.max(scores[branch], axis=1, keepdims=True))
            expos = []
            for branch in range(3):
                block = jnp.exp(scores[branch] - peak)
                if members[branch] is not None:
                    block = jnp.where(members[branch], block, 0.0)
                expos.append(block)
            total = jnp.sum(expos[0], axis=1, keepdims=True)
            for branch in range(1, 3):
                total = total + jnp.sum(expos[branch], axis=1, keepdims=True)
            probs = [block / total for block in expos]
            weights = [block.astype(jnp.bfloat16) for block in probs]
            mixed = jnp.dot(weights[0], values[0], preferred_element_type=jnp.float32)
            for branch in range(1, 3):
                mixed = mixed + jnp.dot(
                    weights[branch], values[branch], preferred_element_type=jnp.float32
                )
            out_ref[:, cols] = mixed.astype(out_ref.dtype)
            balance = jnp.sum(grad.astype(jnp.float32) * mixed, axis=1, keepdims=True)
            query_grad = None
            for branch in range(3):
                flow = lax.dot_general(
                    grad, values[branch], (((1,), (1,)), ((), ())),
                    preferred_element_type=jnp.float32,
                )
                score_grad = probs[branch] * (flow - balance)
                piece = jnp.dot(
                    score_grad.astype(jnp.bfloat16), keys[branch],
                    preferred_element_type=jnp.float32,
                )
                query_grad = piece if query_grad is None else query_grad + piece
                key_terms = (
                    jnp.dot(
                        jnp.transpose(score_grad).astype(jnp.bfloat16),
                        query,
                        preferred_element_type=jnp.float32,
                    )
                    * score_scale
                )
                value_terms = jnp.dot(
                    jnp.transpose(probs[branch]).astype(jnp.bfloat16),
                    grad,
                    preferred_element_type=jnp.float32,
                )
                term_refs[branch][0, :, cols] = key_terms
                term_refs[branch][1, :, cols] = value_terms
            qgrad_ref[:, cols] = (query_grad * score_scale).astype(qgrad_ref.dtype)

    return kernel


def make_per_device(branch_bits):
    top_bits = max(branch_bits)

    def per_device(query_rows, key_rows, value_rows, output_grad, head_offsets):
        local_rows, model_width = query_rows.shape
        head_count = head_offsets.shape[1]
        head_dim = model_width // head_count
        score_scale = 1.0 / math.sqrt(head_dim)
        kv_rows = jnp.stack([key_rows, value_rows])

        buffers = [
            pick_rows(kv_rows, STRIDES[branch], head_offsets[branch]) for branch in range(3)
        ]
        for bit in reversed(range(top_bits)):
            active = [branch for branch in range(3) if branch_bits[branch] > bit]
            outgoing = jnp.concatenate(
                [buffers[branch].reshape(-1, model_width) for branch in active]
            )
            incoming = exchange(outgoing, bit)
            cursor = 0
            for branch in active:
                count = buffers[branch].size // model_width
                arrived = incoming[cursor : cursor + count].reshape(buffers[branch].shape)
                cursor += count
                buffers[branch] = jnp.stack([buffers[branch], arrived], axis=1)
        gathered = [buffers[branch].reshape(2, -1, model_width) for branch in range(3)]

        block_width = 128 if (128 % head_dim == 0 and model_width % 128 == 0) else model_width
        pairs = model_width // block_width
        row_block = pl.BlockSpec((local_rows, block_width), lambda p, offs: (0, p))
        kv_blocks = [
            pl.BlockSpec((2, block.shape[1], block_width), lambda p, offs: (0, 0, p))
            for block in gathered
        ]
        outs = pl.pallas_call(
            attention_kernel(head_dim, score_scale),
            out_shape=(
                jax.ShapeDtypeStruct((local_rows, model_width), jnp.bfloat16),
                jax.ShapeDtypeStruct((local_rows, model_width), jnp.bfloat16),
            )
            + tuple(jax.ShapeDtypeStruct(block.shape, jnp.float32) for block in gathered),
            grid_spec=pltpu.PrefetchScalarGridSpec(
                num_scalar_prefetch=1,
                grid=(pairs,),
                in_specs=[row_block, row_block] + kv_blocks,
                out_specs=[row_block, row_block] + kv_blocks,
            ),
            compiler_params=pltpu.CompilerParams(vmem_limit_bytes=100 * 1024 * 1024),
        )(head_offsets, query_rows, output_grad, *gathered)
        attended, query_grad = outs[:2]
        terms = outs[2:]

        partial = [
            terms[branch].reshape((2,) + (2,) * branch_bits[branch] + (-1, model_width))
            for branch in range(3)
        ]
        for bit in range(top_bits):
            active = [branch for branch in range(3) if branch_bits[branch] > bit]
            outgoing = jnp.concatenate(
                [
                    partial[branch][:, 1].reshape(-1, model_width).astype(jnp.bfloat16)
                    for branch in active
                ]
            )
            incoming = exchange(outgoing, bit).astype(jnp.float32)
            cursor = 0
            for branch in active:
                kept = partial[branch][:, 0]
                count = kept.size // model_width
                partial[branch] = kept + incoming[cursor : cursor + count].reshape(kept.shape)
                cursor += count
        total_grad = None
        for branch in range(3):
            spread = spread_rows(partial[branch], STRIDES[branch], head_offsets[branch])
            total_grad = spread if total_grad is None else total_grad + spread

        return (
            attended,
            query_grad,
            total_grad[0].astype(jnp.bfloat16),
            total_grad[1].astype(jnp.bfloat16),
        )

    return per_device


def solution(mesh):
    group_count = mesh.shape["groups"]
    seq_devices = mesh.shape["seq"]

    def run(query_rows, key_rows, value_rows, output_grad, head_offsets):
        local_rows = query_rows.shape[0] // (group_count * seq_devices)
        tokens_all = seq_devices * local_rows
        seg_lengths = [min(LEN_NEAR, tokens_all), min(LEN_MID, tokens_all), min(LEN_FAR, tokens_all)]
        branch_bits = [(seg_length // local_rows).bit_length() - 1 for seg_length in seg_lengths]
        row_spec = P(("groups", "seq"), None)
        return jax.shard_map(
            make_per_device(branch_bits),
            mesh=mesh,
            in_specs=(row_spec, row_spec, row_spec, row_spec, P()),
            out_specs=(row_spec, row_spec, row_spec, row_spec),
            check_vma=False,
        )(query_rows, key_rows, value_rows, output_grad, head_offsets)

    return run
```

```python
import math

import jax
import jax.numpy as jnp
from jax import lax
from jax.experimental import pallas as pl
from jax.experimental.pallas import tpu as pltpu
from jax.sharding import PartitionSpec as P

LEN_NEAR = 1024
LEN_MID = 4096
LEN_FAR = 16384
DILATION_FIRST = 1
DILATION_SECOND = 4
DILATION_THIRD = 16

NEG_FILL = -1e30
STRIDES = (DILATION_FIRST, DILATION_SECOND, DILATION_THIRD)


def exchange(block, bit):
    count = lax.axis_size("seq")
    route = [(index, index ^ (1 << bit)) for index in range(count)]
    return lax.ppermute(block, "seq", route)


def pick_rows(rows, stride, offsets_row):
    if stride == 1:
        return rows
    pair, count, width = rows.shape
    heads = offsets_row.shape[0]
    grouped = rows.reshape(pair, count // stride, stride, heads, width // heads)
    chosen = (jnp.arange(stride, dtype=jnp.int32)[:, None] == offsets_row[None, :])[
        None, None, :, :, None
    ]
    picked = jnp.sum(jnp.where(chosen, grouped, jnp.zeros((), rows.dtype)), axis=2)
    return picked.reshape(pair, count // stride, width)


def spread_rows(picked, stride, offsets_row):
    if stride == 1:
        return picked
    pair, count, width = picked.shape
    heads = offsets_row.shape[0]
    grouped = picked.reshape(pair, count, 1, heads, width // heads)
    chosen = (jnp.arange(stride, dtype=jnp.int32)[:, None] == offsets_row[None, :])[
        None, None, :, :, None
    ]
    widened = jnp.where(chosen, grouped, jnp.zeros((), picked.dtype))
    return widened.reshape(pair, count * stride, width)


def attention_kernel(head_dim, score_scale, head_base):
    def kernel(offsets_ref, query_ref, grad_ref, *refs):
        kv_refs = refs[:3]
        out_ref, qgrad_ref = refs[3:5]
        term_refs = refs[5:]
        pair = pl.program_id(0)
        rows = query_ref.shape[0]
        heads_per_block = query_ref.shape[1] // head_dim
        for sub in range(heads_per_block):
            head = head_base + pair * heads_per_block + sub
            cols = slice(sub * head_dim, (sub + 1) * head_dim)
            query = query_ref[:, cols]
            grad = grad_ref[:, cols]
            keys = [kv_ref[0, :, cols] for kv_ref in kv_refs]
            values = [kv_ref[1, :, cols] for kv_ref in kv_refs]
            members = []
            scores = []
            for branch in range(3):
                block = (
                    lax.dot_general(
                        query, keys[branch], (((1,), (1,)), ((), ())),
                        preferred_element_type=jnp.float32,
                    )
                    * score_scale
                )
                if STRIDES[branch] == 1:
                    member = None
                else:
                    row_index = lax.broadcasted_iota(jnp.int32, block.shape, 0)
                    member = (row_index % STRIDES[branch]) == offsets_ref[branch, head]
                    block = jnp.where(member, block, NEG_FILL)
                members.append(member)
                scores.append(block)
            peak = jnp.max(scores[0], axis=1, keepdims=True)
            for branch in range(1, 3):
                peak = jnp.maximum(peak, jnp.max(scores[branch], axis=1, keepdims=True))
            expos = []
            for branch in range(3):
                block = jnp.exp(scores[branch] - peak)
                if members[branch] is not None:
                    block = jnp.where(members[branch], block, 0.0)
                expos.append(block)
            total = jnp.sum(expos[0], axis=1, keepdims=True)
            for branch in range(1, 3):
                total = total + jnp.sum(expos[branch], axis=1, keepdims=True)
            probs = [block / total for block in expos]
            weights = [block.astype(jnp.bfloat16) for block in probs]
            mixed = jnp.dot(weights[0], values[0], preferred_element_type=jnp.float32)
            for branch in range(1, 3):
                mixed = mixed + jnp.dot(
                    weights[branch], values[branch], preferred_element_type=jnp.float32
                )
            out_ref[:, cols] = mixed.astype(out_ref.dtype)
            balance = jnp.sum(grad.astype(jnp.float32) * mixed, axis=1, keepdims=True)
            query_grad = None
            for branch in range(3):
                flow = lax.dot_general(
                    grad, values[branch], (((1,), (1,)), ((), ())),
                    preferred_element_type=jnp.float32,
                )
                score_grad = probs[branch] * (flow - balance)
                piece = jnp.dot(
                    score_grad.astype(jnp.bfloat16), keys[branch],
                    preferred_element_type=jnp.float32,
                )
                query_grad = piece if query_grad is None else query_grad + piece
                key_terms = (
                    jnp.dot(
                        jnp.transpose(score_grad).astype(jnp.bfloat16),
                        query,
                        preferred_element_type=jnp.float32,
                    )
                    * score_scale
                )
                value_terms = jnp.dot(
                    jnp.transpose(probs[branch]).astype(jnp.bfloat16),
                    grad,
                    preferred_element_type=jnp.float32,
                )
                term_refs[branch][0, :, cols] = key_terms
                term_refs[branch][1, :, cols] = value_terms
            qgrad_ref[:, cols] = (query_grad * score_scale).astype(qgrad_ref.dtype)

    return kernel


def gather_order(top_bits, swapped):
    order = list(reversed(range(top_bits)))
    if swapped and top_bits >= 3:
        first, second = order.index(1), order.index(2)
        order[first], order[second] = order[second], order[first]
    return order


def make_per_device(branch_bits):
    top_bits = max(branch_bits)

    def per_device(query_rows, key_rows, value_rows, output_grad, head_offsets):
        local_rows, model_width = query_rows.shape
        head_count = head_offsets.shape[1]
        head_dim = model_width // head_count
        score_scale = 1.0 / math.sqrt(head_dim)
        kv_rows = jnp.stack([key_rows, value_rows])
        picked = [
            pick_rows(kv_rows, STRIDES[branch], head_offsets[branch]) for branch in range(3)
        ]
        block_width = 128 if (128 % head_dim == 0 and model_width % 128 == 0) else model_width
        halves = 2 if model_width % (2 * block_width) == 0 else 1
        half_width = model_width // halves
        heads_per_half = head_count // halves

        gathered_halves = []
        layouts = []
        for half in range(halves):
            cols = slice(half * half_width, (half + 1) * half_width)
            buffers = [block[:, :, cols] for block in picked]
            axis_bits = [[] for _ in range(3)]
            for bit in gather_order(top_bits, half == 1):
                active = [branch for branch in range(3) if branch_bits[branch] > bit]
                outgoing = jnp.concatenate(
                    [buffers[branch].reshape(-1, half_width) for branch in active]
                )
                incoming = exchange(outgoing, bit)
                cursor = 0
                for branch in active:
                    count = buffers[branch].size // half_width
                    arrived = incoming[cursor : cursor + count].reshape(buffers[branch].shape)
                    cursor += count
                    buffers[branch] = jnp.stack([buffers[branch], arrived], axis=1)
                    axis_bits[branch].insert(0, bit)
            gathered_halves.append([buffers[branch].reshape(2, -1, half_width) for branch in range(3)])
            layouts.append(axis_bits)

        results = []
        for half in range(halves):
            gathered = gathered_halves[half]
            cols = slice(half * half_width, (half + 1) * half_width)
            pairs = half_width // block_width
            row_block = pl.BlockSpec((local_rows, block_width), lambda p, offs: (0, p))
            kv_blocks = [
                pl.BlockSpec((2, block.shape[1], block_width), lambda p, offs: (0, 0, p))
                for block in gathered
            ]
            outs = pl.pallas_call(
                attention_kernel(head_dim, score_scale, half * heads_per_half),
                out_shape=(
                    jax.ShapeDtypeStruct((local_rows, half_width), jnp.bfloat16),
                    jax.ShapeDtypeStruct((local_rows, half_width), jnp.bfloat16),
                )
                + tuple(jax.ShapeDtypeStruct(block.shape, jnp.float32) for block in gathered),
                grid_spec=pltpu.PrefetchScalarGridSpec(
                    num_scalar_prefetch=1,
                    grid=(pairs,),
                    in_specs=[row_block, row_block] + kv_blocks,
                    out_specs=[row_block, row_block] + kv_blocks,
                ),
                compiler_params=pltpu.CompilerParams(vmem_limit_bytes=100 * 1024 * 1024),
            )(head_offsets, query_rows[:, cols], output_grad[:, cols], *gathered)
            attended, query_grad = outs[:2]
            terms = outs[2:]

            axis_bits = [list(bits) for bits in layouts[half]]
            partial = [
                terms[branch].reshape((2,) + (2,) * branch_bits[branch] + (-1, half_width))
                for branch in range(3)
            ]
            for bit in reversed(gather_order(top_bits, half == 1)):
                active = [branch for branch in range(3) if branch_bits[branch] > bit]
                places = {branch: 1 + axis_bits[branch].index(bit) for branch in active}
                outgoing = jnp.concatenate(
                    [
                        lax.index_in_dim(partial[branch], 1, places[branch], keepdims=False)
                        .reshape(-1, half_width)
                        .astype(jnp.bfloat16)
                        for branch in active
                    ]
                )
                incoming = exchange(outgoing, bit).astype(jnp.float32)
                cursor = 0
                for branch in active:
                    kept = lax.index_in_dim(partial[branch], 0, places[branch], keepdims=False)
                    count = kept.size // half_width
                    partial[branch] = kept + incoming[cursor : cursor + count].reshape(kept.shape)
                    cursor += count
                    axis_bits[branch].remove(bit)
            offsets_half = head_offsets[:, half * heads_per_half : (half + 1) * heads_per_half]
            total_grad = None
            for branch in range(3):
                spread = spread_rows(partial[branch], STRIDES[branch], offsets_half[branch])
                total_grad = spread if total_grad is None else total_grad + spread
            results.append((attended, query_grad, total_grad[0], total_grad[1]))

        return tuple(
            jnp.concatenate([result[index] for result in results], axis=1).astype(jnp.bfloat16)
            for index in range(4)
        )

    return per_device


def solution(mesh):
    group_count = mesh.shape["groups"]
    seq_devices = mesh.shape["seq"]

    def run(query_rows, key_rows, value_rows, output_grad, head_offsets):
        local_rows = query_rows.shape[0] // (group_count * seq_devices)
        tokens_all = seq_devices * local_rows
        seg_lengths = [min(LEN_NEAR, tokens_all), min(LEN_MID, tokens_all), min(LEN_FAR, tokens_all)]
        branch_bits = [(seg_length // local_rows).bit_length() - 1 for seg_length in seg_lengths]
        row_spec = P(("groups", "seq"), None)
        return jax.shard_map(
            make_per_device(branch_bits),
            mesh=mesh,
            in_specs=(row_spec, row_spec, row_spec, row_spec, P()),
            out_specs=(row_spec, row_spec, row_spec, row_spec),
            check_vma=False,
        )(query_rows, key_rows, value_rows, output_grad, head_offsets)

    return run
```

```python
import math

import jax
import jax.numpy as jnp
from jax import lax
from jax.experimental import pallas as pl
from jax.experimental.pallas import tpu as pltpu
from jax.sharding import PartitionSpec as P

LEN_NEAR = 1024
LEN_MID = 4096
LEN_FAR = 16384
DILATION_FIRST = 1
DILATION_SECOND = 4
DILATION_THIRD = 16

NEG_FILL = -1e30
STRIDES = (DILATION_FIRST, DILATION_SECOND, DILATION_THIRD)


def exchange(block, bit):
    count = lax.axis_size("seq")
    route = [(index, index ^ (1 << bit)) for index in range(count)]
    return lax.ppermute(block, "seq", route)


def pick_rows(rows, stride, offsets_row):
    if stride == 1:
        return rows
    pair, count, width = rows.shape
    heads = offsets_row.shape[0]
    grouped = rows.reshape(pair, count // stride, stride, heads, width // heads)
    chosen = (jnp.arange(stride, dtype=jnp.int32)[:, None] == offsets_row[None, :])[
        None, None, :, :, None
    ]
    picked = jnp.sum(jnp.where(chosen, grouped, jnp.zeros((), rows.dtype)), axis=2)
    return picked.reshape(pair, count // stride, width)


def spread_rows(picked, stride, offsets_row):
    if stride == 1:
        return picked
    pair, count, width = picked.shape
    heads = offsets_row.shape[0]
    grouped = picked.reshape(pair, count, 1, heads, width // heads)
    chosen = (jnp.arange(stride, dtype=jnp.int32)[:, None] == offsets_row[None, :])[
        None, None, :, :, None
    ]
    widened = jnp.where(chosen, grouped, jnp.zeros((), picked.dtype))
    return widened.reshape(pair, count * stride, width)


def attention_kernel(head_dim, score_scale, head_base):
    def kernel(offsets_ref, query_ref, grad_ref, *refs):
        kv_refs = refs[:6]
        out_ref, qgrad_ref = refs[6:8]
        term_refs = refs[8:]
        pair = pl.program_id(0)
        rows = query_ref.shape[0]
        heads_per_block = query_ref.shape[1] // head_dim
        for sub in range(heads_per_block):
            head = head_base + pair * heads_per_block + sub
            cols = slice(sub * head_dim, (sub + 1) * head_dim)
            query = query_ref[:, cols]
            grad = grad_ref[:, cols]
            keys = [kv_ref[0, :, cols] for kv_ref in kv_refs]
            values = [kv_ref[1, :, cols] for kv_ref in kv_refs]
            members = []
            scores = []
            for piece in range(6):
                branch = piece // 2
                block = (
                    lax.dot_general(
                        query, keys[piece], (((1,), (1,)), ((), ())),
                        preferred_element_type=jnp.float32,
                    )
                    * score_scale
                )
                if STRIDES[branch] == 1:
                    member = None
                else:
                    row_index = lax.broadcasted_iota(jnp.int32, block.shape, 0)
                    member = (row_index % STRIDES[branch]) == offsets_ref[branch, head]
                    block = jnp.where(member, block, NEG_FILL)
                members.append(member)
                scores.append(block)
            peak = jnp.max(scores[0], axis=1, keepdims=True)
            for piece in range(1, 6):
                peak = jnp.maximum(peak, jnp.max(scores[piece], axis=1, keepdims=True))
            expos = []
            for piece in range(6):
                block = jnp.exp(scores[piece] - peak)
                if members[piece] is not None:
                    block = jnp.where(members[piece], block, 0.0)
                expos.append(block)
            total = jnp.sum(expos[0], axis=1, keepdims=True)
            for piece in range(1, 6):
                total = total + jnp.sum(expos[piece], axis=1, keepdims=True)
            probs = [block / total for block in expos]
            weights = [block.astype(jnp.bfloat16) for block in probs]
            mixed = jnp.dot(weights[0], values[0], preferred_element_type=jnp.float32)
            for piece in range(1, 6):
                mixed = mixed + jnp.dot(
                    weights[piece], values[piece], preferred_element_type=jnp.float32
                )
            out_ref[:, cols] = mixed.astype(out_ref.dtype)
            balance = jnp.sum(grad.astype(jnp.float32) * mixed, axis=1, keepdims=True)
            query_grad = None
            for piece in range(6):
                flow = lax.dot_general(
                    grad, values[piece], (((1,), (1,)), ((), ())),
                    preferred_element_type=jnp.float32,
                )
                score_grad = probs[piece] * (flow - balance)
                part = jnp.dot(
                    score_grad.astype(jnp.bfloat16), keys[piece],
                    preferred_element_type=jnp.float32,
                )
                query_grad = part if query_grad is None else query_grad + part
                key_terms = (
                    jnp.dot(
                        jnp.transpose(score_grad).astype(jnp.bfloat16),
                        query,
                        preferred_element_type=jnp.float32,
                    )
                    * score_scale
                )
                value_terms = jnp.dot(
                    jnp.transpose(probs[piece]).astype(jnp.bfloat16),
                    grad,
                    preferred_element_type=jnp.float32,
                )
                term_refs[piece][0, :, cols] = key_terms
                term_refs[piece][1, :, cols] = value_terms
            qgrad_ref[:, cols] = (query_grad * score_scale).astype(qgrad_ref.dtype)

    return kernel


def gather_order(top_bits, swapped):
    order = list(reversed(range(top_bits)))
    if swapped and top_bits >= 3:
        first, second = order.index(1), order.index(2)
        order[first], order[second] = order[second], order[first]
    return order


def make_per_device(branch_bits):
    top_bits = max(branch_bits)

    def per_device(query_rows, key_rows, value_rows, output_grad, head_offsets):
        local_rows, model_width = query_rows.shape
        head_count = head_offsets.shape[1]
        head_dim = model_width // head_count
        score_scale = 1.0 / math.sqrt(head_dim)
        kv_rows = jnp.stack([key_rows, value_rows])
        picked = [
            pick_rows(kv_rows, STRIDES[branch], head_offsets[branch]) for branch in range(3)
        ]
        block_width = 128 if (128 % head_dim == 0 and model_width % 128 == 0) else model_width
        halves = 2 if model_width % (2 * block_width) == 0 else 1
        half_width = model_width // halves
        heads_per_half = head_count // halves

        gathered_halves = []
        layouts = []
        for half in range(halves):
            cols = slice(half * half_width, (half + 1) * half_width)
            buffers = [block[:, :, cols] for block in picked]
            axis_bits = [[] for _ in range(3)]
            order = gather_order(top_bits, half == 1)
            for bit in order[:-1]:
                active = [branch for branch in range(3) if branch_bits[branch] > bit]
                outgoing = jnp.concatenate(
                    [buffers[branch].reshape(-1, half_width) for branch in active]
                )
                incoming = exchange(outgoing, bit)
                cursor = 0
                for branch in active:
                    count = buffers[branch].size // half_width
                    arrived = incoming[cursor : cursor + count].reshape(buffers[branch].shape)
                    cursor += count
                    buffers[branch] = jnp.stack([buffers[branch], arrived], axis=1)
                    axis_bits[branch].insert(0, bit)
            last = order[-1]
            mine = [buffers[branch].reshape(2, -1, half_width) for branch in range(3)]
            arrived = exchange(tuple(mine), last)
            pieces = []
            for branch in range(3):
                pieces += [mine[branch], arrived[branch]]
            gathered_halves.append(pieces)
            layouts.append(axis_bits)

        results = []
        for half in range(halves):
            gathered = gathered_halves[half]
            cols = slice(half * half_width, (half + 1) * half_width)
            order = gather_order(top_bits, half == 1)
            last = order[-1]
            pairs = half_width // block_width
            row_block = pl.BlockSpec((local_rows, block_width), lambda p, offs: (0, p))
            kv_blocks = [
                pl.BlockSpec((2, block.shape[1], block_width), lambda p, offs: (0, 0, p))
                for block in gathered
            ]
            outs = pl.pallas_call(
                attention_kernel(head_dim, score_scale, half * heads_per_half),
                out_shape=(
                    jax.ShapeDtypeStruct((local_rows, half_width), jnp.bfloat16),
                    jax.ShapeDtypeStruct((local_rows, half_width), jnp.bfloat16),
                )
                + tuple(jax.ShapeDtypeStruct(block.shape, jnp.float32) for block in gathered),
                grid_spec=pltpu.PrefetchScalarGridSpec(
                    num_scalar_prefetch=1,
                    grid=(pairs,),
                    in_specs=[row_block, row_block] + kv_blocks,
                    out_specs=[row_block, row_block] + kv_blocks,
                ),
                compiler_params=pltpu.CompilerParams(vmem_limit_bytes=100 * 1024 * 1024),
            )(head_offsets, query_rows[:, cols], output_grad[:, cols], *gathered)
            attended, query_grad = outs[:2]
            terms = outs[2:]

            axis_bits = [list(bits) for bits in layouts[half]]
            returned = exchange(tuple(terms[2 * branch + 1] for branch in range(3)), last)
            partial = [
                (terms[2 * branch] + returned[branch]).reshape(
                    (2,) + (2,) * len(axis_bits[branch]) + (-1, half_width)
                )
                for branch in range(3)
            ]
            for bit in reversed(order[:-1]):
                active = [branch for branch in range(3) if branch_bits[branch] > bit]
                places = {branch: 1 + axis_bits[branch].index(bit) for branch in active}
                outgoing = jnp.concatenate(
                    [
                        lax.index_in_dim(partial[branch], 1, places[branch], keepdims=False)
                        .reshape(-1, half_width)
                        .astype(jnp.bfloat16)
                        for branch in active
                    ]
                )
                incoming = exchange(outgoing, bit).astype(jnp.float32)
                cursor = 0
                for branch in active:
                    kept = lax.index_in_dim(partial[branch], 0, places[branch], keepdims=False)
                    count = kept.size // half_width
                    partial[branch] = kept + incoming[cursor : cursor + count].reshape(kept.shape)
                    cursor += count
                    axis_bits[branch].remove(bit)
            offsets_half = head_offsets[:, half * heads_per_half : (half + 1) * heads_per_half]
            total_grad = None
            for branch in range(3):
                spread = spread_rows(partial[branch], STRIDES[branch], offsets_half[branch])
                total_grad = spread if total_grad is None else total_grad + spread
            results.append((attended, query_grad, total_grad[0], total_grad[1]))

        return tuple(
            jnp.concatenate([result[index] for result in results], axis=1).astype(jnp.bfloat16)
            for index in range(4)
        )

    return per_device


def solution(mesh):
    group_count = mesh.shape["groups"]
    seq_devices = mesh.shape["seq"]

    def run(query_rows, key_rows, value_rows, output_grad, head_offsets):
        local_rows = query_rows.shape[0] // (group_count * seq_devices)
        tokens_all = seq_devices * local_rows
        seg_lengths = [min(LEN_NEAR, tokens_all), min(LEN_MID, tokens_all), min(LEN_FAR, tokens_all)]
        branch_bits = [(seg_length // local_rows).bit_length() - 1 for seg_length in seg_lengths]
        row_spec = P(("groups", "seq"), None)
        return jax.shard_map(
            make_per_device(branch_bits),
            mesh=mesh,
            in_specs=(row_spec, row_spec, row_spec, row_spec, P()),
            out_specs=(row_spec, row_spec, row_spec, row_spec),
            check_vma=False,
        )(query_rows, key_rows, value_rows, output_grad, head_offsets)

    return run
```

```python
import math

import jax
import jax.numpy as jnp
from jax import lax
from jax.experimental import pallas as pl
from jax.experimental.pallas import tpu as pltpu
from jax.sharding import PartitionSpec as P

LEN_NEAR = 1024
LEN_MID = 4096
LEN_FAR = 16384
DILATION_FIRST = 1
DILATION_SECOND = 4
DILATION_THIRD = 16

NEG_FILL = -1e30
STRIDES = (DILATION_FIRST, DILATION_SECOND, DILATION_THIRD)


def exchange(block, bit):
    count = lax.axis_size("seq")
    route = [(index, index ^ (1 << bit)) for index in range(count)]
    return lax.ppermute(block, "seq", route)


def pick_rows(rows, stride, offsets_row):
    if stride == 1:
        return rows
    pair, count, width = rows.shape
    heads = offsets_row.shape[0]
    grouped = rows.reshape(pair, count // stride, stride, heads, width // heads)
    chosen = (jnp.arange(stride, dtype=jnp.int32)[:, None] == offsets_row[None, :])[
        None, None, :, :, None
    ]
    picked = jnp.sum(jnp.where(chosen, grouped, jnp.zeros((), rows.dtype)), axis=2)
    return picked.reshape(pair, count // stride, width)


def spread_rows(picked, stride, offsets_row):
    if stride == 1:
        return picked
    pair, count, width = picked.shape
    heads = offsets_row.shape[0]
    grouped = picked.reshape(pair, count, 1, heads, width // heads)
    chosen = (jnp.arange(stride, dtype=jnp.int32)[:, None] == offsets_row[None, :])[
        None, None, :, :, None
    ]
    widened = jnp.where(chosen, grouped, jnp.zeros((), picked.dtype))
    return widened.reshape(pair, count * stride, width)


def attention_kernel(head_dim, score_scale, head_base):
    def kernel(offsets_ref, query_ref, grad_ref, *refs):
        kv_refs = refs[:3]
        out_ref, qgrad_ref = refs[3:5]
        term_refs = refs[5:]
        pair = pl.program_id(0)
        rows = query_ref.shape[0]
        heads_per_block = query_ref.shape[1] // head_dim
        for sub in range(heads_per_block):
            head = head_base + pair * heads_per_block + sub
            cols = slice(sub * head_dim, (sub + 1) * head_dim)
            query = query_ref[:, cols]
            grad = grad_ref[:, cols]
            keys = [kv_ref[0, :, cols] for kv_ref in kv_refs]
            values = [kv_ref[1, :, cols] for kv_ref in kv_refs]
            members = []
            scores = []
            for branch in range(3):
                block = (
                    lax.dot_general(
                        query, keys[branch], (((1,), (1,)), ((), ())),
                        preferred_element_type=jnp.float32,
                    )
                    * score_scale
                )
                if STRIDES[branch] == 1:
                    member = None
                else:
                    row_index = lax.broadcasted_iota(jnp.int32, block.shape, 0)
                    member = (row_index % STRIDES[branch]) == offsets_ref[branch, head]
                    block = jnp.where(member, block, NEG_FILL)
                members.append(member)
                scores.append(block)
            peak = jnp.max(scores[0], axis=1, keepdims=True)
            for branch in range(1, 3):
                peak = jnp.maximum(peak, jnp.max(scores[branch], axis=1, keepdims=True))
            expos = []
            for branch in range(3):
                block = jnp.exp(scores[branch] - peak)
                if members[branch] is not None:
                    block = jnp.where(members[branch], block, 0.0)
                expos.append(block)
            total = jnp.sum(expos[0], axis=1, keepdims=True)
            for branch in range(1, 3):
                total = total + jnp.sum(expos[branch], axis=1, keepdims=True)
            probs = [block / total for block in expos]
            weights = [block.astype(jnp.bfloat16) for block in probs]
            mixed = jnp.dot(weights[0], values[0], preferred_element_type=jnp.float32)
            for branch in range(1, 3):
                mixed = mixed + jnp.dot(
                    weights[branch], values[branch], preferred_element_type=jnp.float32
                )
            out_ref[:, cols] = mixed.astype(out_ref.dtype)
            balance = jnp.sum(grad.astype(jnp.float32) * mixed, axis=1, keepdims=True)
            query_grad = None
            for branch in range(3):
                flow = lax.dot_general(
                    grad, values[branch], (((1,), (1,)), ((), ())),
                    preferred_element_type=jnp.float32,
                )
                score_grad = probs[branch] * (flow - balance)
                piece = jnp.dot(
                    score_grad.astype(jnp.bfloat16), keys[branch],
                    preferred_element_type=jnp.float32,
                )
                query_grad = piece if query_grad is None else query_grad + piece
                key_terms = (
                    lax.dot_general(
                        score_grad.astype(jnp.bfloat16), query, (((0,), (0,)), ((), ())),
                        preferred_element_type=jnp.float32,
                    )
                    * score_scale
                )
                value_terms = lax.dot_general(
                    weights[branch], grad, (((0,), (0,)), ((), ())),
                    preferred_element_type=jnp.float32,
                )
                term_refs[branch][0, :, cols] = key_terms
                term_refs[branch][1, :, cols] = value_terms
            qgrad_ref[:, cols] = (query_grad * score_scale).astype(qgrad_ref.dtype)

    return kernel


def gather_order(top_bits, swapped):
    order = list(reversed(range(top_bits)))
    if swapped and top_bits >= 3:
        first, second = order.index(1), order.index(2)
        order[first], order[second] = order[second], order[first]
    return order


def make_per_device(branch_bits):
    top_bits = max(branch_bits)

    def per_device(query_rows, key_rows, value_rows, output_grad, head_offsets):
        local_rows, model_width = query_rows.shape
        head_count = head_offsets.shape[1]
        head_dim = model_width // head_count
        score_scale = 1.0 / math.sqrt(head_dim)
        kv_rows = jnp.stack([key_rows, value_rows])
        picked = [
            pick_rows(kv_rows, STRIDES[branch], head_offsets[branch]) for branch in range(3)
        ]
        block_width = 128 if (128 % head_dim == 0 and model_width % 128 == 0) else model_width
        halves = 2 if model_width % (2 * block_width) == 0 else 1
        half_width = model_width // halves
        heads_per_half = head_count // halves

        gathered_halves = []
        layouts = []
        for half in range(halves):
            cols = slice(half * half_width, (half + 1) * half_width)
            buffers = [block[:, :, cols] for block in picked]
            axis_bits = [[] for _ in range(3)]
            for bit in gather_order(top_bits, half == 1):
                active = [branch for branch in range(3) if branch_bits[branch] > bit]
                outgoing = jnp.concatenate(
                    [buffers[branch].reshape(-1, half_width) for branch in active]
                )
                incoming = exchange(outgoing, bit)
                cursor = 0
                for branch in active:
                    count = buffers[branch].size // half_width
                    arrived = incoming[cursor : cursor + count].reshape(buffers[branch].shape)
                    cursor += count
                    buffers[branch] = jnp.stack([buffers[branch], arrived], axis=1)
                    axis_bits[branch].insert(0, bit)
            gathered_halves.append([buffers[branch].reshape(2, -1, half_width) for branch in range(3)])
            layouts.append(axis_bits)

        results = []
        for half in range(halves):
            gathered = gathered_halves[half]
            cols = slice(half * half_width, (half + 1) * half_width)
            pairs = half_width // block_width
            row_block = pl.BlockSpec((local_rows, block_width), lambda p, offs: (0, p))
            kv_blocks = [
                pl.BlockSpec((2, block.shape[1], block_width), lambda p, offs: (0, 0, p))
                for block in gathered
            ]
            outs = pl.pallas_call(
                attention_kernel(head_dim, score_scale, half * heads_per_half),
                out_shape=(
                    jax.ShapeDtypeStruct((local_rows, half_width), jnp.bfloat16),
                    jax.ShapeDtypeStruct((local_rows, half_width), jnp.bfloat16),
                )
                + tuple(jax.ShapeDtypeStruct(block.shape, jnp.float32) for block in gathered),
                grid_spec=pltpu.PrefetchScalarGridSpec(
                    num_scalar_prefetch=1,
                    grid=(pairs,),
                    in_specs=[row_block, row_block] + kv_blocks,
                    out_specs=[row_block, row_block] + kv_blocks,
                ),
                compiler_params=pltpu.CompilerParams(vmem_limit_bytes=100 * 1024 * 1024),
            )(head_offsets, query_rows[:, cols], output_grad[:, cols], *gathered)
            attended, query_grad = outs[:2]
            terms = outs[2:]

            axis_bits = [list(bits) for bits in layouts[half]]
            partial = [
                terms[branch].reshape((2,) + (2,) * branch_bits[branch] + (-1, half_width))
                for branch in range(3)
            ]
            for bit in reversed(gather_order(top_bits, half == 1)):
                active = [branch for branch in range(3) if branch_bits[branch] > bit]
                places = {branch: 1 + axis_bits[branch].index(bit) for branch in active}
                outgoing = jnp.concatenate(
                    [
                        lax.index_in_dim(partial[branch], 1, places[branch], keepdims=False)
                        .reshape(-1, half_width)
                        .astype(jnp.bfloat16)
                        for branch in active
                    ]
                )
                incoming = exchange(outgoing, bit).astype(jnp.float32)
                cursor = 0
                for branch in active:
                    kept = lax.index_in_dim(partial[branch], 0, places[branch], keepdims=False)
                    count = kept.size // half_width
                    partial[branch] = kept + incoming[cursor : cursor + count].reshape(kept.shape)
                    cursor += count
                    axis_bits[branch].remove(bit)
            offsets_half = head_offsets[:, half * heads_per_half : (half + 1) * heads_per_half]
            total_grad = None
            for branch in range(3):
                spread = spread_rows(partial[branch], STRIDES[branch], offsets_half[branch])
                total_grad = spread if total_grad is None else total_grad + spread
            results.append((attended, query_grad, total_grad[0], total_grad[1]))

        return tuple(
            jnp.concatenate([result[index] for result in results], axis=1).astype(jnp.bfloat16)
            for index in range(4)
        )

    return per_device


def solution(mesh):
    group_count = mesh.shape["groups"]
    seq_devices = mesh.shape["seq"]

    def run(query_rows, key_rows, value_rows, output_grad, head_offsets):
        local_rows = query_rows.shape[0] // (group_count * seq_devices)
        tokens_all = seq_devices * local_rows
        seg_lengths = [min(LEN_NEAR, tokens_all), min(LEN_MID, tokens_all), min(LEN_FAR, tokens_all)]
        branch_bits = [(seg_length // local_rows).bit_length() - 1 for seg_length in seg_lengths]
        row_spec = P(("groups", "seq"), None)
        return jax.shard_map(
            make_per_device(branch_bits),
            mesh=mesh,
            in_specs=(row_spec, row_spec, row_spec, row_spec, P()),
            out_specs=(row_spec, row_spec, row_spec, row_spec),
            check_vma=False,
        )(query_rows, key_rows, value_rows, output_grad, head_offsets)

    return run
```

```python
import math

import jax
import jax.numpy as jnp
from jax import lax
from jax.experimental import pallas as pl
from jax.experimental.pallas import tpu as pltpu
from jax.sharding import PartitionSpec as P

LEN_NEAR = 1024
LEN_MID = 4096
LEN_FAR = 16384
DILATION_FIRST = 1
DILATION_SECOND = 4
DILATION_THIRD = 16

NEG_FILL = -1e30
STRIDES = (DILATION_FIRST, DILATION_SECOND, DILATION_THIRD)


def exchange(block, bit):
    count = lax.axis_size("seq")
    route = [(index, index ^ (1 << bit)) for index in range(count)]
    return lax.ppermute(block, "seq", route)


def pick_rows(rows, stride, offsets_row):
    if stride == 1:
        return rows
    pair, count, width = rows.shape
    heads = offsets_row.shape[0]
    grouped = rows.reshape(pair, count // stride, stride, heads, width // heads)
    chosen = (jnp.arange(stride, dtype=jnp.int32)[:, None] == offsets_row[None, :])[
        None, None, :, :, None
    ]
    picked = jnp.sum(jnp.where(chosen, grouped, jnp.zeros((), rows.dtype)), axis=2)
    return picked.reshape(pair, count // stride, width)


def spread_rows(picked, stride, offsets_row):
    if stride == 1:
        return picked
    pair, count, width = picked.shape
    heads = offsets_row.shape[0]
    grouped = picked.reshape(pair, count, 1, heads, width // heads)
    chosen = (jnp.arange(stride, dtype=jnp.int32)[:, None] == offsets_row[None, :])[
        None, None, :, :, None
    ]
    widened = jnp.where(chosen, grouped, jnp.zeros((), picked.dtype))
    return widened.reshape(pair, count * stride, width)


def attention_kernel(head_dim, score_scale, head_base):
    def kernel(offsets_ref, query_ref, grad_ref, *refs):
        kv_refs = refs[:3]
        out_ref, qgrad_ref = refs[3:5]
        term_refs = refs[5:]
        pair = pl.program_id(0)
        rows = query_ref.shape[0]
        heads_per_block = query_ref.shape[1] // head_dim
        for sub in range(heads_per_block):
            head = head_base + pair * heads_per_block + sub
            cols = slice(sub * head_dim, (sub + 1) * head_dim)
            query = query_ref[:, cols]
            grad = grad_ref[:, cols]
            keys = [kv_ref[0, :, cols] for kv_ref in kv_refs]
            values = [kv_ref[1, :, cols] for kv_ref in kv_refs]
            members = []
            scores = []
            for branch in range(3):
                block = (
                    lax.dot_general(
                        query, keys[branch], (((1,), (1,)), ((), ())),
                        preferred_element_type=jnp.float32,
                    )
                    * score_scale
                )
                if STRIDES[branch] == 1:
                    member = None
                else:
                    row_index = lax.broadcasted_iota(jnp.int32, block.shape, 0)
                    member = (row_index % STRIDES[branch]) == offsets_ref[branch, head]
                    block = jnp.where(member, block, NEG_FILL)
                members.append(member)
                scores.append(block)
            peak = jnp.max(scores[0], axis=1, keepdims=True)
            for branch in range(1, 3):
                peak = jnp.maximum(peak, jnp.max(scores[branch], axis=1, keepdims=True))
            expos = []
            for branch in range(3):
                block = jnp.exp(scores[branch] - peak)
                if members[branch] is not None:
                    block = jnp.where(members[branch], block, 0.0)
                expos.append(block)
            total = jnp.sum(expos[0], axis=1, keepdims=True)
            for branch in range(1, 3):
                total = total + jnp.sum(expos[branch], axis=1, keepdims=True)
            probs = [block / total for block in expos]
            weights = [block.astype(jnp.bfloat16) for block in probs]
            mixed = jnp.dot(weights[0], values[0], preferred_element_type=jnp.float32)
            for branch in range(1, 3):
                mixed = mixed + jnp.dot(
                    weights[branch], values[branch], preferred_element_type=jnp.float32
                )
            out_ref[:, cols] = mixed.astype(out_ref.dtype)
            balance = jnp.sum(grad.astype(jnp.float32) * mixed, axis=1, keepdims=True)
            query_grad = None
            for branch in range(3):
                flow = lax.dot_general(
                    grad, values[branch], (((1,), (1,)), ((), ())),
                    preferred_element_type=jnp.float32,
                )
                score_grad = probs[branch] * (flow - balance)
                piece = jnp.dot(
                    score_grad.astype(jnp.bfloat16), keys[branch],
                    preferred_element_type=jnp.float32,
                )
                query_grad = piece if query_grad is None else query_grad + piece
                key_terms = (
                    lax.dot_general(
                        score_grad.astype(jnp.bfloat16), query, (((0,), (0,)), ((), ())),
                        preferred_element_type=jnp.float32,
                    )
                    * score_scale
                )
                value_terms = lax.dot_general(
                    weights[branch], grad, (((0,), (0,)), ((), ())),
                    preferred_element_type=jnp.float32,
                )
                term_refs[branch][0, :, cols] = key_terms
                term_refs[branch][1, :, cols] = value_terms
            qgrad_ref[:, cols] = (query_grad * score_scale).astype(qgrad_ref.dtype)

    return kernel


def gather_order(top_bits, swapped):
    order = list(reversed(range(top_bits)))
    if swapped and top_bits >= 3:
        first, second = order.index(1), order.index(2)
        order[first], order[second] = order[second], order[first]
    return order


def make_per_device(branch_bits):
    top_bits = max(branch_bits)

    def per_device(query_rows, key_rows, value_rows, output_grad, head_offsets):
        local_rows, model_width = query_rows.shape
        head_count = head_offsets.shape[1]
        head_dim = model_width // head_count
        score_scale = 1.0 / math.sqrt(head_dim)
        kv_rows = jnp.stack([key_rows, value_rows])
        picked = [
            pick_rows(kv_rows, STRIDES[branch], head_offsets[branch]) for branch in range(3)
        ]
        block_width = 128 if (128 % head_dim == 0 and model_width % 128 == 0) else model_width
        halves = 2 if model_width % (2 * block_width) == 0 else 1
        half_width = model_width // halves
        heads_per_half = head_count // halves

        gathered_halves = []
        layouts = []
        for half in range(halves):
            cols = slice(half * half_width, (half + 1) * half_width)
            buffers = [block[:, :, cols] for block in picked]
            axis_bits = [[] for _ in range(3)]
            for bit in gather_order(top_bits, half == 1):
                active = [branch for branch in range(3) if branch_bits[branch] > bit]
                outgoing = jnp.concatenate(
                    [buffers[branch].reshape(-1, half_width) for branch in active]
                )
                incoming = exchange(outgoing, bit)
                cursor = 0
                for branch in active:
                    count = buffers[branch].size // half_width
                    arrived = incoming[cursor : cursor + count].reshape(buffers[branch].shape)
                    cursor += count
                    buffers[branch] = jnp.stack([buffers[branch], arrived], axis=1)
                    axis_bits[branch].insert(0, bit)
            gathered_halves.append([buffers[branch].reshape(2, -1, half_width) for branch in range(3)])
            layouts.append(axis_bits)

        results = []
        for half in range(halves):
            gathered = gathered_halves[half]
            cols = slice(half * half_width, (half + 1) * half_width)
            pairs = half_width // block_width
            row_block = pl.BlockSpec((local_rows, block_width), lambda p, offs: (0, p))
            kv_blocks = [
                pl.BlockSpec((2, block.shape[1], block_width), lambda p, offs: (0, 0, p))
                for block in gathered
            ]
            outs = pl.pallas_call(
                attention_kernel(head_dim, score_scale, half * heads_per_half),
                out_shape=(
                    jax.ShapeDtypeStruct((local_rows, half_width), jnp.bfloat16),
                    jax.ShapeDtypeStruct((local_rows, half_width), jnp.bfloat16),
                )
                + tuple(jax.ShapeDtypeStruct(block.shape, jnp.float32) for block in gathered),
                grid_spec=pltpu.PrefetchScalarGridSpec(
                    num_scalar_prefetch=1,
                    grid=(pairs,),
                    in_specs=[row_block, row_block] + kv_blocks,
                    out_specs=[row_block, row_block] + kv_blocks,
                ),
                compiler_params=pltpu.CompilerParams(vmem_limit_bytes=100 * 1024 * 1024),
            )(head_offsets, query_rows[:, cols], output_grad[:, cols], *gathered)
            attended, query_grad = outs[:2]
            terms = outs[2:]

            axis_bits = [list(bits) for bits in layouts[half]]
            partial = [
                terms[branch].reshape((2,) + (2,) * branch_bits[branch] + (-1, half_width))
                for branch in range(3)
            ]
            for bit in reversed(gather_order(top_bits, half == 1)):
                active = [branch for branch in range(3) if branch_bits[branch] > bit]
                places = {branch: 1 + axis_bits[branch].index(bit) for branch in active}
                outgoing = jnp.concatenate(
                    [
                        lax.index_in_dim(partial[branch], 1, places[branch], keepdims=False)
                        .reshape(-1, half_width)
                        for branch in active
                    ]
                )
                incoming = exchange(outgoing, bit)
                cursor = 0
                for branch in active:
                    kept = lax.index_in_dim(partial[branch], 0, places[branch], keepdims=False)
                    count = kept.size // half_width
                    partial[branch] = kept + incoming[cursor : cursor + count].reshape(kept.shape)
                    cursor += count
                    axis_bits[branch].remove(bit)
            offsets_half = head_offsets[:, half * heads_per_half : (half + 1) * heads_per_half]
            total_grad = None
            for branch in range(3):
                spread = spread_rows(partial[branch], STRIDES[branch], offsets_half[branch])
                total_grad = spread if total_grad is None else total_grad + spread
            results.append((attended, query_grad, total_grad[0], total_grad[1]))

        return tuple(
            jnp.concatenate([result[index] for result in results], axis=1).astype(jnp.bfloat16)
            for index in range(4)
        )

    return per_device


def solution(mesh):
    group_count = mesh.shape["groups"]
    seq_devices = mesh.shape["seq"]

    def run(query_rows, key_rows, value_rows, output_grad, head_offsets):
        local_rows = query_rows.shape[0] // (group_count * seq_devices)
        tokens_all = seq_devices * local_rows
        seg_lengths = [min(LEN_NEAR, tokens_all), min(LEN_MID, tokens_all), min(LEN_FAR, tokens_all)]
        branch_bits = [(seg_length // local_rows).bit_length() - 1 for seg_length in seg_lengths]
        row_spec = P(("groups", "seq"), None)
        return jax.shard_map(
            make_per_device(branch_bits),
            mesh=mesh,
            in_specs=(row_spec, row_spec, row_spec, row_spec, P()),
            out_specs=(row_spec, row_spec, row_spec, row_spec),
            check_vma=False,
        )(query_rows, key_rows, value_rows, output_grad, head_offsets)

    return run
```

```python
import math

import jax
import jax.numpy as jnp
from jax import lax
from jax.experimental import pallas as pl
from jax.experimental.pallas import tpu as pltpu
from jax.sharding import PartitionSpec as P

LEN_NEAR = 1024
LEN_MID = 4096
LEN_FAR = 16384
DILATION_FIRST = 1
DILATION_SECOND = 4
DILATION_THIRD = 16

NEG_FILL = -1e30
STRIDES = (DILATION_FIRST, DILATION_SECOND, DILATION_THIRD)


def exchange(block, bit):
    count = lax.axis_size("seq")
    route = [(index, index ^ (1 << bit)) for index in range(count)]
    return lax.ppermute(block, "seq", route)


def pick_rows(rows, stride, offsets_row):
    if stride == 1:
        return rows
    pair, count, width = rows.shape
    heads = offsets_row.shape[0]
    grouped = rows.reshape(pair, count // stride, stride, heads, width // heads)
    chosen = (jnp.arange(stride, dtype=jnp.int32)[:, None] == offsets_row[None, :])[
        None, None, :, :, None
    ]
    picked = jnp.sum(jnp.where(chosen, grouped, jnp.zeros((), rows.dtype)), axis=2)
    return picked.reshape(pair, count // stride, width)


def spread_rows(picked, stride, offsets_row):
    if stride == 1:
        return picked
    pair, count, width = picked.shape
    heads = offsets_row.shape[0]
    grouped = picked.reshape(pair, count, 1, heads, width // heads)
    chosen = (jnp.arange(stride, dtype=jnp.int32)[:, None] == offsets_row[None, :])[
        None, None, :, :, None
    ]
    widened = jnp.where(chosen, grouped, jnp.zeros((), picked.dtype))
    return widened.reshape(pair, count * stride, width)


def attention_kernel(head_dim, score_scale, head_base):
    def kernel(offsets_ref, query_ref, grad_ref, *refs):
        kv_refs = refs[:3]
        out_ref, qgrad_ref = refs[3:5]
        term_refs = refs[5:]
        pair = pl.program_id(0)
        rows = query_ref.shape[0]
        heads_per_block = query_ref.shape[1] // head_dim
        for sub in range(heads_per_block):
            head = head_base + pair * heads_per_block + sub
            cols = slice(sub * head_dim, (sub + 1) * head_dim)
            query = query_ref[:, cols]
            grad = grad_ref[:, cols]
            keys = [kv_ref[0, :, cols] for kv_ref in kv_refs]
            values = [kv_ref[1, :, cols] for kv_ref in kv_refs]
            members = []
            scores = []
            for branch in range(3):
                block = (
                    lax.dot_general(
                        query, keys[branch], (((1,), (1,)), ((), ())),
                        preferred_element_type=jnp.float32,
                    )
                    * score_scale
                )
                if STRIDES[branch] == 1:
                    member = None
                else:
                    row_index = lax.broadcasted_iota(jnp.int32, block.shape, 0)
                    member = (row_index % STRIDES[branch]) == offsets_ref[branch, head]
                    block = jnp.where(member, block, NEG_FILL)
                members.append(member)
                scores.append(block)
            peak = jnp.max(scores[0], axis=1, keepdims=True)
            for branch in range(1, 3):
                peak = jnp.maximum(peak, jnp.max(scores[branch], axis=1, keepdims=True))
            expos = []
            for branch in range(3):
                block = jnp.exp(scores[branch] - peak)
                if members[branch] is not None:
                    block = jnp.where(members[branch], block, 0.0)
                expos.append(block)
            total = jnp.sum(expos[0], axis=1, keepdims=True)
            for branch in range(1, 3):
                total = total + jnp.sum(expos[branch], axis=1, keepdims=True)
            probs = [block / total for block in expos]
            weights = [block.astype(jnp.bfloat16) for block in probs]
            mixed = jnp.dot(weights[0], values[0], preferred_element_type=jnp.float32)
            for branch in range(1, 3):
                mixed = mixed + jnp.dot(
                    weights[branch], values[branch], preferred_element_type=jnp.float32
                )
            out_ref[:, cols] = mixed.astype(out_ref.dtype)
            balance = jnp.sum(grad.astype(jnp.float32) * mixed, axis=1, keepdims=True)
            query_grad = None
            for branch in range(3):
                flow = lax.dot_general(
                    grad, values[branch], (((1,), (1,)), ((), ())),
                    preferred_element_type=jnp.float32,
                )
                score_grad = probs[branch] * (flow - balance)
                piece = jnp.dot(
                    score_grad.astype(jnp.bfloat16), keys[branch],
                    preferred_element_type=jnp.float32,
                )
                query_grad = piece if query_grad is None else query_grad + piece
                key_terms = (
                    lax.dot_general(
                        score_grad.astype(jnp.bfloat16), query, (((0,), (0,)), ((), ())),
                        preferred_element_type=jnp.float32,
                    )
                    * score_scale
                )
                value_terms = lax.dot_general(
                    weights[branch], grad, (((0,), (0,)), ((), ())),
                    preferred_element_type=jnp.float32,
                )
                term_refs[branch][0, :, cols] = key_terms
                term_refs[branch][1, :, cols] = value_terms
            qgrad_ref[:, cols] = (query_grad * score_scale).astype(qgrad_ref.dtype)

    return kernel


def gather_order(top_bits, swapped):
    order = list(reversed(range(top_bits)))
    if swapped and top_bits >= 3:
        first, second = order.index(1), order.index(2)
        order[first], order[second] = order[second], order[first]
    return order


def make_per_device(branch_bits):
    top_bits = max(branch_bits)

    def per_device(query_rows, key_rows, value_rows, output_grad, head_offsets):
        local_rows, model_width = query_rows.shape
        head_count = head_offsets.shape[1]
        head_dim = model_width // head_count
        score_scale = 1.0 / math.sqrt(head_dim)
        kv_rows = jnp.stack([key_rows, value_rows])
        picked = [
            pick_rows(kv_rows, STRIDES[branch], head_offsets[branch]) for branch in range(3)
        ]
        block_width = 128 if (128 % head_dim == 0 and model_width % 128 == 0) else model_width
        halves = 2 if model_width % (2 * block_width) == 0 else 1
        half_width = model_width // halves
        heads_per_half = head_count // halves

        gathered_halves = []
        layouts = []
        for half in range(halves):
            cols = slice(half * half_width, (half + 1) * half_width)
            buffers = [block[:, :, cols] for block in picked]
            axis_bits = [[] for _ in range(3)]
            for bit in gather_order(top_bits, half == 1):
                active = [branch for branch in range(3) if branch_bits[branch] > bit]
                outgoing = jnp.concatenate(
                    [buffers[branch].reshape(-1, half_width) for branch in active]
                )
                incoming = exchange(outgoing, bit)
                cursor = 0
                for branch in active:
                    count = buffers[branch].size // half_width
                    arrived = incoming[cursor : cursor + count].reshape(buffers[branch].shape)
                    cursor += count
                    buffers[branch] = jnp.stack([buffers[branch], arrived], axis=1)
                    axis_bits[branch].insert(0, bit)
            gathered_halves.append([buffers[branch].reshape(2, -1, half_width) for branch in range(3)])
            layouts.append(axis_bits)

        def run_kernel(half, gathered):
            cols = slice(half * half_width, (half + 1) * half_width)
            pairs = half_width // block_width
            row_block = pl.BlockSpec((local_rows, block_width), lambda p, offs: (0, p))
            kv_blocks = [
                pl.BlockSpec((2, block.shape[1], block_width), lambda p, offs: (0, 0, p))
                for block in gathered
            ]
            return pl.pallas_call(
                attention_kernel(head_dim, score_scale, half * heads_per_half),
                out_shape=(
                    jax.ShapeDtypeStruct((local_rows, half_width), jnp.bfloat16),
                    jax.ShapeDtypeStruct((local_rows, half_width), jnp.bfloat16),
                )
                + tuple(jax.ShapeDtypeStruct(block.shape, jnp.float32) for block in gathered),
                grid_spec=pltpu.PrefetchScalarGridSpec(
                    num_scalar_prefetch=1,
                    grid=(pairs,),
                    in_specs=[row_block, row_block] + kv_blocks,
                    out_specs=[row_block, row_block] + kv_blocks,
                ),
                compiler_params=pltpu.CompilerParams(vmem_limit_bytes=100 * 1024 * 1024),
            )(head_offsets, query_rows[:, cols], output_grad[:, cols], *gathered)

        def reduce_steps(partial, axis_bits, bits):
            for bit in bits:
                active = [branch for branch in range(3) if branch_bits[branch] > bit]
                places = {branch: 1 + axis_bits[branch].index(bit) for branch in active}
                outgoing = jnp.concatenate(
                    [
                        lax.index_in_dim(partial[branch], 1, places[branch], keepdims=False)
                        .reshape(-1, half_width)
                        .astype(jnp.bfloat16)
                        for branch in active
                    ]
                )
                incoming = exchange(outgoing, bit).astype(jnp.float32)
                cursor = 0
                for branch in active:
                    kept = lax.index_in_dim(partial[branch], 0, places[branch], keepdims=False)
                    count = kept.size // half_width
                    partial[branch] = kept + incoming[cursor : cursor + count].reshape(kept.shape)
                    cursor += count
                    axis_bits[branch].remove(bit)
            return partial

        kernel_outs = [None] * halves
        partials = [None] * halves
        axis_states = [None] * halves
        reduce_orders = [list(reversed(gather_order(top_bits, half == 1))) for half in range(halves)]
        for half in range(halves):
            gathered = gathered_halves[half]
            if half > 0:
                partials[half - 1], gathered = lax.optimization_barrier(
                    (partials[half - 1], gathered)
                )
            kernel_outs[half] = run_kernel(half, gathered)
            terms = kernel_outs[half][2:]
            axis_states[half] = [list(bits) for bits in layouts[half]]
            partials[half] = [
                terms[branch].reshape((2,) + (2,) * branch_bits[branch] + (-1, half_width))
                for branch in range(3)
            ]
            partials[half] = reduce_steps(
                partials[half], axis_states[half], reduce_orders[half][:1]
            )
        results = []
        for half in range(halves):
            partial = reduce_steps(partials[half], axis_states[half], reduce_orders[half][1:])
            offsets_half = head_offsets[:, half * heads_per_half : (half + 1) * heads_per_half]
            total_grad = None
            for branch in range(3):
                spread = spread_rows(partial[branch], STRIDES[branch], offsets_half[branch])
                total_grad = spread if total_grad is None else total_grad + spread
            attended, query_grad = kernel_outs[half][:2]
            results.append((attended, query_grad, total_grad[0], total_grad[1]))

        return tuple(
            jnp.concatenate([result[index] for result in results], axis=1).astype(jnp.bfloat16)
            for index in range(4)
        )

    return per_device


def solution(mesh):
    group_count = mesh.shape["groups"]
    seq_devices = mesh.shape["seq"]

    def run(query_rows, key_rows, value_rows, output_grad, head_offsets):
        local_rows = query_rows.shape[0] // (group_count * seq_devices)
        tokens_all = seq_devices * local_rows
        seg_lengths = [min(LEN_NEAR, tokens_all), min(LEN_MID, tokens_all), min(LEN_FAR, tokens_all)]
        branch_bits = [(seg_length // local_rows).bit_length() - 1 for seg_length in seg_lengths]
        row_spec = P(("groups", "seq"), None)
        return jax.shard_map(
            make_per_device(branch_bits),
            mesh=mesh,
            in_specs=(row_spec, row_spec, row_spec, row_spec, P()),
            out_specs=(row_spec, row_spec, row_spec, row_spec),
            check_vma=False,
        )(query_rows, key_rows, value_rows, output_grad, head_offsets)

    return run
```

```python
import math

import jax
import jax.numpy as jnp
from jax import lax
from jax.experimental import pallas as pl
from jax.experimental.pallas import tpu as pltpu
from jax.sharding import PartitionSpec as P

LEN_NEAR = 1024
LEN_MID = 4096
LEN_FAR = 16384
DILATION_FIRST = 1
DILATION_SECOND = 4
DILATION_THIRD = 16

NEG_FILL = -1e30
STRIDES = (DILATION_FIRST, DILATION_SECOND, DILATION_THIRD)


def exchange(block, bit):
    count = lax.axis_size("seq")
    route = [(index, index ^ (1 << bit)) for index in range(count)]
    return lax.ppermute(block, "seq", route)


def pick_rows(rows, stride, offsets_row):
    if stride == 1:
        return rows
    pair, count, width = rows.shape
    heads = offsets_row.shape[0]
    grouped = rows.reshape(pair, count // stride, stride, heads, width // heads)
    chosen = (jnp.arange(stride, dtype=jnp.int32)[:, None] == offsets_row[None, :])[
        None, None, :, :, None
    ]
    picked = jnp.sum(jnp.where(chosen, grouped, jnp.zeros((), rows.dtype)), axis=2)
    return picked.reshape(pair, count // stride, width)


def spread_rows(picked, stride, offsets_row):
    if stride == 1:
        return picked
    pair, count, width = picked.shape
    heads = offsets_row.shape[0]
    grouped = picked.reshape(pair, count, 1, heads, width // heads)
    chosen = (jnp.arange(stride, dtype=jnp.int32)[:, None] == offsets_row[None, :])[
        None, None, :, :, None
    ]
    widened = jnp.where(chosen, grouped, jnp.zeros((), picked.dtype))
    return widened.reshape(pair, count * stride, width)


def attention_kernel(head_dim, score_scale, head_base):
    def kernel(offsets_ref, query_ref, grad_ref, *refs):
        kv_refs = refs[:3]
        out_ref, qgrad_ref = refs[3:5]
        keep_refs = refs[5:8]
        message_ref = refs[8]
        pair = pl.program_id(0)
        rows = query_ref.shape[0]
        heads_per_block = query_ref.shape[1] // head_dim
        for sub in range(heads_per_block):
            head = head_base + pair * heads_per_block + sub
            cols = slice(sub * head_dim, (sub + 1) * head_dim)
            query = query_ref[:, cols]
            grad = grad_ref[:, cols]
            keys = [kv_ref[0, :, cols] for kv_ref in kv_refs]
            values = [kv_ref[1, :, cols] for kv_ref in kv_refs]
            members = []
            scores = []
            for branch in range(3):
                block = (
                    lax.dot_general(
                        query, keys[branch], (((1,), (1,)), ((), ())),
                        preferred_element_type=jnp.float32,
                    )
                    * score_scale
                )
                if STRIDES[branch] == 1:
                    member = None
                else:
                    row_index = lax.broadcasted_iota(jnp.int32, block.shape, 0)
                    member = (row_index % STRIDES[branch]) == offsets_ref[branch, head]
                    block = jnp.where(member, block, NEG_FILL)
                members.append(member)
                scores.append(block)
            peak = jnp.max(scores[0], axis=1, keepdims=True)
            for branch in range(1, 3):
                peak = jnp.maximum(peak, jnp.max(scores[branch], axis=1, keepdims=True))
            expos = []
            for branch in range(3):
                block = jnp.exp(scores[branch] - peak)
                if members[branch] is not None:
                    block = jnp.where(members[branch], block, 0.0)
                expos.append(block)
            total = jnp.sum(expos[0], axis=1, keepdims=True)
            for branch in range(1, 3):
                total = total + jnp.sum(expos[branch], axis=1, keepdims=True)
            probs = [block / total for block in expos]
            weights = [block.astype(jnp.bfloat16) for block in probs]
            mixed = jnp.dot(weights[0], values[0], preferred_element_type=jnp.float32)
            for branch in range(1, 3):
                mixed = mixed + jnp.dot(
                    weights[branch], values[branch], preferred_element_type=jnp.float32
                )
            out_ref[:, cols] = mixed.astype(out_ref.dtype)
            balance = jnp.sum(grad.astype(jnp.float32) * mixed, axis=1, keepdims=True)
            query_grad = None
            for branch in range(3):
                flow = lax.dot_general(
                    grad, values[branch], (((1,), (1,)), ((), ())),
                    preferred_element_type=jnp.float32,
                )
                score_grad = probs[branch] * (flow - balance)
                piece = jnp.dot(
                    score_grad.astype(jnp.bfloat16), keys[branch],
                    preferred_element_type=jnp.float32,
                )
                query_grad = piece if query_grad is None else query_grad + piece
                key_terms = (
                    lax.dot_general(
                        score_grad.astype(jnp.bfloat16), query, (((0,), (0,)), ((), ())),
                        preferred_element_type=jnp.float32,
                    )
                    * score_scale
                )
                value_terms = lax.dot_general(
                    weights[branch], grad, (((0,), (0,)), ((), ())),
                    preferred_element_type=jnp.float32,
                )
                half_keys = key_terms.shape[0] // 2
                start = sum(kv_ref.shape[1] for kv_ref in kv_refs[:branch])
                keep_refs[branch][0, :, cols] = key_terms[:half_keys]
                keep_refs[branch][1, :, cols] = value_terms[:half_keys]
                message_ref[start : start + half_keys, cols] = key_terms[half_keys:].astype(
                    message_ref.dtype
                )
                message_ref[start + half_keys : start + 2 * half_keys, cols] = value_terms[
                    half_keys:
                ].astype(message_ref.dtype)
            qgrad_ref[:, cols] = (query_grad * score_scale).astype(qgrad_ref.dtype)

    return kernel


def gather_order(top_bits, swapped):
    order = list(reversed(range(top_bits)))
    if swapped and top_bits >= 3:
        first, second = order.index(1), order.index(2)
        order[first], order[second] = order[second], order[first]
    return order


def make_per_device(branch_bits):
    top_bits = max(branch_bits)

    def per_device(query_rows, key_rows, value_rows, output_grad, head_offsets):
        local_rows, model_width = query_rows.shape
        head_count = head_offsets.shape[1]
        head_dim = model_width // head_count
        score_scale = 1.0 / math.sqrt(head_dim)
        kv_rows = jnp.stack([key_rows, value_rows])
        picked = [
            pick_rows(kv_rows, STRIDES[branch], head_offsets[branch]) for branch in range(3)
        ]
        block_width = 128 if (128 % head_dim == 0 and model_width % 128 == 0) else model_width
        halves = 2 if model_width % (2 * block_width) == 0 else 1
        half_width = model_width // halves
        heads_per_half = head_count // halves

        gathered_halves = []
        layouts = []
        for half in range(halves):
            cols = slice(half * half_width, (half + 1) * half_width)
            buffers = [block[:, :, cols] for block in picked]
            axis_bits = [[] for _ in range(3)]
            for bit in gather_order(top_bits, half == 1):
                active = [branch for branch in range(3) if branch_bits[branch] > bit]
                outgoing = jnp.concatenate(
                    [buffers[branch].reshape(-1, half_width) for branch in active]
                )
                incoming = exchange(outgoing, bit)
                cursor = 0
                for branch in active:
                    count = buffers[branch].size // half_width
                    arrived = incoming[cursor : cursor + count].reshape(buffers[branch].shape)
                    cursor += count
                    buffers[branch] = jnp.stack([buffers[branch], arrived], axis=1)
                    axis_bits[branch].insert(0, bit)
            gathered_halves.append([buffers[branch].reshape(2, -1, half_width) for branch in range(3)])
            layouts.append(axis_bits)

        results = []
        for half in range(halves):
            gathered = gathered_halves[half]
            cols = slice(half * half_width, (half + 1) * half_width)
            pairs = half_width // block_width
            key_rows_total = sum(block.shape[1] for block in gathered)
            row_block = pl.BlockSpec((local_rows, block_width), lambda p, offs: (0, p))
            kv_blocks = [
                pl.BlockSpec((2, block.shape[1], block_width), lambda p, offs: (0, 0, p))
                for block in gathered
            ]
            outs = pl.pallas_call(
                attention_kernel(head_dim, score_scale, half * heads_per_half),
                out_shape=(
                    jax.ShapeDtypeStruct((local_rows, half_width), jnp.bfloat16),
                    jax.ShapeDtypeStruct((local_rows, half_width), jnp.bfloat16),
                )
                + tuple(
                    jax.ShapeDtypeStruct((2, block.shape[1] // 2, half_width), jnp.float32)
                    for block in gathered
                )
                + (jax.ShapeDtypeStruct((key_rows_total, half_width), jnp.bfloat16),),
                grid_spec=pltpu.PrefetchScalarGridSpec(
                    num_scalar_prefetch=1,
                    grid=(pairs,),
                    in_specs=[row_block, row_block] + kv_blocks,
                    out_specs=[row_block, row_block]
                    + [
                        pl.BlockSpec((2, block.shape[1] // 2, block_width), lambda p, offs: (0, 0, p))
                        for block in gathered
                    ]
                    + [pl.BlockSpec((key_rows_total, block_width), lambda p, offs: (0, p))],
                ),
                compiler_params=pltpu.CompilerParams(vmem_limit_bytes=100 * 1024 * 1024),
            )(head_offsets, query_rows[:, cols], output_grad[:, cols], *gathered)
            attended, query_grad = outs[:2]
            kept_terms = outs[2:5]
            message = outs[5]

            axis_bits = [list(bits) for bits in layouts[half]]
            order = list(reversed(gather_order(top_bits, half == 1)))
            first = order[0]
            incoming = exchange(message, first).astype(jnp.float32)
            partial = []
            cursor = 0
            for branch in range(3):
                axis_bits[branch].remove(first)
                kept = kept_terms[branch].reshape(
                    (2,) + (2,) * len(axis_bits[branch]) + (-1, half_width)
                )
                count = kept.size // half_width
                partial.append(kept + incoming[cursor : cursor + count].reshape(kept.shape))
                cursor += count
            for bit in order[1:]:
                active = [branch for branch in range(3) if branch_bits[branch] > bit]
                places = {branch: 1 + axis_bits[branch].index(bit) for branch in active}
                outgoing = jnp.concatenate(
                    [
                        lax.index_in_dim(partial[branch], 1, places[branch], keepdims=False)
                        .reshape(-1, half_width)
                        .astype(jnp.bfloat16)
                        for branch in active
                    ]
                )
                incoming = exchange(outgoing, bit).astype(jnp.float32)
                cursor = 0
                for branch in active:
                    kept = lax.index_in_dim(partial[branch], 0, places[branch], keepdims=False)
                    count = kept.size // half_width
                    partial[branch] = kept + incoming[cursor : cursor + count].reshape(kept.shape)
                    cursor += count
                    axis_bits[branch].remove(bit)
            offsets_half = head_offsets[:, half * heads_per_half : (half + 1) * heads_per_half]
            total_grad = None
            for branch in range(3):
                spread = spread_rows(partial[branch], STRIDES[branch], offsets_half[branch])
                total_grad = spread if total_grad is None else total_grad + spread
            results.append((attended, query_grad, total_grad[0], total_grad[1]))

        return tuple(
            jnp.concatenate([result[index] for result in results], axis=1).astype(jnp.bfloat16)
            for index in range(4)
        )

    return per_device


def solution(mesh):
    group_count = mesh.shape["groups"]
    seq_devices = mesh.shape["seq"]

    def run(query_rows, key_rows, value_rows, output_grad, head_offsets):
        local_rows = query_rows.shape[0] // (group_count * seq_devices)
        tokens_all = seq_devices * local_rows
        seg_lengths = [min(LEN_NEAR, tokens_all), min(LEN_MID, tokens_all), min(LEN_FAR, tokens_all)]
        branch_bits = [(seg_length // local_rows).bit_length() - 1 for seg_length in seg_lengths]
        row_spec = P(("groups", "seq"), None)
        return jax.shard_map(
            make_per_device(branch_bits),
            mesh=mesh,
            in_specs=(row_spec, row_spec, row_spec, row_spec, P()),
            out_specs=(row_spec, row_spec, row_spec, row_spec),
            check_vma=False,
        )(query_rows, key_rows, value_rows, output_grad, head_offsets)

    return run
```

```python
import math

import jax
import jax.numpy as jnp
from jax import lax
from jax.experimental import pallas as pl
from jax.experimental.pallas import tpu as pltpu
from jax.sharding import PartitionSpec as P

LEN_NEAR = 1024
LEN_MID = 4096
LEN_FAR = 16384
DILATION_FIRST = 1
DILATION_SECOND = 4
DILATION_THIRD = 16

NEG_FILL = -1e30
STRIDES = (DILATION_FIRST, DILATION_SECOND, DILATION_THIRD)


def exchange(block, bit):
    count = lax.axis_size("seq")
    route = [(index, index ^ (1 << bit)) for index in range(count)]
    return lax.ppermute(block, "seq", route)


def pick_rows(rows, stride, offsets_row):
    if stride == 1:
        return rows
    pair, count, width = rows.shape
    heads = offsets_row.shape[0]
    grouped = rows.reshape(pair, count // stride, stride, heads, width // heads)
    chosen = (jnp.arange(stride, dtype=jnp.int32)[:, None] == offsets_row[None, :])[
        None, None, :, :, None
    ]
    picked = jnp.sum(jnp.where(chosen, grouped, jnp.zeros((), rows.dtype)), axis=2)
    return picked.reshape(pair, count // stride, width)


def spread_rows(picked, stride, offsets_row):
    if stride == 1:
        return picked
    pair, count, width = picked.shape
    heads = offsets_row.shape[0]
    grouped = picked.reshape(pair, count, 1, heads, width // heads)
    chosen = (jnp.arange(stride, dtype=jnp.int32)[:, None] == offsets_row[None, :])[
        None, None, :, :, None
    ]
    widened = jnp.where(chosen, grouped, jnp.zeros((), picked.dtype))
    return widened.reshape(pair, count * stride, width)


def attention_kernel(head_dim, score_scale, head_base, half_counts):
    def kernel(offsets_ref, query_ref, grad_ref, mine_ref, arrived_ref, *refs):
        out_ref, qgrad_ref = refs[0:2]
        keep_refs = refs[2:5]
        message_ref = refs[5]
        pair = pl.program_id(0)
        rows = query_ref.shape[0]
        heads_per_block = query_ref.shape[1] // head_dim
        for sub in range(heads_per_block):
            head = head_base + pair * heads_per_block + sub
            cols = slice(sub * head_dim, (sub + 1) * head_dim)
            query = query_ref[:, cols]
            grad = grad_ref[:, cols]
            keys = []
            values = []
            start = 0
            for count in half_counts:
                keys.append(
                    jnp.concatenate(
                        [mine_ref[start : start + count, cols], arrived_ref[start : start + count, cols]]
                    )
                )
                values.append(
                    jnp.concatenate(
                        [
                            mine_ref[start + count : start + 2 * count, cols],
                            arrived_ref[start + count : start + 2 * count, cols],
                        ]
                    )
                )
                start += 2 * count
            members = []
            scores = []
            for branch in range(3):
                block = (
                    lax.dot_general(
                        query, keys[branch], (((1,), (1,)), ((), ())),
                        preferred_element_type=jnp.float32,
                    )
                    * score_scale
                )
                if STRIDES[branch] == 1:
                    member = None
                else:
                    row_index = lax.broadcasted_iota(jnp.int32, block.shape, 0)
                    member = (row_index % STRIDES[branch]) == offsets_ref[branch, head]
                    block = jnp.where(member, block, NEG_FILL)
                members.append(member)
                scores.append(block)
            peak = jnp.max(scores[0], axis=1, keepdims=True)
            for branch in range(1, 3):
                peak = jnp.maximum(peak, jnp.max(scores[branch], axis=1, keepdims=True))
            expos = []
            for branch in range(3):
                block = jnp.exp(scores[branch] - peak)
                if members[branch] is not None:
                    block = jnp.where(members[branch], block, 0.0)
                expos.append(block)
            total = jnp.sum(expos[0], axis=1, keepdims=True)
            for branch in range(1, 3):
                total = total + jnp.sum(expos[branch], axis=1, keepdims=True)
            probs = [block / total for block in expos]
            weights = [block.astype(jnp.bfloat16) for block in probs]
            mixed = jnp.dot(weights[0], values[0], preferred_element_type=jnp.float32)
            for branch in range(1, 3):
                mixed = mixed + jnp.dot(
                    weights[branch], values[branch], preferred_element_type=jnp.float32
                )
            out_ref[:, cols] = mixed.astype(out_ref.dtype)
            balance = jnp.sum(grad.astype(jnp.float32) * mixed, axis=1, keepdims=True)
            query_grad = None
            for branch in range(3):
                flow = lax.dot_general(
                    grad, values[branch], (((1,), (1,)), ((), ())),
                    preferred_element_type=jnp.float32,
                )
                score_grad = probs[branch] * (flow - balance)
                piece = jnp.dot(
                    score_grad.astype(jnp.bfloat16), keys[branch],
                    preferred_element_type=jnp.float32,
                )
                query_grad = piece if query_grad is None else query_grad + piece
                key_terms = (
                    lax.dot_general(
                        score_grad.astype(jnp.bfloat16), query, (((0,), (0,)), ((), ())),
                        preferred_element_type=jnp.float32,
                    )
                    * score_scale
                )
                value_terms = lax.dot_general(
                    weights[branch], grad, (((0,), (0,)), ((), ())),
                    preferred_element_type=jnp.float32,
                )
                half_keys = key_terms.shape[0] // 2
                start = 2 * sum(half_counts[:branch])
                keep_refs[branch][0, :, cols] = key_terms[:half_keys]
                keep_refs[branch][1, :, cols] = value_terms[:half_keys]
                message_ref[start : start + half_keys, cols] = key_terms[half_keys:].astype(
                    message_ref.dtype
                )
                message_ref[start + half_keys : start + 2 * half_keys, cols] = value_terms[
                    half_keys:
                ].astype(message_ref.dtype)
            qgrad_ref[:, cols] = (query_grad * score_scale).astype(qgrad_ref.dtype)

    return kernel


def gather_order(top_bits, swapped):
    order = list(reversed(range(top_bits)))
    if swapped and top_bits >= 3:
        first, second = order.index(1), order.index(2)
        order[first], order[second] = order[second], order[first]
    return order


def make_per_device(branch_bits):
    top_bits = max(branch_bits)

    def per_device(query_rows, key_rows, value_rows, output_grad, head_offsets):
        local_rows, model_width = query_rows.shape
        head_count = head_offsets.shape[1]
        head_dim = model_width // head_count
        score_scale = 1.0 / math.sqrt(head_dim)
        kv_rows = jnp.stack([key_rows, value_rows])
        picked = [
            pick_rows(kv_rows, STRIDES[branch], head_offsets[branch]) for branch in range(3)
        ]
        block_width = 128 if (128 % head_dim == 0 and model_width % 128 == 0) else model_width
        halves = 2 if model_width % (2 * block_width) == 0 else 1
        half_width = model_width // halves
        heads_per_half = head_count // halves

        gathered_halves = []
        layouts = []
        for half in range(halves):
            cols = slice(half * half_width, (half + 1) * half_width)
            buffers = [block[:, :, cols] for block in picked]
            axis_bits = [[] for _ in range(3)]
            order = gather_order(top_bits, half == 1)
            for bit in order[:-1]:
                active = [branch for branch in range(3) if branch_bits[branch] > bit]
                outgoing = jnp.concatenate(
                    [buffers[branch].reshape(-1, half_width) for branch in active]
                )
                incoming = exchange(outgoing, bit)
                cursor = 0
                for branch in active:
                    count = buffers[branch].size // half_width
                    arrived = incoming[cursor : cursor + count].reshape(buffers[branch].shape)
                    cursor += count
                    buffers[branch] = jnp.stack([buffers[branch], arrived], axis=1)
                    axis_bits[branch].insert(0, bit)
            for branch in range(3):
                axis_bits[branch].insert(0, order[-1])
            mine = jnp.concatenate([buffers[branch].reshape(-1, half_width) for branch in range(3)])
            half_counts = [buffers[branch].size // (2 * half_width) for branch in range(3)]
            gathered_halves.append((mine, exchange(mine, order[-1]), half_counts))
            layouts.append(axis_bits)

        results = []
        for half in range(halves):
            mine, arrived, half_counts = gathered_halves[half]
            cols = slice(half * half_width, (half + 1) * half_width)
            pairs = half_width // block_width
            key_rows_total = 2 * sum(half_counts)
            row_block = pl.BlockSpec((local_rows, block_width), lambda p, offs: (0, p))
            message_block = pl.BlockSpec((key_rows_total, block_width), lambda p, offs: (0, p))
            outs = pl.pallas_call(
                attention_kernel(head_dim, score_scale, half * heads_per_half, half_counts),
                out_shape=(
                    jax.ShapeDtypeStruct((local_rows, half_width), jnp.bfloat16),
                    jax.ShapeDtypeStruct((local_rows, half_width), jnp.bfloat16),
                )
                + tuple(
                    jax.ShapeDtypeStruct((2, count, half_width), jnp.float32)
                    for count in half_counts
                )
                + (jax.ShapeDtypeStruct((key_rows_total, half_width), jnp.bfloat16),),
                grid_spec=pltpu.PrefetchScalarGridSpec(
                    num_scalar_prefetch=1,
                    grid=(pairs,),
                    in_specs=[row_block, row_block, message_block, message_block],
                    out_specs=[row_block, row_block]
                    + [
                        pl.BlockSpec((2, count, block_width), lambda p, offs: (0, 0, p))
                        for count in half_counts
                    ]
                    + [message_block],
                ),
                compiler_params=pltpu.CompilerParams(vmem_limit_bytes=100 * 1024 * 1024),
            )(head_offsets, query_rows[:, cols], output_grad[:, cols], mine, arrived)
            attended, query_grad = outs[:2]
            kept_terms = outs[2:5]
            message = outs[5]

            axis_bits = [list(bits) for bits in layouts[half]]
            order = list(reversed(gather_order(top_bits, half == 1)))
            first = order[0]
            incoming = exchange(message, first).astype(jnp.float32)
            partial = []
            cursor = 0
            for branch in range(3):
                axis_bits[branch].remove(first)
                kept = kept_terms[branch].reshape(
                    (2,) + (2,) * len(axis_bits[branch]) + (-1, half_width)
                )
                count = kept.size // half_width
                partial.append(kept + incoming[cursor : cursor + count].reshape(kept.shape))
                cursor += count
            for bit in order[1:]:
                active = [branch for branch in range(3) if branch_bits[branch] > bit]
                places = {branch: 1 + axis_bits[branch].index(bit) for branch in active}
                outgoing = jnp.concatenate(
                    [
                        lax.index_in_dim(partial[branch], 1, places[branch], keepdims=False)
                        .reshape(-1, half_width)
                        .astype(jnp.bfloat16)
                        for branch in active
                    ]
                )
                incoming = exchange(outgoing, bit).astype(jnp.float32)
                cursor = 0
                for branch in active:
                    kept = lax.index_in_dim(partial[branch], 0, places[branch], keepdims=False)
                    count = kept.size // half_width
                    partial[branch] = kept + incoming[cursor : cursor + count].reshape(kept.shape)
                    cursor += count
                    axis_bits[branch].remove(bit)
            offsets_half = head_offsets[:, half * heads_per_half : (half + 1) * heads_per_half]
            total_grad = None
            for branch in range(3):
                spread = spread_rows(partial[branch], STRIDES[branch], offsets_half[branch])
                total_grad = spread if total_grad is None else total_grad + spread
            results.append((attended, query_grad, total_grad[0], total_grad[1]))

        return tuple(
            jnp.concatenate([result[index] for result in results], axis=1).astype(jnp.bfloat16)
            for index in range(4)
        )

    return per_device


def solution(mesh):
    group_count = mesh.shape["groups"]
    seq_devices = mesh.shape["seq"]

    def run(query_rows, key_rows, value_rows, output_grad, head_offsets):
        local_rows = query_rows.shape[0] // (group_count * seq_devices)
        tokens_all = seq_devices * local_rows
        seg_lengths = [min(LEN_NEAR, tokens_all), min(LEN_MID, tokens_all), min(LEN_FAR, tokens_all)]
        branch_bits = [(seg_length // local_rows).bit_length() - 1 for seg_length in seg_lengths]
        row_spec = P(("groups", "seq"), None)
        return jax.shard_map(
            make_per_device(branch_bits),
            mesh=mesh,
            in_specs=(row_spec, row_spec, row_spec, row_spec, P()),
            out_specs=(row_spec, row_spec, row_spec, row_spec),
            check_vma=False,
        )(query_rows, key_rows, value_rows, output_grad, head_offsets)

    return run
```

```python
import math

import jax
import jax.numpy as jnp
from jax import lax
from jax.experimental import pallas as pl
from jax.experimental.pallas import tpu as pltpu
from jax.sharding import PartitionSpec as P

LEN_NEAR = 1024
LEN_MID = 4096
LEN_FAR = 16384
DILATION_FIRST = 1
DILATION_SECOND = 4
DILATION_THIRD = 16

NEG_FILL = -1e30
STRIDES = (DILATION_FIRST, DILATION_SECOND, DILATION_THIRD)


def exchange(block, bit):
    count = lax.axis_size("seq")
    route = [(index, index ^ (1 << bit)) for index in range(count)]
    return lax.ppermute(block, "seq", route)


def pick_rows(rows, stride, offsets_row):
    if stride == 1:
        return rows
    pair, count, width = rows.shape
    heads = offsets_row.shape[0]
    grouped = rows.reshape(pair, count // stride, stride, heads, width // heads)
    chosen = (jnp.arange(stride, dtype=jnp.int32)[:, None] == offsets_row[None, :])[
        None, None, :, :, None
    ]
    picked = jnp.sum(jnp.where(chosen, grouped, jnp.zeros((), rows.dtype)), axis=2)
    return picked.reshape(pair, count // stride, width)


def spread_rows(picked, stride, offsets_row):
    if stride == 1:
        return picked
    pair, count, width = picked.shape
    heads = offsets_row.shape[0]
    grouped = picked.reshape(pair, count, 1, heads, width // heads)
    chosen = (jnp.arange(stride, dtype=jnp.int32)[:, None] == offsets_row[None, :]).astype(
        picked.dtype
    )[None, None, :, :, None]
    return (grouped * chosen).reshape(pair, count * stride, width)


def attention_kernel(head_dim, score_scale, head_base, half_counts):
    def kernel(offsets_ref, query_ref, grad_ref, mine_ref, arrived_ref, *refs):
        out_ref, qgrad_ref = refs[0:2]
        keep_refs = refs[2:5]
        message_ref = refs[5]
        pair = pl.program_id(0)
        rows = query_ref.shape[0]
        heads_per_block = query_ref.shape[1] // head_dim
        for sub in range(heads_per_block):
            head = head_base + pair * heads_per_block + sub
            cols = slice(sub * head_dim, (sub + 1) * head_dim)
            query = query_ref[:, cols]
            grad = grad_ref[:, cols]
            keys = []
            values = []
            start = 0
            for count in half_counts:
                keys.append(
                    jnp.concatenate(
                        [mine_ref[start : start + count, cols], arrived_ref[start : start + count, cols]]
                    )
                )
                values.append(
                    jnp.concatenate(
                        [
                            mine_ref[start + count : start + 2 * count, cols],
                            arrived_ref[start + count : start + 2 * count, cols],
                        ]
                    )
                )
                start += 2 * count
            members = []
            scores = []
            for branch in range(3):
                block = (
                    lax.dot_general(
                        query, keys[branch], (((1,), (1,)), ((), ())),
                        preferred_element_type=jnp.float32,
                    )
                    * score_scale
                )
                if STRIDES[branch] == 1:
                    member = None
                else:
                    row_index = lax.broadcasted_iota(jnp.int32, block.shape, 0)
                    member = (row_index % STRIDES[branch]) == offsets_ref[branch, head]
                    block = jnp.where(member, block, NEG_FILL)
                members.append(member)
                scores.append(block)
            peak = jnp.max(scores[0], axis=1, keepdims=True)
            for branch in range(1, 3):
                peak = jnp.maximum(peak, jnp.max(scores[branch], axis=1, keepdims=True))
            expos = []
            for branch in range(3):
                block = jnp.exp(scores[branch] - peak)
                if members[branch] is not None:
                    block = jnp.where(members[branch], block, 0.0)
                expos.append(block)
            total = jnp.sum(expos[0], axis=1, keepdims=True)
            for branch in range(1, 3):
                total = total + jnp.sum(expos[branch], axis=1, keepdims=True)
            probs = [block / total for block in expos]
            weights = [block.astype(jnp.bfloat16) for block in probs]
            mixed = jnp.dot(weights[0], values[0], preferred_element_type=jnp.float32)
            for branch in range(1, 3):
                mixed = mixed + jnp.dot(
                    weights[branch], values[branch], preferred_element_type=jnp.float32
                )
            out_ref[:, cols] = mixed.astype(out_ref.dtype)
            balance = jnp.sum(grad.astype(jnp.float32) * mixed, axis=1, keepdims=True)
            query_grad = None
            for branch in range(3):
                flow = lax.dot_general(
                    grad, values[branch], (((1,), (1,)), ((), ())),
                    preferred_element_type=jnp.float32,
                )
                score_grad = probs[branch] * (flow - balance)
                piece = jnp.dot(
                    score_grad.astype(jnp.bfloat16), keys[branch],
                    preferred_element_type=jnp.float32,
                )
                query_grad = piece if query_grad is None else query_grad + piece
                key_terms = (
                    lax.dot_general(
                        score_grad.astype(jnp.bfloat16), query, (((0,), (0,)), ((), ())),
                        preferred_element_type=jnp.float32,
                    )
                    * score_scale
                )
                value_terms = lax.dot_general(
                    weights[branch], grad, (((0,), (0,)), ((), ())),
                    preferred_element_type=jnp.float32,
                )
                half_keys = key_terms.shape[0] // 2
                start = 2 * sum(half_counts[:branch])
                keep_refs[branch][0, :, cols] = key_terms[:half_keys]
                keep_refs[branch][1, :, cols] = value_terms[:half_keys]
                message_ref[start : start + half_keys, cols] = key_terms[half_keys:].astype(
                    message_ref.dtype
                )
                message_ref[start + half_keys : start + 2 * half_keys, cols] = value_terms[
                    half_keys:
                ].astype(message_ref.dtype)
            qgrad_ref[:, cols] = (query_grad * score_scale).astype(qgrad_ref.dtype)

    return kernel


def gather_order(top_bits, swapped):
    order = list(reversed(range(top_bits)))
    if swapped and top_bits >= 3:
        first, second = order.index(1), order.index(2)
        order[first], order[second] = order[second], order[first]
    return order


def make_per_device(branch_bits):
    top_bits = max(branch_bits)

    def per_device(query_rows, key_rows, value_rows, output_grad, head_offsets):
        local_rows, model_width = query_rows.shape
        head_count = head_offsets.shape[1]
        head_dim = model_width // head_count
        score_scale = 1.0 / math.sqrt(head_dim)
        kv_rows = jnp.stack([key_rows, value_rows])
        picked = [
            pick_rows(kv_rows, STRIDES[branch], head_offsets[branch]) for branch in range(3)
        ]
        block_width = 128 if (128 % head_dim == 0 and model_width % 128 == 0) else model_width
        halves = 2 if model_width % (2 * block_width) == 0 else 1
        half_width = model_width // halves
        heads_per_half = head_count // halves

        gathered_halves = []
        layouts = []
        for half in range(halves):
            cols = slice(half * half_width, (half + 1) * half_width)
            buffers = [block[:, :, cols] for block in picked]
            axis_bits = [[] for _ in range(3)]
            order = gather_order(top_bits, half == 1)
            for bit in order[:-1]:
                active = [branch for branch in range(3) if branch_bits[branch] > bit]
                outgoing = jnp.concatenate(
                    [buffers[branch].reshape(-1, half_width) for branch in active]
                )
                incoming = exchange(outgoing, bit)
                cursor = 0
                for branch in active:
                    count = buffers[branch].size // half_width
                    arrived = incoming[cursor : cursor + count].reshape(buffers[branch].shape)
                    cursor += count
                    buffers[branch] = jnp.stack([buffers[branch], arrived], axis=1)
                    axis_bits[branch].insert(0, bit)
            for branch in range(3):
                axis_bits[branch].insert(0, order[-1])
            mine = jnp.concatenate([buffers[branch].reshape(-1, half_width) for branch in range(3)])
            half_counts = [buffers[branch].size // (2 * half_width) for branch in range(3)]
            gathered_halves.append((mine, exchange(mine, order[-1]), half_counts))
            layouts.append(axis_bits)

        results = []
        for half in range(halves):
            mine, arrived, half_counts = gathered_halves[half]
            cols = slice(half * half_width, (half + 1) * half_width)
            pairs = half_width // block_width
            key_rows_total = 2 * sum(half_counts)
            row_block = pl.BlockSpec((local_rows, block_width), lambda p, offs: (0, p))
            message_block = pl.BlockSpec((key_rows_total, block_width), lambda p, offs: (0, p))
            outs = pl.pallas_call(
                attention_kernel(head_dim, score_scale, half * heads_per_half, half_counts),
                out_shape=(
                    jax.ShapeDtypeStruct((local_rows, half_width), jnp.bfloat16),
                    jax.ShapeDtypeStruct((local_rows, half_width), jnp.bfloat16),
                )
                + tuple(
                    jax.ShapeDtypeStruct((2, count, half_width), jnp.float32)
                    for count in half_counts
                )
                + (jax.ShapeDtypeStruct((key_rows_total, half_width), jnp.bfloat16),),
                grid_spec=pltpu.PrefetchScalarGridSpec(
                    num_scalar_prefetch=1,
                    grid=(pairs,),
                    in_specs=[row_block, row_block, message_block, message_block],
                    out_specs=[row_block, row_block]
                    + [
                        pl.BlockSpec((2, count, block_width), lambda p, offs: (0, 0, p))
                        for count in half_counts
                    ]
                    + [message_block],
                ),
                compiler_params=pltpu.CompilerParams(vmem_limit_bytes=100 * 1024 * 1024),
            )(head_offsets, query_rows[:, cols], output_grad[:, cols], mine, arrived)
            attended, query_grad = outs[:2]
            kept_terms = outs[2:5]
            message = outs[5]

            axis_bits = [list(bits) for bits in layouts[half]]
            order = list(reversed(gather_order(top_bits, half == 1)))
            first = order[0]
            incoming = exchange(message, first).astype(jnp.float32)
            partial = []
            cursor = 0
            for branch in range(3):
                axis_bits[branch].remove(first)
                kept = kept_terms[branch].reshape(
                    (2,) + (2,) * len(axis_bits[branch]) + (-1, half_width)
                )
                count = kept.size // half_width
                partial.append(kept + incoming[cursor : cursor + count].reshape(kept.shape))
                cursor += count
            for bit in order[1:]:
                active = [branch for branch in range(3) if branch_bits[branch] > bit]
                places = {branch: 1 + axis_bits[branch].index(bit) for branch in active}
                outgoing = jnp.concatenate(
                    [
                        lax.index_in_dim(partial[branch], 1, places[branch], keepdims=False)
                        .reshape(-1, half_width)
                        .astype(jnp.bfloat16)
                        for branch in active
                    ]
                )
                incoming = exchange(outgoing, bit).astype(jnp.float32)
                cursor = 0
                for branch in active:
                    kept = lax.index_in_dim(partial[branch], 0, places[branch], keepdims=False)
                    count = kept.size // half_width
                    partial[branch] = kept + incoming[cursor : cursor + count].reshape(kept.shape)
                    cursor += count
                    axis_bits[branch].remove(bit)
            offsets_half = head_offsets[:, half * heads_per_half : (half + 1) * heads_per_half]
            total_grad = None
            for branch in range(3):
                spread = spread_rows(partial[branch], STRIDES[branch], offsets_half[branch])
                total_grad = spread if total_grad is None else total_grad + spread
            results.append((attended, query_grad, total_grad[0], total_grad[1]))

        return tuple(
            jnp.concatenate([result[index] for result in results], axis=1).astype(jnp.bfloat16)
            for index in range(4)
        )

    return per_device


def solution(mesh):
    group_count = mesh.shape["groups"]
    seq_devices = mesh.shape["seq"]

    def run(query_rows, key_rows, value_rows, output_grad, head_offsets):
        local_rows = query_rows.shape[0] // (group_count * seq_devices)
        tokens_all = seq_devices * local_rows
        seg_lengths = [min(LEN_NEAR, tokens_all), min(LEN_MID, tokens_all), min(LEN_FAR, tokens_all)]
        branch_bits = [(seg_length // local_rows).bit_length() - 1 for seg_length in seg_lengths]
        row_spec = P(("groups", "seq"), None)
        return jax.shard_map(
            make_per_device(branch_bits),
            mesh=mesh,
            in_specs=(row_spec, row_spec, row_spec, row_spec, P()),
            out_specs=(row_spec, row_spec, row_spec, row_spec),
            check_vma=False,
        )(query_rows, key_rows, value_rows, output_grad, head_offsets)

    return run
```

```python
import math

import jax
import jax.numpy as jnp
from jax import lax
from jax.experimental import pallas as pl
from jax.experimental.pallas import tpu as pltpu
from jax.sharding import PartitionSpec as P

LEN_NEAR = 1024
LEN_MID = 4096
LEN_FAR = 16384
DILATION_FIRST = 1
DILATION_SECOND = 4
DILATION_THIRD = 16

NEG_FILL = -1e30
STRIDES = (DILATION_FIRST, DILATION_SECOND, DILATION_THIRD)


def exchange(block, bit):
    count = lax.axis_size("seq")
    route = [(index, index ^ (1 << bit)) for index in range(count)]
    return lax.ppermute(block, "seq", route)


def pick_rows(rows, stride, offsets_row):
    if stride == 1:
        return rows
    pair, count, width = rows.shape
    heads = offsets_row.shape[0]
    grouped = rows.reshape(pair, count // stride, stride, heads, width // heads)
    chosen = (jnp.arange(stride, dtype=jnp.int32)[:, None] == offsets_row[None, :])[
        None, None, :, :, None
    ]
    picked = jnp.sum(jnp.where(chosen, grouped, jnp.zeros((), rows.dtype)), axis=2)
    return picked.reshape(pair, count // stride, width)


def spread_rows(picked, stride, offsets_row):
    if stride == 1:
        return picked
    pair, count, width = picked.shape
    heads = offsets_row.shape[0]
    grouped = picked.reshape(pair, count, 1, heads, width // heads)
    chosen = (jnp.arange(stride, dtype=jnp.int32)[:, None] == offsets_row[None, :]).astype(
        picked.dtype
    )[None, None, :, :, None]
    return (grouped * chosen).reshape(pair, count * stride, width)


def attention_kernel(head_dim, score_scale, head_base, half_counts, aliased):
    def kernel(offsets_ref, query_ref, grad_ref, mine_ref, arrived_ref, *refs):
        refs = refs[aliased:]
        out_ref, qgrad_ref = refs[0:2]
        keep_refs = refs[2:5]
        message_ref = refs[5]
        pair = pl.program_id(0)
        rows = query_ref.shape[0]
        heads_per_block = query_ref.shape[1] // head_dim
        for sub in range(heads_per_block):
            head = head_base + pair * heads_per_block + sub
            cols = slice(sub * head_dim, (sub + 1) * head_dim)
            query = query_ref[:, cols]
            grad = grad_ref[:, cols]
            keys = []
            values = []
            start = 0
            for count in half_counts:
                keys.append(
                    jnp.concatenate(
                        [mine_ref[start : start + count, cols], arrived_ref[start : start + count, cols]]
                    )
                )
                values.append(
                    jnp.concatenate(
                        [
                            mine_ref[start + count : start + 2 * count, cols],
                            arrived_ref[start + count : start + 2 * count, cols],
                        ]
                    )
                )
                start += 2 * count
            members = []
            scores = []
            for branch in range(3):
                block = (
                    lax.dot_general(
                        query, keys[branch], (((1,), (1,)), ((), ())),
                        preferred_element_type=jnp.float32,
                    )
                    * score_scale
                )
                if STRIDES[branch] == 1:
                    member = None
                else:
                    row_index = lax.broadcasted_iota(jnp.int32, block.shape, 0)
                    member = (row_index % STRIDES[branch]) == offsets_ref[branch, head]
                    block = jnp.where(member, block, NEG_FILL)
                members.append(member)
                scores.append(block)
            peak = jnp.max(scores[0], axis=1, keepdims=True)
            for branch in range(1, 3):
                peak = jnp.maximum(peak, jnp.max(scores[branch], axis=1, keepdims=True))
            expos = []
            for branch in range(3):
                block = jnp.exp(scores[branch] - peak)
                if members[branch] is not None:
                    block = jnp.where(members[branch], block, 0.0)
                expos.append(block)
            total = jnp.sum(expos[0], axis=1, keepdims=True)
            for branch in range(1, 3):
                total = total + jnp.sum(expos[branch], axis=1, keepdims=True)
            probs = [block / total for block in expos]
            weights = [block.astype(jnp.bfloat16) for block in probs]
            mixed = jnp.dot(weights[0], values[0], preferred_element_type=jnp.float32)
            for branch in range(1, 3):
                mixed = mixed + jnp.dot(
                    weights[branch], values[branch], preferred_element_type=jnp.float32
                )
            out_ref[:, cols] = mixed.astype(out_ref.dtype)
            balance = jnp.sum(grad.astype(jnp.float32) * mixed, axis=1, keepdims=True)
            query_grad = None
            for branch in range(3):
                flow = lax.dot_general(
                    grad, values[branch], (((1,), (1,)), ((), ())),
                    preferred_element_type=jnp.float32,
                )
                score_grad = probs[branch] * (flow - balance)
                piece = jnp.dot(
                    score_grad.astype(jnp.bfloat16), keys[branch],
                    preferred_element_type=jnp.float32,
                )
                query_grad = piece if query_grad is None else query_grad + piece
                key_terms = (
                    lax.dot_general(
                        score_grad.astype(jnp.bfloat16), query, (((0,), (0,)), ((), ())),
                        preferred_element_type=jnp.float32,
                    )
                    * score_scale
                )
                value_terms = lax.dot_general(
                    weights[branch], grad, (((0,), (0,)), ((), ())),
                    preferred_element_type=jnp.float32,
                )
                half_keys = key_terms.shape[0] // 2
                start = 2 * sum(half_counts[:branch])
                keep_refs[branch][0, :, cols] = key_terms[:half_keys]
                keep_refs[branch][1, :, cols] = value_terms[:half_keys]
                message_ref[start : start + half_keys, cols] = key_terms[half_keys:].astype(
                    message_ref.dtype
                )
                message_ref[start + half_keys : start + 2 * half_keys, cols] = value_terms[
                    half_keys:
                ].astype(message_ref.dtype)
            qgrad_ref[:, cols] = (query_grad * score_scale).astype(qgrad_ref.dtype)

    return kernel


def gather_order(top_bits, swapped):
    order = list(reversed(range(top_bits)))
    if swapped and top_bits >= 3:
        first, second = order.index(1), order.index(2)
        order[first], order[second] = order[second], order[first]
    return order


def make_per_device(branch_bits):
    top_bits = max(branch_bits)

    def per_device(query_rows, key_rows, value_rows, output_grad, head_offsets):
        local_rows, model_width = query_rows.shape
        head_count = head_offsets.shape[1]
        head_dim = model_width // head_count
        score_scale = 1.0 / math.sqrt(head_dim)
        kv_rows = jnp.stack([key_rows, value_rows])
        picked = [
            pick_rows(kv_rows, STRIDES[branch], head_offsets[branch]) for branch in range(3)
        ]
        block_width = 128 if (128 % head_dim == 0 and model_width % 128 == 0) else model_width
        halves = 2 if model_width % (2 * block_width) == 0 else 1
        half_width = model_width // halves
        heads_per_half = head_count // halves

        gathered_halves = []
        layouts = []
        for half in range(halves):
            cols = slice(half * half_width, (half + 1) * half_width)
            buffers = [block[:, :, cols] for block in picked]
            axis_bits = [[] for _ in range(3)]
            order = gather_order(top_bits, half == 1)
            for bit in order[:-1]:
                active = [branch for branch in range(3) if branch_bits[branch] > bit]
                outgoing = jnp.concatenate(
                    [buffers[branch].reshape(-1, half_width) for branch in active]
                )
                incoming = exchange(outgoing, bit)
                cursor = 0
                for branch in active:
                    count = buffers[branch].size // half_width
                    arrived = incoming[cursor : cursor + count].reshape(buffers[branch].shape)
                    cursor += count
                    buffers[branch] = jnp.stack([buffers[branch], arrived], axis=1)
                    axis_bits[branch].insert(0, bit)
            for branch in range(3):
                axis_bits[branch].insert(0, order[-1])
            mine = jnp.concatenate([buffers[branch].reshape(-1, half_width) for branch in range(3)])
            half_counts = [buffers[branch].size // (2 * half_width) for branch in range(3)]
            gathered_halves.append((mine, exchange(mine, order[-1]), half_counts))
            layouts.append(axis_bits)

        results = []
        full_outs = ()
        for half in range(halves):
            mine, arrived, half_counts = gathered_halves[half]
            cols = slice(half * half_width, (half + 1) * half_width)
            pairs = half_width // block_width
            key_rows_total = 2 * sum(half_counts)
            row_block = pl.BlockSpec((local_rows, block_width), lambda p, offs: (0, p))
            wide_block = pl.BlockSpec(
                (local_rows, block_width), lambda p, offs, base=half * pairs: (0, p + base)
            )
            message_block = pl.BlockSpec((key_rows_total, block_width), lambda p, offs: (0, p))
            outs = pl.pallas_call(
                attention_kernel(
                    head_dim, score_scale, half * heads_per_half, half_counts, len(full_outs)
                ),
                out_shape=(
                    jax.ShapeDtypeStruct((local_rows, model_width), jnp.bfloat16),
                    jax.ShapeDtypeStruct((local_rows, model_width), jnp.bfloat16),
                )
                + tuple(
                    jax.ShapeDtypeStruct((2, count, half_width), jnp.float32)
                    for count in half_counts
                )
                + (jax.ShapeDtypeStruct((key_rows_total, half_width), jnp.bfloat16),),
                grid_spec=pltpu.PrefetchScalarGridSpec(
                    num_scalar_prefetch=1,
                    grid=(pairs,),
                    in_specs=[row_block, row_block, message_block, message_block]
                    + [pl.BlockSpec(memory_space=pl.ANY) for _ in full_outs],
                    out_specs=[wide_block, wide_block]
                    + [
                        pl.BlockSpec((2, count, block_width), lambda p, offs: (0, 0, p))
                        for count in half_counts
                    ]
                    + [message_block],
                ),
                input_output_aliases={5 + index: index for index in range(len(full_outs))},
                compiler_params=pltpu.CompilerParams(vmem_limit_bytes=100 * 1024 * 1024),
            )(head_offsets, query_rows[:, cols], output_grad[:, cols], mine, arrived, *full_outs)
            full_outs = tuple(outs[:2])
            kept_terms = outs[2:5]
            message = outs[5]

            axis_bits = [list(bits) for bits in layouts[half]]
            order = list(reversed(gather_order(top_bits, half == 1)))
            first = order[0]
            incoming = exchange(message, first).astype(jnp.float32)
            partial = []
            cursor = 0
            for branch in range(3):
                axis_bits[branch].remove(first)
                kept = kept_terms[branch].reshape(
                    (2,) + (2,) * len(axis_bits[branch]) + (-1, half_width)
                )
                count = kept.size // half_width
                partial.append(kept + incoming[cursor : cursor + count].reshape(kept.shape))
                cursor += count
            for bit in order[1:]:
                active = [branch for branch in range(3) if branch_bits[branch] > bit]
                places = {branch: 1 + axis_bits[branch].index(bit) for branch in active}
                outgoing = jnp.concatenate(
                    [
                        lax.index_in_dim(partial[branch], 1, places[branch], keepdims=False)
                        .reshape(-1, half_width)
                        .astype(jnp.bfloat16)
                        for branch in active
                    ]
                )
                incoming = exchange(outgoing, bit).astype(jnp.float32)
                cursor = 0
                for branch in active:
                    kept = lax.index_in_dim(partial[branch], 0, places[branch], keepdims=False)
                    count = kept.size // half_width
                    partial[branch] = kept + incoming[cursor : cursor + count].reshape(kept.shape)
                    cursor += count
                    axis_bits[branch].remove(bit)
            offsets_half = head_offsets[:, half * heads_per_half : (half + 1) * heads_per_half]
            total_grad = None
            for branch in range(3):
                spread = spread_rows(partial[branch], STRIDES[branch], offsets_half[branch])
                total_grad = spread if total_grad is None else total_grad + spread
            results.append((total_grad[0], total_grad[1]))

        return full_outs + tuple(
            jnp.concatenate([result[index] for result in results], axis=1).astype(jnp.bfloat16)
            for index in range(2)
        )

    return per_device


def solution(mesh):
    group_count = mesh.shape["groups"]
    seq_devices = mesh.shape["seq"]

    def run(query_rows, key_rows, value_rows, output_grad, head_offsets):
        local_rows = query_rows.shape[0] // (group_count * seq_devices)
        tokens_all = seq_devices * local_rows
        seg_lengths = [min(LEN_NEAR, tokens_all), min(LEN_MID, tokens_all), min(LEN_FAR, tokens_all)]
        branch_bits = [(seg_length // local_rows).bit_length() - 1 for seg_length in seg_lengths]
        row_spec = P(("groups", "seq"), None)
        return jax.shard_map(
            make_per_device(branch_bits),
            mesh=mesh,
            in_specs=(row_spec, row_spec, row_spec, row_spec, P()),
            out_specs=(row_spec, row_spec, row_spec, row_spec),
            check_vma=False,
        )(query_rows, key_rows, value_rows, output_grad, head_offsets)

    return run
```

```python
import math

import jax
import jax.numpy as jnp
from jax import lax
from jax.experimental import pallas as pl
from jax.experimental.pallas import tpu as pltpu
from jax.sharding import PartitionSpec as P

LEN_NEAR = 1024
LEN_MID = 4096
LEN_FAR = 16384
DILATION_FIRST = 1
DILATION_SECOND = 4
DILATION_THIRD = 16

NEG_FILL = -1e30
STRIDES = (DILATION_FIRST, DILATION_SECOND, DILATION_THIRD)


def exchange(block, bit):
    count = lax.axis_size("seq")
    route = [(index, index ^ (1 << bit)) for index in range(count)]
    return lax.ppermute(block, "seq", route)


def pick_rows(rows, stride, offsets_row):
    if stride == 1:
        return rows
    pair, count, width = rows.shape
    heads = offsets_row.shape[0]
    grouped = rows.reshape(pair, count // stride, stride, heads, width // heads)
    chosen = (jnp.arange(stride, dtype=jnp.int32)[:, None] == offsets_row[None, :])[
        None, None, :, :, None
    ]
    picked = jnp.sum(jnp.where(chosen, grouped, jnp.zeros((), rows.dtype)), axis=2)
    return picked.reshape(pair, count // stride, width)


def spread_rows(picked, stride, offsets_row):
    if stride == 1:
        return picked
    pair, count, width = picked.shape
    heads = offsets_row.shape[0]
    grouped = picked.reshape(pair, count, 1, heads, width // heads)
    chosen = (jnp.arange(stride, dtype=jnp.int32)[:, None] == offsets_row[None, :]).astype(
        picked.dtype
    )[None, None, :, :, None]
    return (grouped * chosen).reshape(pair, count * stride, width)


def attention_kernel(head_dim, score_scale, head_base, half_counts, aliased):
    def kernel(offsets_ref, query_ref, grad_ref, mine_ref, arrived_ref, *refs):
        refs = refs[aliased:]
        out_ref, qgrad_ref = refs[0:2]
        keep_refs = refs[2:5]
        message_ref = refs[5]
        pair = pl.program_id(0)
        rows = query_ref.shape[0]
        heads_per_block = query_ref.shape[1] // head_dim
        for sub in range(heads_per_block):
            head = head_base + pair * heads_per_block + sub
            cols = slice(sub * head_dim, (sub + 1) * head_dim)
            query = query_ref[:, cols]
            grad = grad_ref[:, cols]
            keys = []
            values = []
            start = 0
            for count in half_counts:
                keys.append(
                    jnp.concatenate(
                        [mine_ref[start : start + count, cols], arrived_ref[start : start + count, cols]]
                    )
                )
                values.append(
                    jnp.concatenate(
                        [
                            mine_ref[start + count : start + 2 * count, cols],
                            arrived_ref[start + count : start + 2 * count, cols],
                        ]
                    )
                )
                start += 2 * count
            members = []
            scores = []
            for branch in range(3):
                block = (
                    lax.dot_general(
                        query, keys[branch], (((1,), (1,)), ((), ())),
                        preferred_element_type=jnp.float32,
                    )
                    * score_scale
                )
                if STRIDES[branch] == 1:
                    member = None
                else:
                    row_index = lax.broadcasted_iota(jnp.int32, block.shape, 0)
                    member = (row_index % STRIDES[branch]) == offsets_ref[branch, head]
                    block = jnp.where(member, block, NEG_FILL)
                members.append(member)
                scores.append(block)
            peak = jnp.max(scores[0], axis=1, keepdims=True)
            for branch in range(1, 3):
                peak = jnp.maximum(peak, jnp.max(scores[branch], axis=1, keepdims=True))
            expos = []
            for branch in range(3):
                block = jnp.exp(scores[branch] - peak)
                if members[branch] is not None:
                    block = jnp.where(members[branch], block, 0.0)
                expos.append(block)
            total = jnp.sum(expos[0], axis=1, keepdims=True)
            for branch in range(1, 3):
                total = total + jnp.sum(expos[branch], axis=1, keepdims=True)
            inverse = 1.0 / total
            probs = [block * inverse for block in expos]
            weights = [block.astype(jnp.bfloat16) for block in probs]
            mixed = jnp.dot(weights[0], values[0], preferred_element_type=jnp.float32)
            for branch in range(1, 3):
                mixed = mixed + jnp.dot(
                    weights[branch], values[branch], preferred_element_type=jnp.float32
                )
            out_ref[:, cols] = mixed.astype(out_ref.dtype)
            balance = jnp.sum(grad.astype(jnp.float32) * mixed, axis=1, keepdims=True)
            query_grad = None
            for branch in range(3):
                flow = lax.dot_general(
                    grad, values[branch], (((1,), (1,)), ((), ())),
                    preferred_element_type=jnp.float32,
                )
                score_grad = probs[branch] * (flow - balance)
                piece = jnp.dot(
                    score_grad.astype(jnp.bfloat16), keys[branch],
                    preferred_element_type=jnp.float32,
                )
                query_grad = piece if query_grad is None else query_grad + piece
                key_terms = (
                    lax.dot_general(
                        score_grad.astype(jnp.bfloat16), query, (((0,), (0,)), ((), ())),
                        preferred_element_type=jnp.float32,
                    )
                    * score_scale
                )
                value_terms = lax.dot_general(
                    weights[branch], grad, (((0,), (0,)), ((), ())),
                    preferred_element_type=jnp.float32,
                )
                half_keys = key_terms.shape[0] // 2
                start = 2 * sum(half_counts[:branch])
                keep_refs[branch][0, :, cols] = key_terms[:half_keys]
                keep_refs[branch][1, :, cols] = value_terms[:half_keys]
                message_ref[start : start + half_keys, cols] = key_terms[half_keys:].astype(
                    message_ref.dtype
                )
                message_ref[start + half_keys : start + 2 * half_keys, cols] = value_terms[
                    half_keys:
                ].astype(message_ref.dtype)
            qgrad_ref[:, cols] = (query_grad * score_scale).astype(qgrad_ref.dtype)

    return kernel


def gather_order(top_bits, swapped):
    order = list(reversed(range(top_bits)))
    if swapped and top_bits >= 3:
        first, second = order.index(1), order.index(2)
        order[first], order[second] = order[second], order[first]
    return order


def make_per_device(branch_bits):
    top_bits = max(branch_bits)

    def per_device(query_rows, key_rows, value_rows, output_grad, head_offsets):
        local_rows, model_width = query_rows.shape
        head_count = head_offsets.shape[1]
        head_dim = model_width // head_count
        score_scale = 1.0 / math.sqrt(head_dim)
        kv_rows = jnp.stack([key_rows, value_rows])
        picked = [
            pick_rows(kv_rows, STRIDES[branch], head_offsets[branch]) for branch in range(3)
        ]
        block_width = 128 if (128 % head_dim == 0 and model_width % 128 == 0) else model_width
        halves = 2 if model_width % (2 * block_width) == 0 else 1
        half_width = model_width // halves
        heads_per_half = head_count // halves

        gathered_halves = []
        layouts = []
        for half in range(halves):
            cols = slice(half * half_width, (half + 1) * half_width)
            buffers = [block[:, :, cols] for block in picked]
            axis_bits = [[] for _ in range(3)]
            order = gather_order(top_bits, half == 1)
            for bit in order[:-1]:
                active = [branch for branch in range(3) if branch_bits[branch] > bit]
                outgoing = jnp.concatenate(
                    [buffers[branch].reshape(-1, half_width) for branch in active]
                )
                incoming = exchange(outgoing, bit)
                cursor = 0
                for branch in active:
                    count = buffers[branch].size // half_width
                    arrived = incoming[cursor : cursor + count].reshape(buffers[branch].shape)
                    cursor += count
                    buffers[branch] = jnp.stack([buffers[branch], arrived], axis=1)
                    axis_bits[branch].insert(0, bit)
            for branch in range(3):
                axis_bits[branch].insert(0, order[-1])
            mine = jnp.concatenate([buffers[branch].reshape(-1, half_width) for branch in range(3)])
            half_counts = [buffers[branch].size // (2 * half_width) for branch in range(3)]
            gathered_halves.append((mine, exchange(mine, order[-1]), half_counts))
            layouts.append(axis_bits)

        results = []
        full_outs = ()
        for half in range(halves):
            mine, arrived, half_counts = gathered_halves[half]
            cols = slice(half * half_width, (half + 1) * half_width)
            pairs = half_width // block_width
            key_rows_total = 2 * sum(half_counts)
            row_block = pl.BlockSpec((local_rows, block_width), lambda p, offs: (0, p))
            wide_block = pl.BlockSpec(
                (local_rows, block_width), lambda p, offs, base=half * pairs: (0, p + base)
            )
            message_block = pl.BlockSpec((key_rows_total, block_width), lambda p, offs: (0, p))
            outs = pl.pallas_call(
                attention_kernel(
                    head_dim, score_scale, half * heads_per_half, half_counts, len(full_outs)
                ),
                out_shape=(
                    jax.ShapeDtypeStruct((local_rows, model_width), jnp.bfloat16),
                    jax.ShapeDtypeStruct((local_rows, model_width), jnp.bfloat16),
                )
                + tuple(
                    jax.ShapeDtypeStruct((2, count, half_width), jnp.float32)
                    for count in half_counts
                )
                + (jax.ShapeDtypeStruct((key_rows_total, half_width), jnp.bfloat16),),
                grid_spec=pltpu.PrefetchScalarGridSpec(
                    num_scalar_prefetch=1,
                    grid=(pairs,),
                    in_specs=[row_block, row_block, message_block, message_block]
                    + [pl.BlockSpec(memory_space=pl.ANY) for _ in full_outs],
                    out_specs=[wide_block, wide_block]
                    + [
                        pl.BlockSpec((2, count, block_width), lambda p, offs: (0, 0, p))
                        for count in half_counts
                    ]
                    + [message_block],
                ),
                input_output_aliases={5 + index: index for index in range(len(full_outs))},
                compiler_params=pltpu.CompilerParams(vmem_limit_bytes=100 * 1024 * 1024),
            )(head_offsets, query_rows[:, cols], output_grad[:, cols], mine, arrived, *full_outs)
            full_outs = tuple(outs[:2])
            kept_terms = outs[2:5]
            message = outs[5]

            axis_bits = [list(bits) for bits in layouts[half]]
            order = list(reversed(gather_order(top_bits, half == 1)))
            first = order[0]
            incoming = exchange(message, first).astype(jnp.float32)
            partial = []
            cursor = 0
            for branch in range(3):
                axis_bits[branch].remove(first)
                kept = kept_terms[branch].reshape(
                    (2,) + (2,) * len(axis_bits[branch]) + (-1, half_width)
                )
                count = kept.size // half_width
                partial.append(kept + incoming[cursor : cursor + count].reshape(kept.shape))
                cursor += count
            for bit in order[1:]:
                active = [branch for branch in range(3) if branch_bits[branch] > bit]
                places = {branch: 1 + axis_bits[branch].index(bit) for branch in active}
                outgoing = jnp.concatenate(
                    [
                        lax.index_in_dim(partial[branch], 1, places[branch], keepdims=False)
                        .reshape(-1, half_width)
                        .astype(jnp.bfloat16)
                        for branch in active
                    ]
                )
                incoming = exchange(outgoing, bit).astype(jnp.float32)
                cursor = 0
                for branch in active:
                    kept = lax.index_in_dim(partial[branch], 0, places[branch], keepdims=False)
                    count = kept.size // half_width
                    partial[branch] = kept + incoming[cursor : cursor + count].reshape(kept.shape)
                    cursor += count
                    axis_bits[branch].remove(bit)
            offsets_half = head_offsets[:, half * heads_per_half : (half + 1) * heads_per_half]
            total_grad = None
            for branch in range(3):
                spread = spread_rows(partial[branch], STRIDES[branch], offsets_half[branch])
                total_grad = spread if total_grad is None else total_grad + spread
            results.append((total_grad[0], total_grad[1]))

        return full_outs + tuple(
            jnp.concatenate([result[index] for result in results], axis=1).astype(jnp.bfloat16)
            for index in range(2)
        )

    return per_device


def solution(mesh):
    group_count = mesh.shape["groups"]
    seq_devices = mesh.shape["seq"]

    def run(query_rows, key_rows, value_rows, output_grad, head_offsets):
        local_rows = query_rows.shape[0] // (group_count * seq_devices)
        tokens_all = seq_devices * local_rows
        seg_lengths = [min(LEN_NEAR, tokens_all), min(LEN_MID, tokens_all), min(LEN_FAR, tokens_all)]
        branch_bits = [(seg_length // local_rows).bit_length() - 1 for seg_length in seg_lengths]
        row_spec = P(("groups", "seq"), None)
        return jax.shard_map(
            make_per_device(branch_bits),
            mesh=mesh,
            in_specs=(row_spec, row_spec, row_spec, row_spec, P()),
            out_specs=(row_spec, row_spec, row_spec, row_spec),
            check_vma=False,
        )(query_rows, key_rows, value_rows, output_grad, head_offsets)

    return run
```

```python
import math

import jax
import jax.numpy as jnp
from jax import lax
from jax.experimental import pallas as pl
from jax.experimental.pallas import tpu as pltpu
from jax.sharding import PartitionSpec as P

LEN_NEAR = 1024
LEN_MID = 4096
LEN_FAR = 16384
DILATION_FIRST = 1
DILATION_SECOND = 4
DILATION_THIRD = 16

NEG_FILL = -1e30
STRIDES = (DILATION_FIRST, DILATION_SECOND, DILATION_THIRD)


def exchange(block, bit):
    count = lax.axis_size("seq")
    route = [(index, index ^ (1 << bit)) for index in range(count)]
    return lax.ppermute(block, "seq", route)


def pick_rows(rows, stride, offsets_row):
    if stride == 1:
        return rows
    pair, count, width = rows.shape
    heads = offsets_row.shape[0]
    grouped = rows.reshape(pair, count // stride, stride, heads, width // heads)
    chosen = (jnp.arange(stride, dtype=jnp.int32)[:, None] == offsets_row[None, :])[
        None, None, :, :, None
    ]
    picked = jnp.sum(jnp.where(chosen, grouped, jnp.zeros((), rows.dtype)), axis=2)
    return picked.reshape(pair, count // stride, width)


def spread_rows(picked, stride, offsets_row):
    if stride == 1:
        return picked
    pair, count, width = picked.shape
    heads = offsets_row.shape[0]
    grouped = picked.reshape(pair, count, 1, heads, width // heads)
    chosen = (jnp.arange(stride, dtype=jnp.int32)[:, None] == offsets_row[None, :]).astype(
        picked.dtype
    )[None, None, :, :, None]
    return (grouped * chosen).reshape(pair, count * stride, width)


def attention_kernel(head_dim, score_scale, head_base, half_counts, aliased):
    def kernel(offsets_ref, query_ref, grad_ref, mine_ref, arrived_ref, *refs):
        refs = refs[aliased:]
        out_ref, qgrad_ref = refs[0:2]
        keep_refs = refs[2:5]
        message_ref = refs[5]
        pair = pl.program_id(0)
        rows = query_ref.shape[0]
        heads_per_block = query_ref.shape[1] // head_dim
        for sub in range(heads_per_block):
            head = head_base + pair * heads_per_block + sub
            cols = slice(sub * head_dim, (sub + 1) * head_dim)
            query = query_ref[:, cols]
            grad = grad_ref[:, cols]
            keys = []
            values = []
            start = 0
            for count in half_counts:
                keys.append(
                    jnp.concatenate(
                        [mine_ref[start : start + count, cols], arrived_ref[start : start + count, cols]]
                    )
                )
                values.append(
                    jnp.concatenate(
                        [
                            mine_ref[start + count : start + 2 * count, cols],
                            arrived_ref[start + count : start + 2 * count, cols],
                        ]
                    )
                )
                start += 2 * count
            members = []
            scores = []
            for branch in range(3):
                block = (
                    lax.dot_general(
                        query, keys[branch], (((1,), (1,)), ((), ())),
                        preferred_element_type=jnp.float32,
                    )
                    * score_scale
                )
                if STRIDES[branch] == 1:
                    member = None
                else:
                    row_index = lax.broadcasted_iota(jnp.int32, block.shape, 0)
                    member = (row_index % STRIDES[branch]) == offsets_ref[branch, head]
                    block = jnp.where(member, block, NEG_FILL)
                members.append(member)
                scores.append(block)
            peak = jnp.max(scores[0], axis=1, keepdims=True)
            for branch in range(1, 3):
                peak = jnp.maximum(peak, jnp.max(scores[branch], axis=1, keepdims=True))
            expos = []
            for branch in range(3):
                block = jnp.exp(scores[branch] - peak)
                if members[branch] is not None:
                    block = jnp.where(members[branch], block, 0.0)
                expos.append(block)
            total = jnp.sum(expos[0], axis=1, keepdims=True)
            for branch in range(1, 3):
                total = total + jnp.sum(expos[branch], axis=1, keepdims=True)
            probs = [block / total for block in expos]
            weights = [block.astype(jnp.bfloat16) for block in probs]
            mixed = jnp.dot(weights[0], values[0], preferred_element_type=jnp.float32)
            for branch in range(1, 3):
                mixed = mixed + jnp.dot(
                    weights[branch], values[branch], preferred_element_type=jnp.float32
                )
            out_ref[:, cols] = mixed.astype(out_ref.dtype)
            balance = jnp.sum(grad.astype(jnp.float32) * mixed, axis=1, keepdims=True)
            query_grad = None
            for branch in range(3):
                flow = lax.dot_general(
                    grad, values[branch], (((1,), (1,)), ((), ())),
                    preferred_element_type=jnp.float32,
                )
                score_grad = probs[branch] * (flow - balance)
                piece = jnp.dot(
                    score_grad.astype(jnp.bfloat16), keys[branch],
                    preferred_element_type=jnp.float32,
                )
                query_grad = piece if query_grad is None else query_grad + piece
                key_terms = (
                    lax.dot_general(
                        score_grad.astype(jnp.bfloat16), query, (((0,), (0,)), ((), ())),
                        preferred_element_type=jnp.float32,
                    )
                    * score_scale
                )
                value_terms = lax.dot_general(
                    weights[branch], grad, (((0,), (0,)), ((), ())),
                    preferred_element_type=jnp.float32,
                )
                half_keys = key_terms.shape[0] // 2
                start = 2 * sum(half_counts[:branch])
                keep_refs[branch][0, :, cols] = key_terms[:half_keys]
                keep_refs[branch][1, :, cols] = value_terms[:half_keys]
                message_ref[start : start + half_keys, cols] = key_terms[half_keys:].astype(
                    message_ref.dtype
                )
                message_ref[start + half_keys : start + 2 * half_keys, cols] = value_terms[
                    half_keys:
                ].astype(message_ref.dtype)
            qgrad_ref[:, cols] = (query_grad * score_scale).astype(qgrad_ref.dtype)

    return kernel


def gather_order(top_bits, swapped):
    order = list(reversed(range(top_bits)))
    if swapped and top_bits >= 3:
        first, second = order.index(1), order.index(2)
        order[first], order[second] = order[second], order[first]
    return order


def make_per_device(branch_bits):
    top_bits = max(branch_bits)

    def per_device(query_rows, key_rows, value_rows, output_grad, head_offsets):
        local_rows, model_width = query_rows.shape
        head_count = head_offsets.shape[1]
        head_dim = model_width // head_count
        score_scale = 1.0 / math.sqrt(head_dim)
        kv_rows = jnp.stack([key_rows, value_rows])
        picked = [
            pick_rows(kv_rows, STRIDES[branch], head_offsets[branch]) for branch in range(3)
        ]
        block_width = 128 if (128 % head_dim == 0 and model_width % 128 == 0) else model_width
        halves = 2 if model_width % (2 * block_width) == 0 else 1
        half_width = model_width // halves
        heads_per_half = head_count // halves

        gathered_halves = []
        layouts = []
        orders = [gather_order(top_bits, half == 1) for half in range(halves)]
        shared = 1 if len(orders[0]) > 1 and all(o[0] == orders[0][0] for o in orders) else 0
        shared_bits = [[] for _ in range(3)]
        if shared:
            bit = orders[0][0]
            active = [branch for branch in range(3) if branch_bits[branch] > bit]
            outgoing = jnp.concatenate([picked[branch].reshape(-1, model_width) for branch in active])
            incoming = exchange(outgoing, bit)
            cursor = 0
            picked = list(picked)
            for branch in active:
                count = picked[branch].size // model_width
                arrived = incoming[cursor : cursor + count].reshape(picked[branch].shape)
                cursor += count
                picked[branch] = jnp.stack([picked[branch], arrived], axis=1)
                shared_bits[branch].insert(0, bit)
        for half in range(halves):
            cols = slice(half * half_width, (half + 1) * half_width)
            buffers = [block[..., cols] for block in picked]
            axis_bits = [list(bits) for bits in shared_bits]
            order = orders[half]
            for bit in order[shared:-1]:
                active = [branch for branch in range(3) if branch_bits[branch] > bit]
                outgoing = jnp.concatenate(
                    [buffers[branch].reshape(-1, half_width) for branch in active]
                )
                incoming = exchange(outgoing, bit)
                cursor = 0
                for branch in active:
                    count = buffers[branch].size // half_width
                    arrived = incoming[cursor : cursor + count].reshape(buffers[branch].shape)
                    cursor += count
                    buffers[branch] = jnp.stack([buffers[branch], arrived], axis=1)
                    axis_bits[branch].insert(0, bit)
            for branch in range(3):
                axis_bits[branch].insert(0, order[-1])
            mine = jnp.concatenate([buffers[branch].reshape(-1, half_width) for branch in range(3)])
            half_counts = [buffers[branch].size // (2 * half_width) for branch in range(3)]
            gathered_halves.append((mine, exchange(mine, order[-1]), half_counts))
            layouts.append(axis_bits)

        results = []
        full_outs = ()
        for half in range(halves):
            mine, arrived, half_counts = gathered_halves[half]
            cols = slice(half * half_width, (half + 1) * half_width)
            pairs = half_width // block_width
            key_rows_total = 2 * sum(half_counts)
            row_block = pl.BlockSpec((local_rows, block_width), lambda p, offs: (0, p))
            wide_block = pl.BlockSpec(
                (local_rows, block_width), lambda p, offs, base=half * pairs: (0, p + base)
            )
            message_block = pl.BlockSpec((key_rows_total, block_width), lambda p, offs: (0, p))
            outs = pl.pallas_call(
                attention_kernel(
                    head_dim, score_scale, half * heads_per_half, half_counts, len(full_outs)
                ),
                out_shape=(
                    jax.ShapeDtypeStruct((local_rows, model_width), jnp.bfloat16),
                    jax.ShapeDtypeStruct((local_rows, model_width), jnp.bfloat16),
                )
                + tuple(
                    jax.ShapeDtypeStruct((2, count, half_width), jnp.float32)
                    for count in half_counts
                )
                + (jax.ShapeDtypeStruct((key_rows_total, half_width), jnp.bfloat16),),
                grid_spec=pltpu.PrefetchScalarGridSpec(
                    num_scalar_prefetch=1,
                    grid=(pairs,),
                    in_specs=[row_block, row_block, message_block, message_block]
                    + [pl.BlockSpec(memory_space=pl.ANY) for _ in full_outs],
                    out_specs=[wide_block, wide_block]
                    + [
                        pl.BlockSpec((2, count, block_width), lambda p, offs: (0, 0, p))
                        for count in half_counts
                    ]
                    + [message_block],
                ),
                input_output_aliases={5 + index: index for index in range(len(full_outs))},
                compiler_params=pltpu.CompilerParams(vmem_limit_bytes=100 * 1024 * 1024),
            )(head_offsets, query_rows[:, cols], output_grad[:, cols], mine, arrived, *full_outs)
            full_outs = tuple(outs[:2])
            kept_terms = outs[2:5]
            message = outs[5]

            axis_bits = [list(bits) for bits in layouts[half]]
            order = list(reversed(gather_order(top_bits, half == 1)))
            first = order[0]
            incoming = exchange(message, first).astype(jnp.float32)
            partial = []
            cursor = 0
            for branch in range(3):
                axis_bits[branch].remove(first)
                kept = kept_terms[branch].reshape(
                    (2,) + (2,) * len(axis_bits[branch]) + (-1, half_width)
                )
                count = kept.size // half_width
                partial.append(kept + incoming[cursor : cursor + count].reshape(kept.shape))
                cursor += count
            for bit in order[1 : len(order) - shared]:
                active = [branch for branch in range(3) if branch_bits[branch] > bit]
                places = {branch: 1 + axis_bits[branch].index(bit) for branch in active}
                outgoing = jnp.concatenate(
                    [
                        lax.index_in_dim(partial[branch], 1, places[branch], keepdims=False)
                        .reshape(-1, half_width)
                        .astype(jnp.bfloat16)
                        for branch in active
                    ]
                )
                incoming = exchange(outgoing, bit).astype(jnp.float32)
                cursor = 0
                for branch in active:
                    kept = lax.index_in_dim(partial[branch], 0, places[branch], keepdims=False)
                    count = kept.size // half_width
                    partial[branch] = kept + incoming[cursor : cursor + count].reshape(kept.shape)
                    cursor += count
                    axis_bits[branch].remove(bit)
            results.append((partial, axis_bits))

        partial = [
            jnp.concatenate([result[0][branch] for result in results], axis=-1)
            for branch in range(3)
        ]
        axis_bits = results[0][1]
        if shared:
            bit = orders[0][0]
            active = [branch for branch in range(3) if branch_bits[branch] > bit]
            places = {branch: 1 + axis_bits[branch].index(bit) for branch in active}
            outgoing = jnp.concatenate(
                [
                    lax.index_in_dim(partial[branch], 1, places[branch], keepdims=False)
                    .reshape(-1, model_width)
                    .astype(jnp.bfloat16)
                    for branch in active
                ]
            )
            incoming = exchange(outgoing, bit).astype(jnp.float32)
            cursor = 0
            for branch in active:
                kept = lax.index_in_dim(partial[branch], 0, places[branch], keepdims=False)
                count = kept.size // model_width
                partial[branch] = kept + incoming[cursor : cursor + count].reshape(kept.shape)
                cursor += count
        total_grad = None
        for branch in range(3):
            spread = spread_rows(partial[branch], STRIDES[branch], head_offsets[branch])
            total_grad = spread if total_grad is None else total_grad + spread
        return full_outs + (
            total_grad[0].astype(jnp.bfloat16),
            total_grad[1].astype(jnp.bfloat16),
        )

    return per_device


def solution(mesh):
    group_count = mesh.shape["groups"]
    seq_devices = mesh.shape["seq"]

    def run(query_rows, key_rows, value_rows, output_grad, head_offsets):
        local_rows = query_rows.shape[0] // (group_count * seq_devices)
        tokens_all = seq_devices * local_rows
        seg_lengths = [min(LEN_NEAR, tokens_all), min(LEN_MID, tokens_all), min(LEN_FAR, tokens_all)]
        branch_bits = [(seg_length // local_rows).bit_length() - 1 for seg_length in seg_lengths]
        row_spec = P(("groups", "seq"), None)
        return jax.shard_map(
            make_per_device(branch_bits),
            mesh=mesh,
            in_specs=(row_spec, row_spec, row_spec, row_spec, P()),
            out_specs=(row_spec, row_spec, row_spec, row_spec),
            check_vma=False,
        )(query_rows, key_rows, value_rows, output_grad, head_offsets)

    return run
```

```python
import math

import jax
import jax.numpy as jnp
from jax import lax
from jax.experimental import pallas as pl
from jax.experimental.pallas import tpu as pltpu
from jax.sharding import PartitionSpec as P

LEN_NEAR = 1024
LEN_MID = 4096
LEN_FAR = 16384
DILATION_FIRST = 1
DILATION_SECOND = 4
DILATION_THIRD = 16

NEG_FILL = -1e30
STRIDES = (DILATION_FIRST, DILATION_SECOND, DILATION_THIRD)


def exchange(block, bit):
    count = lax.axis_size("seq")
    route = [(index, index ^ (1 << bit)) for index in range(count)]
    return lax.ppermute(block, "seq", route)


def pick_rows(rows, stride, offsets_row):
    if stride == 1:
        return rows
    pair, count, width = rows.shape
    heads = offsets_row.shape[0]
    grouped = rows.reshape(pair, count // stride, stride, heads, width // heads)
    chosen = (jnp.arange(stride, dtype=jnp.int32)[:, None] == offsets_row[None, :])[
        None, None, :, :, None
    ]
    picked = jnp.sum(jnp.where(chosen, grouped, jnp.zeros((), rows.dtype)), axis=2)
    return picked.reshape(pair, count // stride, width)


def spread_rows(picked, stride, offsets_row):
    if stride == 1:
        return picked
    pair, count, width = picked.shape
    heads = offsets_row.shape[0]
    grouped = picked.reshape(pair, count, 1, heads, width // heads)
    chosen = (jnp.arange(stride, dtype=jnp.int32)[:, None] == offsets_row[None, :]).astype(
        picked.dtype
    )[None, None, :, :, None]
    return (grouped * chosen).reshape(pair, count * stride, width)


def attention_kernel(head_dim, score_scale, head_base, half_counts, aliased):
    def kernel(offsets_ref, query_ref, grad_ref, mine_ref, arrived_ref, *refs):
        refs = refs[aliased:]
        out_ref, qgrad_ref = refs[0:2]
        keep_refs = refs[2:5]
        message_ref = refs[5]
        pair = pl.program_id(0)
        rows = query_ref.shape[0]
        heads_per_block = query_ref.shape[1] // head_dim
        for sub in range(heads_per_block):
            head = head_base + pair * heads_per_block + sub
            cols = slice(sub * head_dim, (sub + 1) * head_dim)
            query = query_ref[:, cols]
            grad = grad_ref[:, cols]
            keys = []
            values = []
            start = 0
            for count in half_counts:
                keys.append(
                    jnp.concatenate(
                        [mine_ref[start : start + count, cols], arrived_ref[start : start + count, cols]]
                    )
                )
                values.append(
                    jnp.concatenate(
                        [
                            mine_ref[start + count : start + 2 * count, cols],
                            arrived_ref[start + count : start + 2 * count, cols],
                        ]
                    )
                )
                start += 2 * count
            members = []
            scores = []
            for branch in range(3):
                block = (
                    lax.dot_general(
                        query, keys[branch], (((1,), (1,)), ((), ())),
                        preferred_element_type=jnp.float32,
                    )
                    * score_scale
                )
                if STRIDES[branch] == 1:
                    member = None
                else:
                    row_index = lax.broadcasted_iota(jnp.int32, block.shape, 0)
                    member = (row_index % STRIDES[branch]) == offsets_ref[branch, head]
                    block = jnp.where(member, block, NEG_FILL)
                members.append(member)
                scores.append(block)
            peak = jnp.max(scores[0], axis=1, keepdims=True)
            for branch in range(1, 3):
                peak = jnp.maximum(peak, jnp.max(scores[branch], axis=1, keepdims=True))
            expos = []
            for branch in range(3):
                block = jnp.exp(scores[branch] - peak)
                if members[branch] is not None:
                    block = jnp.where(members[branch], block, 0.0)
                expos.append(block)
            total = jnp.sum(expos[0], axis=1, keepdims=True)
            for branch in range(1, 3):
                total = total + jnp.sum(expos[branch], axis=1, keepdims=True)
            probs = [block / total for block in expos]
            weights = [block.astype(jnp.bfloat16) for block in probs]
            mixed = jnp.dot(weights[0], values[0], preferred_element_type=jnp.float32)
            for branch in range(1, 3):
                mixed = mixed + jnp.dot(
                    weights[branch], values[branch], preferred_element_type=jnp.float32
                )
            out_ref[:, cols] = mixed.astype(out_ref.dtype)
            balance = jnp.sum(grad.astype(jnp.float32) * mixed, axis=1, keepdims=True)
            query_grad = None
            for branch in range(3):
                flow = lax.dot_general(
                    grad, values[branch], (((1,), (1,)), ((), ())),
                    preferred_element_type=jnp.float32,
                )
                score_grad = probs[branch] * (flow - balance)
                piece = jnp.dot(
                    score_grad.astype(jnp.bfloat16), keys[branch],
                    preferred_element_type=jnp.float32,
                )
                query_grad = piece if query_grad is None else query_grad + piece
                key_terms = (
                    lax.dot_general(
                        score_grad.astype(jnp.bfloat16), query, (((0,), (0,)), ((), ())),
                        preferred_element_type=jnp.float32,
                    )
                    * score_scale
                )
                value_terms = lax.dot_general(
                    weights[branch], grad, (((0,), (0,)), ((), ())),
                    preferred_element_type=jnp.float32,
                )
                half_keys = key_terms.shape[0] // 2
                start = 2 * sum(half_counts[:branch])
                keep_refs[branch][0, :, cols] = key_terms[:half_keys]
                keep_refs[branch][1, :, cols] = value_terms[:half_keys]
                message_ref[start : start + half_keys, cols] = key_terms[half_keys:].astype(
                    message_ref.dtype
                )
                message_ref[start + half_keys : start + 2 * half_keys, cols] = value_terms[
                    half_keys:
                ].astype(message_ref.dtype)
            qgrad_ref[:, cols] = (query_grad * score_scale).astype(qgrad_ref.dtype)

    return kernel


def gather_order(top_bits, swapped):
    order = list(reversed(range(top_bits)))
    if swapped and top_bits >= 3:
        first, second = order.index(1), order.index(2)
        order[first], order[second] = order[second], order[first]
    return order


def make_per_device(branch_bits):
    top_bits = max(branch_bits)

    def per_device(query_rows, key_rows, value_rows, output_grad, head_offsets):
        local_rows, model_width = query_rows.shape
        head_count = head_offsets.shape[1]
        head_dim = model_width // head_count
        score_scale = 1.0 / math.sqrt(head_dim)
        kv_rows = jnp.stack([key_rows, value_rows])
        picked = [
            pick_rows(kv_rows, STRIDES[branch], head_offsets[branch]) for branch in range(3)
        ]
        block_width = 128 if (128 % head_dim == 0 and model_width % 128 == 0) else model_width
        halves = 2 if model_width % (2 * block_width) == 0 else 1
        half_width = model_width // halves
        heads_per_half = head_count // halves

        gathered_halves = []
        layouts = []
        orders = [gather_order(top_bits, half == 1) for half in range(halves)]
        shared = 1 if len(orders[0]) > 1 and all(o[0] == orders[0][0] for o in orders) else 0
        shared_bits = [[] for _ in range(3)]
        if shared:
            bit = orders[0][0]
            active = [branch for branch in range(3) if branch_bits[branch] > bit]
            outgoing = jnp.concatenate([picked[branch].reshape(-1, model_width) for branch in active])
            incoming = exchange(outgoing, bit)
            cursor = 0
            picked = list(picked)
            for branch in active:
                count = picked[branch].size // model_width
                arrived = incoming[cursor : cursor + count].reshape(picked[branch].shape)
                cursor += count
                picked[branch] = jnp.stack([picked[branch], arrived], axis=1)
                shared_bits[branch].insert(0, bit)
        for half in range(halves):
            cols = slice(half * half_width, (half + 1) * half_width)
            buffers = [
                jnp.stack([key_rows[:, cols], value_rows[:, cols]])
                if STRIDES[branch] == 1 and not shared_bits[branch]
                else picked[branch][..., cols]
                for branch in range(3)
            ]
            axis_bits = [list(bits) for bits in shared_bits]
            order = orders[half]
            for bit in order[shared:-1]:
                active = [branch for branch in range(3) if branch_bits[branch] > bit]
                outgoing = jnp.concatenate(
                    [buffers[branch].reshape(-1, half_width) for branch in active]
                )
                incoming = exchange(outgoing, bit)
                cursor = 0
                for branch in active:
                    count = buffers[branch].size // half_width
                    arrived = incoming[cursor : cursor + count].reshape(buffers[branch].shape)
                    cursor += count
                    buffers[branch] = jnp.stack([buffers[branch], arrived], axis=1)
                    axis_bits[branch].insert(0, bit)
            for branch in range(3):
                axis_bits[branch].insert(0, order[-1])
            mine = jnp.concatenate([buffers[branch].reshape(-1, half_width) for branch in range(3)])
            half_counts = [buffers[branch].size // (2 * half_width) for branch in range(3)]
            gathered_halves.append((mine, exchange(mine, order[-1]), half_counts))
            layouts.append(axis_bits)

        results = []
        full_outs = ()
        for half in range(halves):
            mine, arrived, half_counts = gathered_halves[half]
            cols = slice(half * half_width, (half + 1) * half_width)
            pairs = half_width // block_width
            key_rows_total = 2 * sum(half_counts)
            row_block = pl.BlockSpec((local_rows, block_width), lambda p, offs: (0, p))
            wide_block = pl.BlockSpec(
                (local_rows, block_width), lambda p, offs, base=half * pairs: (0, p + base)
            )
            message_block = pl.BlockSpec((key_rows_total, block_width), lambda p, offs: (0, p))
            outs = pl.pallas_call(
                attention_kernel(
                    head_dim, score_scale, half * heads_per_half, half_counts, len(full_outs)
                ),
                out_shape=(
                    jax.ShapeDtypeStruct((local_rows, model_width), jnp.bfloat16),
                    jax.ShapeDtypeStruct((local_rows, model_width), jnp.bfloat16),
                )
                + tuple(
                    jax.ShapeDtypeStruct((2, count, half_width), jnp.float32)
                    for count in half_counts
                )
                + (jax.ShapeDtypeStruct((key_rows_total, half_width), jnp.bfloat16),),
                grid_spec=pltpu.PrefetchScalarGridSpec(
                    num_scalar_prefetch=1,
                    grid=(pairs,),
                    in_specs=[row_block, row_block, message_block, message_block]
                    + [pl.BlockSpec(memory_space=pl.ANY) for _ in full_outs],
                    out_specs=[wide_block, wide_block]
                    + [
                        pl.BlockSpec((2, count, block_width), lambda p, offs: (0, 0, p))
                        for count in half_counts
                    ]
                    + [message_block],
                ),
                input_output_aliases={5 + index: index for index in range(len(full_outs))},
                compiler_params=pltpu.CompilerParams(vmem_limit_bytes=100 * 1024 * 1024),
            )(head_offsets, query_rows[:, cols], output_grad[:, cols], mine, arrived, *full_outs)
            full_outs = tuple(outs[:2])
            kept_terms = outs[2:5]
            message = outs[5]

            axis_bits = [list(bits) for bits in layouts[half]]
            order = list(reversed(gather_order(top_bits, half == 1)))
            first = order[0]
            incoming = exchange(message, first).astype(jnp.float32)
            partial = []
            cursor = 0
            for branch in range(3):
                axis_bits[branch].remove(first)
                kept = kept_terms[branch].reshape(
                    (2,) + (2,) * len(axis_bits[branch]) + (-1, half_width)
                )
                count = kept.size // half_width
                partial.append(kept + incoming[cursor : cursor + count].reshape(kept.shape))
                cursor += count
            for bit in order[1 : len(order) - shared]:
                active = [branch for branch in range(3) if branch_bits[branch] > bit]
                places = {branch: 1 + axis_bits[branch].index(bit) for branch in active}
                outgoing = jnp.concatenate(
                    [
                        lax.index_in_dim(partial[branch], 1, places[branch], keepdims=False)
                        .reshape(-1, half_width)
                        .astype(jnp.bfloat16)
                        for branch in active
                    ]
                )
                incoming = exchange(outgoing, bit).astype(jnp.float32)
                cursor = 0
                for branch in active:
                    kept = lax.index_in_dim(partial[branch], 0, places[branch], keepdims=False)
                    count = kept.size // half_width
                    partial[branch] = kept + incoming[cursor : cursor + count].reshape(kept.shape)
                    cursor += count
                    axis_bits[branch].remove(bit)
            results.append((partial, axis_bits))

        partial = [
            jnp.concatenate([result[0][branch] for result in results], axis=-1)
            for branch in range(3)
        ]
        axis_bits = results[0][1]
        if shared:
            bit = orders[0][0]
            active = [branch for branch in range(3) if branch_bits[branch] > bit]
            places = {branch: 1 + axis_bits[branch].index(bit) for branch in active}
            outgoing = jnp.concatenate(
                [
                    lax.index_in_dim(partial[branch], 1, places[branch], keepdims=False)
                    .reshape(-1, model_width)
                    .astype(jnp.bfloat16)
                    for branch in active
                ]
            )
            incoming = exchange(outgoing, bit).astype(jnp.float32)
            cursor = 0
            for branch in active:
                kept = lax.index_in_dim(partial[branch], 0, places[branch], keepdims=False)
                count = kept.size // model_width
                partial[branch] = kept + incoming[cursor : cursor + count].reshape(kept.shape)
                cursor += count
        total_grad = None
        for branch in range(3):
            spread = spread_rows(partial[branch], STRIDES[branch], head_offsets[branch])
            total_grad = spread if total_grad is None else total_grad + spread
        return full_outs + (
            total_grad[0].astype(jnp.bfloat16),
            total_grad[1].astype(jnp.bfloat16),
        )

    return per_device


def solution(mesh):
    group_count = mesh.shape["groups"]
    seq_devices = mesh.shape["seq"]

    def run(query_rows, key_rows, value_rows, output_grad, head_offsets):
        local_rows = query_rows.shape[0] // (group_count * seq_devices)
        tokens_all = seq_devices * local_rows
        seg_lengths = [min(LEN_NEAR, tokens_all), min(LEN_MID, tokens_all), min(LEN_FAR, tokens_all)]
        branch_bits = [(seg_length // local_rows).bit_length() - 1 for seg_length in seg_lengths]
        row_spec = P(("groups", "seq"), None)
        return jax.shard_map(
            make_per_device(branch_bits),
            mesh=mesh,
            in_specs=(row_spec, row_spec, row_spec, row_spec, P()),
            out_specs=(row_spec, row_spec, row_spec, row_spec),
            check_vma=False,
        )(query_rows, key_rows, value_rows, output_grad, head_offsets)

    return run
```

```python
import math

import jax
import jax.numpy as jnp
from jax import lax
from jax.experimental import pallas as pl
from jax.experimental.pallas import tpu as pltpu
from jax.sharding import PartitionSpec as P

LEN_NEAR = 1024
LEN_MID = 4096
LEN_FAR = 16384
DILATION_FIRST = 1
DILATION_SECOND = 4
DILATION_THIRD = 16

NEG_FILL = -1e30
STRIDES = (DILATION_FIRST, DILATION_SECOND, DILATION_THIRD)


def exchange(block, bit):
    count = lax.axis_size("seq")
    route = [(index, index ^ (1 << bit)) for index in range(count)]
    return lax.ppermute(block, "seq", route)


def pick_rows(rows, stride, offsets_row):
    if stride == 1:
        return rows
    pair, count, width = rows.shape
    heads = offsets_row.shape[0]
    grouped = rows.reshape(pair, count // stride, stride, heads, width // heads)
    chosen = (jnp.arange(stride, dtype=jnp.int32)[:, None] == offsets_row[None, :])[
        None, None, :, :, None
    ]
    picked = jnp.sum(jnp.where(chosen, grouped, jnp.zeros((), rows.dtype)), axis=2)
    return picked.reshape(pair, count // stride, width)


def spread_rows(picked, stride, offsets_row):
    if stride == 1:
        return picked
    pair, count, width = picked.shape
    heads = offsets_row.shape[0]
    grouped = picked.reshape(pair, count, 1, heads, width // heads)
    chosen = (jnp.arange(stride, dtype=jnp.int32)[:, None] == offsets_row[None, :]).astype(
        picked.dtype
    )[None, None, :, :, None]
    return (grouped * chosen).reshape(pair, count * stride, width)


def attention_kernel(head_dim, score_scale, head_base, half_counts, aliased):
    def kernel(offsets_ref, query_ref, grad_ref, mine_ref, arrived_ref, *refs):
        refs = refs[aliased:]
        out_ref, qgrad_ref = refs[0:2]
        keep_refs = refs[2:5]
        message_ref = refs[5]
        pair = pl.program_id(0)
        rows = query_ref.shape[0]
        heads_per_block = query_ref.shape[1] // head_dim
        for sub in range(heads_per_block):
            head = head_base + pair * heads_per_block + sub
            cols = slice(sub * head_dim, (sub + 1) * head_dim)
            query = query_ref[:, cols]
            grad = grad_ref[:, cols]
            keys = []
            values = []
            start = 0
            for count in half_counts:
                keys.append(
                    jnp.concatenate(
                        [mine_ref[start : start + count, cols], arrived_ref[start : start + count, cols]]
                    )
                )
                values.append(
                    jnp.concatenate(
                        [
                            mine_ref[start + count : start + 2 * count, cols],
                            arrived_ref[start + count : start + 2 * count, cols],
                        ]
                    )
                )
                start += 2 * count
            members = []
            scores = []
            for branch in range(3):
                block = (
                    lax.dot_general(
                        query, keys[branch], (((1,), (1,)), ((), ())),
                        preferred_element_type=jnp.float32,
                    )
                    * score_scale
                )
                if STRIDES[branch] == 1:
                    member = None
                else:
                    row_index = lax.broadcasted_iota(jnp.int32, block.shape, 0)
                    member = (row_index % STRIDES[branch]) == offsets_ref[branch, head]
                    block = jnp.where(member, block, NEG_FILL)
                members.append(member)
                scores.append(block)
            peak = jnp.max(scores[0], axis=1, keepdims=True)
            for branch in range(1, 3):
                peak = jnp.maximum(peak, jnp.max(scores[branch], axis=1, keepdims=True))
            expos = []
            for branch in range(3):
                expos.append(jnp.exp(scores[branch] - peak))
            total = jnp.sum(expos[0], axis=1, keepdims=True)
            for branch in range(1, 3):
                total = total + jnp.sum(expos[branch], axis=1, keepdims=True)
            probs = [block / total for block in expos]
            weights = [block.astype(jnp.bfloat16) for block in probs]
            mixed = jnp.dot(weights[0], values[0], preferred_element_type=jnp.float32)
            for branch in range(1, 3):
                mixed = mixed + jnp.dot(
                    weights[branch], values[branch], preferred_element_type=jnp.float32
                )
            out_ref[:, cols] = mixed.astype(out_ref.dtype)
            balance = jnp.sum(grad.astype(jnp.float32) * mixed, axis=1, keepdims=True)
            query_grad = None
            for branch in range(3):
                flow = lax.dot_general(
                    grad, values[branch], (((1,), (1,)), ((), ())),
                    preferred_element_type=jnp.float32,
                )
                score_grad = probs[branch] * (flow - balance)
                piece = jnp.dot(
                    score_grad.astype(jnp.bfloat16), keys[branch],
                    preferred_element_type=jnp.float32,
                )
                query_grad = piece if query_grad is None else query_grad + piece
                key_terms = (
                    lax.dot_general(
                        score_grad.astype(jnp.bfloat16), query, (((0,), (0,)), ((), ())),
                        preferred_element_type=jnp.float32,
                    )
                    * score_scale
                )
                value_terms = lax.dot_general(
                    weights[branch], grad, (((0,), (0,)), ((), ())),
                    preferred_element_type=jnp.float32,
                )
                half_keys = key_terms.shape[0] // 2
                start = 2 * sum(half_counts[:branch])
                keep_refs[branch][0, :, cols] = key_terms[:half_keys]
                keep_refs[branch][1, :, cols] = value_terms[:half_keys]
                message_ref[start : start + half_keys, cols] = key_terms[half_keys:].astype(
                    message_ref.dtype
                )
                message_ref[start + half_keys : start + 2 * half_keys, cols] = value_terms[
                    half_keys:
                ].astype(message_ref.dtype)
            qgrad_ref[:, cols] = (query_grad * score_scale).astype(qgrad_ref.dtype)

    return kernel


def gather_order(top_bits, swapped):
    order = list(reversed(range(top_bits)))
    if swapped and top_bits >= 3:
        first, second = order.index(1), order.index(2)
        order[first], order[second] = order[second], order[first]
    return order


def make_per_device(branch_bits):
    top_bits = max(branch_bits)

    def per_device(query_rows, key_rows, value_rows, output_grad, head_offsets):
        local_rows, model_width = query_rows.shape
        head_count = head_offsets.shape[1]
        head_dim = model_width // head_count
        score_scale = 1.0 / math.sqrt(head_dim)
        kv_rows = jnp.stack([key_rows, value_rows])
        picked = [
            pick_rows(kv_rows, STRIDES[branch], head_offsets[branch]) for branch in range(3)
        ]
        block_width = 128 if (128 % head_dim == 0 and model_width % 128 == 0) else model_width
        halves = 2 if model_width % (2 * block_width) == 0 else 1
        half_width = model_width // halves
        heads_per_half = head_count // halves

        gathered_halves = []
        layouts = []
        orders = [gather_order(top_bits, half == 1) for half in range(halves)]
        shared = 1 if len(orders[0]) > 1 and all(o[0] == orders[0][0] for o in orders) else 0
        shared_bits = [[] for _ in range(3)]
        if shared:
            bit = orders[0][0]
            active = [branch for branch in range(3) if branch_bits[branch] > bit]
            outgoing = jnp.concatenate([picked[branch].reshape(-1, model_width) for branch in active])
            incoming = exchange(outgoing, bit)
            cursor = 0
            picked = list(picked)
            for branch in active:
                count = picked[branch].size // model_width
                arrived = incoming[cursor : cursor + count].reshape(picked[branch].shape)
                cursor += count
                picked[branch] = jnp.stack([picked[branch], arrived], axis=1)
                shared_bits[branch].insert(0, bit)
        for half in range(halves):
            cols = slice(half * half_width, (half + 1) * half_width)
            buffers = [block[..., cols] for block in picked]
            axis_bits = [list(bits) for bits in shared_bits]
            order = orders[half]
            for bit in order[shared:-1]:
                active = [branch for branch in range(3) if branch_bits[branch] > bit]
                outgoing = jnp.concatenate(
                    [buffers[branch].reshape(-1, half_width) for branch in active]
                )
                incoming = exchange(outgoing, bit)
                cursor = 0
                for branch in active:
                    count = buffers[branch].size // half_width
                    arrived = incoming[cursor : cursor + count].reshape(buffers[branch].shape)
                    cursor += count
                    buffers[branch] = jnp.stack([buffers[branch], arrived], axis=1)
                    axis_bits[branch].insert(0, bit)
            for branch in range(3):
                axis_bits[branch].insert(0, order[-1])
            mine = jnp.concatenate([buffers[branch].reshape(-1, half_width) for branch in range(3)])
            half_counts = [buffers[branch].size // (2 * half_width) for branch in range(3)]
            gathered_halves.append((mine, exchange(mine, order[-1]), half_counts))
            layouts.append(axis_bits)

        results = []
        full_outs = ()
        for half in range(halves):
            mine, arrived, half_counts = gathered_halves[half]
            cols = slice(half * half_width, (half + 1) * half_width)
            pairs = half_width // block_width
            key_rows_total = 2 * sum(half_counts)
            row_block = pl.BlockSpec((local_rows, block_width), lambda p, offs: (0, p))
            wide_block = pl.BlockSpec(
                (local_rows, block_width), lambda p, offs, base=half * pairs: (0, p + base)
            )
            message_block = pl.BlockSpec((key_rows_total, block_width), lambda p, offs: (0, p))
            outs = pl.pallas_call(
                attention_kernel(
                    head_dim, score_scale, half * heads_per_half, half_counts, len(full_outs)
                ),
                out_shape=(
                    jax.ShapeDtypeStruct((local_rows, model_width), jnp.bfloat16),
                    jax.ShapeDtypeStruct((local_rows, model_width), jnp.bfloat16),
                )
                + tuple(
                    jax.ShapeDtypeStruct((2, count, half_width), jnp.float32)
                    for count in half_counts
                )
                + (jax.ShapeDtypeStruct((key_rows_total, half_width), jnp.bfloat16),),
                grid_spec=pltpu.PrefetchScalarGridSpec(
                    num_scalar_prefetch=1,
                    grid=(pairs,),
                    in_specs=[row_block, row_block, message_block, message_block]
                    + [pl.BlockSpec(memory_space=pl.ANY) for _ in full_outs],
                    out_specs=[wide_block, wide_block]
                    + [
                        pl.BlockSpec((2, count, block_width), lambda p, offs: (0, 0, p))
                        for count in half_counts
                    ]
                    + [message_block],
                ),
                input_output_aliases={5 + index: index for index in range(len(full_outs))},
                compiler_params=pltpu.CompilerParams(vmem_limit_bytes=100 * 1024 * 1024),
            )(head_offsets, query_rows[:, cols], output_grad[:, cols], mine, arrived, *full_outs)
            full_outs = tuple(outs[:2])
            kept_terms = outs[2:5]
            message = outs[5]

            axis_bits = [list(bits) for bits in layouts[half]]
            order = list(reversed(gather_order(top_bits, half == 1)))
            first = order[0]
            incoming = exchange(message, first).astype(jnp.float32)
            partial = []
            cursor = 0
            for branch in range(3):
                axis_bits[branch].remove(first)
                kept = kept_terms[branch].reshape(
                    (2,) + (2,) * len(axis_bits[branch]) + (-1, half_width)
                )
                count = kept.size // half_width
                partial.append(kept + incoming[cursor : cursor + count].reshape(kept.shape))
                cursor += count
            for bit in order[1 : len(order) - shared]:
                active = [branch for branch in range(3) if branch_bits[branch] > bit]
                places = {branch: 1 + axis_bits[branch].index(bit) for branch in active}
                outgoing = jnp.concatenate(
                    [
                        lax.index_in_dim(partial[branch], 1, places[branch], keepdims=False)
                        .reshape(-1, half_width)
                        .astype(jnp.bfloat16)
                        for branch in active
                    ]
                )
                incoming = exchange(outgoing, bit).astype(jnp.float32)
                cursor = 0
                for branch in active:
                    kept = lax.index_in_dim(partial[branch], 0, places[branch], keepdims=False)
                    count = kept.size // half_width
                    partial[branch] = kept + incoming[cursor : cursor + count].reshape(kept.shape)
                    cursor += count
                    axis_bits[branch].remove(bit)
            results.append((partial, axis_bits))

        partial = [
            jnp.concatenate([result[0][branch] for result in results], axis=-1)
            for branch in range(3)
        ]
        axis_bits = results[0][1]
        if shared:
            bit = orders[0][0]
            active = [branch for branch in range(3) if branch_bits[branch] > bit]
            places = {branch: 1 + axis_bits[branch].index(bit) for branch in active}
            outgoing = jnp.concatenate(
                [
                    lax.index_in_dim(partial[branch], 1, places[branch], keepdims=False)
                    .reshape(-1, model_width)
                    .astype(jnp.bfloat16)
                    for branch in active
                ]
            )
            incoming = exchange(outgoing, bit).astype(jnp.float32)
            cursor = 0
            for branch in active:
                kept = lax.index_in_dim(partial[branch], 0, places[branch], keepdims=False)
                count = kept.size // model_width
                partial[branch] = kept + incoming[cursor : cursor + count].reshape(kept.shape)
                cursor += count
        total_grad = None
        for branch in range(3):
            spread = spread_rows(partial[branch], STRIDES[branch], head_offsets[branch])
            total_grad = spread if total_grad is None else total_grad + spread
        return full_outs + (
            total_grad[0].astype(jnp.bfloat16),
            total_grad[1].astype(jnp.bfloat16),
        )

    return per_device


def solution(mesh):
    group_count = mesh.shape["groups"]
    seq_devices = mesh.shape["seq"]

    def run(query_rows, key_rows, value_rows, output_grad, head_offsets):
        local_rows = query_rows.shape[0] // (group_count * seq_devices)
        tokens_all = seq_devices * local_rows
        seg_lengths = [min(LEN_NEAR, tokens_all), min(LEN_MID, tokens_all), min(LEN_FAR, tokens_all)]
        branch_bits = [(seg_length // local_rows).bit_length() - 1 for seg_length in seg_lengths]
        row_spec = P(("groups", "seq"), None)
        return jax.shard_map(
            make_per_device(branch_bits),
            mesh=mesh,
            in_specs=(row_spec, row_spec, row_spec, row_spec, P()),
            out_specs=(row_spec, row_spec, row_spec, row_spec),
            check_vma=False,
        )(query_rows, key_rows, value_rows, output_grad, head_offsets)

    return run
```

```python
import math

import jax
import jax.numpy as jnp
from jax import lax
from jax.experimental import pallas as pl
from jax.experimental.pallas import tpu as pltpu
from jax.sharding import PartitionSpec as P

LEN_NEAR = 1024
LEN_MID = 4096
LEN_FAR = 16384
DILATION_FIRST = 1
DILATION_SECOND = 4
DILATION_THIRD = 16

NEG_FILL = -1e30
STRIDES = (DILATION_FIRST, DILATION_SECOND, DILATION_THIRD)


def exchange(block, bit):
    count = lax.axis_size("seq")
    route = [(index, index ^ (1 << bit)) for index in range(count)]
    return lax.ppermute(block, "seq", route)


def pick_rows(rows, stride, offsets_row):
    if stride == 1:
        return rows
    pair, count, width = rows.shape
    heads = offsets_row.shape[0]
    grouped = rows.reshape(pair, count // stride, stride, heads, width // heads)
    chosen = (jnp.arange(stride, dtype=jnp.int32)[:, None] == offsets_row[None, :])[
        None, None, :, :, None
    ]
    picked = jnp.sum(jnp.where(chosen, grouped, jnp.zeros((), rows.dtype)), axis=2)
    return picked.reshape(pair, count // stride, width)


def spread_rows(picked, stride, offsets_row):
    if stride == 1:
        return picked
    pair, count, width = picked.shape
    heads = offsets_row.shape[0]
    grouped = picked.reshape(pair, count, 1, heads, width // heads)
    chosen = (jnp.arange(stride, dtype=jnp.int32)[:, None] == offsets_row[None, :]).astype(
        picked.dtype
    )[None, None, :, :, None]
    return (grouped * chosen).reshape(pair, count * stride, width)


def attention_kernel(head_dim, score_scale, head_base, half_counts, aliased):
    def kernel(offsets_ref, query_ref, grad_ref, mine_ref, arrived_ref, *refs):
        refs = refs[aliased:]
        out_ref, qgrad_ref = refs[0:2]
        keep_refs = refs[2:5]
        message_ref = refs[5]
        pair = pl.program_id(0)
        rows = query_ref.shape[0]
        heads_per_block = query_ref.shape[1] // head_dim
        for sub in range(heads_per_block):
            head = head_base + pair * heads_per_block + sub
            cols = slice(sub * head_dim, (sub + 1) * head_dim)
            query = query_ref[:, cols]
            grad = grad_ref[:, cols]
            keys = []
            values = []
            start = 0
            for count in half_counts:
                keys.append(
                    jnp.concatenate(
                        [mine_ref[start : start + count, cols], arrived_ref[start : start + count, cols]]
                    )
                )
                values.append(
                    jnp.concatenate(
                        [
                            mine_ref[start + count : start + 2 * count, cols],
                            arrived_ref[start + count : start + 2 * count, cols],
                        ]
                    )
                )
                start += 2 * count
            members = []
            scores = []
            for branch in range(3):
                block = (
                    lax.dot_general(
                        query, keys[branch], (((1,), (1,)), ((), ())),
                        preferred_element_type=jnp.float32,
                    )
                    * score_scale
                )
                if STRIDES[branch] == 1:
                    member = None
                else:
                    row_index = lax.broadcasted_iota(jnp.int32, block.shape, 0)
                    member = (row_index % STRIDES[branch]) == offsets_ref[branch, head]
                    block = jnp.where(member, block, NEG_FILL)
                members.append(member)
                scores.append(block)
            peak = jnp.max(scores[0], axis=1, keepdims=True)
            for branch in range(1, 3):
                peak = jnp.maximum(peak, jnp.max(scores[branch], axis=1, keepdims=True))
            expos = []
            for branch in range(3):
                expos.append(jnp.exp(scores[branch] - peak))
            total = jnp.sum(expos[0], axis=1, keepdims=True)
            for branch in range(1, 3):
                total = total + jnp.sum(expos[branch], axis=1, keepdims=True)
            probs = [block / total for block in expos]
            weights = [block.astype(jnp.bfloat16) for block in probs]
            mixed = jnp.dot(weights[0], values[0], preferred_element_type=jnp.float32)
            for branch in range(1, 3):
                mixed = mixed + jnp.dot(
                    weights[branch], values[branch], preferred_element_type=jnp.float32
                )
            out_ref[:, cols] = mixed.astype(out_ref.dtype)
            balance = jnp.sum(grad.astype(jnp.float32) * mixed, axis=1, keepdims=True)
            query_grad = None
            for branch in range(3):
                flow = lax.dot_general(
                    grad, values[branch], (((1,), (1,)), ((), ())),
                    preferred_element_type=jnp.float32,
                )
                score_grad = probs[branch] * (flow - balance)
                piece = jnp.dot(
                    score_grad.astype(jnp.bfloat16), keys[branch],
                    preferred_element_type=jnp.float32,
                )
                query_grad = piece if query_grad is None else query_grad + piece
                key_terms = (
                    lax.dot_general(
                        score_grad.astype(jnp.bfloat16), query, (((0,), (0,)), ((), ())),
                        preferred_element_type=jnp.float32,
                    )
                    * score_scale
                )
                value_terms = lax.dot_general(
                    weights[branch], grad, (((0,), (0,)), ((), ())),
                    preferred_element_type=jnp.float32,
                )
                half_keys = key_terms.shape[0] // 2
                start = 2 * sum(half_counts[:branch])
                keep_refs[branch][0, :, cols] = key_terms[:half_keys]
                keep_refs[branch][1, :, cols] = value_terms[:half_keys]
                message_ref[start : start + half_keys, cols] = key_terms[half_keys:].astype(
                    message_ref.dtype
                )
                message_ref[start + half_keys : start + 2 * half_keys, cols] = value_terms[
                    half_keys:
                ].astype(message_ref.dtype)
            qgrad_ref[:, cols] = (query_grad * score_scale).astype(qgrad_ref.dtype)

    return kernel


def gather_order(top_bits, swapped):
    order = list(reversed(range(top_bits)))
    if swapped and top_bits >= 3:
        first, second = order.index(1), order.index(2)
        order[first], order[second] = order[second], order[first]
    return order


def make_per_device(branch_bits):
    top_bits = max(branch_bits)

    def per_device(query_rows, key_rows, value_rows, output_grad, head_offsets):
        local_rows, model_width = query_rows.shape
        head_count = head_offsets.shape[1]
        head_dim = model_width // head_count
        score_scale = 1.0 / math.sqrt(head_dim)
        kv_rows = jnp.stack([key_rows, value_rows])
        picked = [
            pick_rows(kv_rows, STRIDES[branch], head_offsets[branch]) for branch in range(3)
        ]
        block_width = 128 if (128 % head_dim == 0 and model_width % 128 == 0) else model_width
        halves = 2 if model_width % (2 * block_width) == 0 else 1
        half_width = model_width // halves
        heads_per_half = head_count // halves

        gathered_halves = []
        layouts = []
        orders = [gather_order(top_bits, half == 1) for half in range(halves)]
        shared = 1 if len(orders[0]) > 1 and all(o[0] == orders[0][0] for o in orders) else 0
        shared_bits = [[] for _ in range(3)]
        if shared:
            bit = orders[0][0]
            active = [branch for branch in range(3) if branch_bits[branch] > bit]
            outgoing = jnp.concatenate([picked[branch].reshape(-1, model_width) for branch in active])
            incoming = exchange(outgoing, bit)
            cursor = 0
            picked = list(picked)
            for branch in active:
                count = picked[branch].size // model_width
                arrived = incoming[cursor : cursor + count].reshape(picked[branch].shape)
                cursor += count
                picked[branch] = jnp.stack([picked[branch], arrived], axis=1)
                shared_bits[branch].insert(0, bit)
        for half in range(halves):
            cols = slice(half * half_width, (half + 1) * half_width)
            buffers = [block[..., cols] for block in picked]
            axis_bits = [list(bits) for bits in shared_bits]
            order = orders[half]
            for bit in order[shared:-1]:
                active = [branch for branch in range(3) if branch_bits[branch] > bit]
                outgoing = jnp.concatenate(
                    [buffers[branch].reshape(-1, half_width) for branch in active]
                )
                incoming = exchange(outgoing, bit)
                cursor = 0
                for branch in active:
                    count = buffers[branch].size // half_width
                    arrived = incoming[cursor : cursor + count].reshape(buffers[branch].shape)
                    cursor += count
                    buffers[branch] = jnp.stack([buffers[branch], arrived], axis=1)
                    axis_bits[branch].insert(0, bit)
            for branch in range(3):
                axis_bits[branch].insert(0, order[-1])
            mine = jnp.concatenate([buffers[branch].reshape(-1, half_width) for branch in range(3)])
            half_counts = [buffers[branch].size // (2 * half_width) for branch in range(3)]
            gathered_halves.append((mine, exchange(mine, order[-1]), half_counts))
            layouts.append(axis_bits)

        results = []
        full_outs = ()
        for half in range(halves):
            mine, arrived, half_counts = gathered_halves[half]
            cols = slice(half * half_width, (half + 1) * half_width)
            pairs = half_width // block_width
            key_rows_total = 2 * sum(half_counts)
            row_block = pl.BlockSpec((local_rows, block_width), lambda p, offs: (0, p))
            wide_block = pl.BlockSpec(
                (local_rows, block_width), lambda p, offs, base=half * pairs: (0, p + base)
            )
            message_block = pl.BlockSpec((key_rows_total, block_width), lambda p, offs: (0, p))
            outs = pl.pallas_call(
                attention_kernel(
                    head_dim, score_scale, half * heads_per_half, half_counts, len(full_outs)
                ),
                out_shape=(
                    jax.ShapeDtypeStruct((local_rows, model_width), jnp.bfloat16),
                    jax.ShapeDtypeStruct((local_rows, model_width), jnp.bfloat16),
                )
                + tuple(
                    jax.ShapeDtypeStruct((2, count, half_width), jnp.float32)
                    for count in half_counts
                )
                + (jax.ShapeDtypeStruct((key_rows_total, half_width), jnp.bfloat16),),
                grid_spec=pltpu.PrefetchScalarGridSpec(
                    num_scalar_prefetch=1,
                    grid=(pairs,),
                    in_specs=[row_block, row_block, message_block, message_block]
                    + [pl.BlockSpec(memory_space=pl.ANY) for _ in full_outs],
                    out_specs=[wide_block, wide_block]
                    + [
                        pl.BlockSpec((2, count, block_width), lambda p, offs: (0, 0, p))
                        for count in half_counts
                    ]
                    + [message_block],
                ),
                input_output_aliases={5 + index: index for index in range(len(full_outs))},
                compiler_params=pltpu.CompilerParams(vmem_limit_bytes=100 * 1024 * 1024),
            )(head_offsets, query_rows[:, cols], output_grad[:, cols], mine, arrived, *full_outs)
            full_outs = tuple(outs[:2])
            kept_terms = outs[2:5]
            message = outs[5]

            axis_bits = [list(bits) for bits in layouts[half]]
            order = list(reversed(gather_order(top_bits, half == 1)))
            first = order[0]
            incoming = exchange(message, first).astype(jnp.float32)
            partial = []
            cursor = 0
            for branch in range(3):
                axis_bits[branch].remove(first)
                kept = kept_terms[branch].reshape(
                    (2,) + (2,) * len(axis_bits[branch]) + (-1, half_width)
                )
                count = kept.size // half_width
                partial.append((kept, incoming[cursor : cursor + count].reshape(kept.shape)))
                cursor += count

            def take(pair, index, place):
                return tuple(lax.index_in_dim(part, index, place, keepdims=False) for part in pair)

            for bit in order[1 : len(order) - shared]:
                active = [branch for branch in range(3) if branch_bits[branch] > bit]
                places = {branch: 1 + axis_bits[branch].index(bit) for branch in active}
                outgoing = jnp.concatenate(
                    [
                        sum(take(partial[branch], 1, places[branch]))
                        .reshape(-1, half_width)
                        .astype(jnp.bfloat16)
                        for branch in active
                    ]
                )
                incoming = exchange(outgoing, bit).astype(jnp.float32)
                cursor = 0
                for branch in active:
                    kept = sum(take(partial[branch], 0, places[branch]))
                    count = kept.size // half_width
                    partial[branch] = (kept, incoming[cursor : cursor + count].reshape(kept.shape))
                    cursor += count
                    axis_bits[branch].remove(bit)
            results.append(([pair[0] + pair[1] for pair in partial], axis_bits))

        partial = [
            jnp.concatenate([result[0][branch] for result in results], axis=-1)
            for branch in range(3)
        ]
        axis_bits = results[0][1]
        if shared:
            bit = orders[0][0]
            active = [branch for branch in range(3) if branch_bits[branch] > bit]
            places = {branch: 1 + axis_bits[branch].index(bit) for branch in active}
            outgoing = jnp.concatenate(
                [
                    lax.index_in_dim(partial[branch], 1, places[branch], keepdims=False)
                    .reshape(-1, model_width)
                    .astype(jnp.bfloat16)
                    for branch in active
                ]
            )
            incoming = exchange(outgoing, bit).astype(jnp.float32)
            cursor = 0
            for branch in active:
                kept = lax.index_in_dim(partial[branch], 0, places[branch], keepdims=False)
                count = kept.size // model_width
                partial[branch] = kept + incoming[cursor : cursor + count].reshape(kept.shape)
                cursor += count
        total_grad = None
        for branch in range(3):
            spread = spread_rows(partial[branch], STRIDES[branch], head_offsets[branch])
            total_grad = spread if total_grad is None else total_grad + spread
        return full_outs + (
            total_grad[0].astype(jnp.bfloat16),
            total_grad[1].astype(jnp.bfloat16),
        )

    return per_device


def solution(mesh):
    group_count = mesh.shape["groups"]
    seq_devices = mesh.shape["seq"]

    def run(query_rows, key_rows, value_rows, output_grad, head_offsets):
        local_rows = query_rows.shape[0] // (group_count * seq_devices)
        tokens_all = seq_devices * local_rows
        seg_lengths = [min(LEN_NEAR, tokens_all), min(LEN_MID, tokens_all), min(LEN_FAR, tokens_all)]
        branch_bits = [(seg_length // local_rows).bit_length() - 1 for seg_length in seg_lengths]
        row_spec = P(("groups", "seq"), None)
        return jax.shard_map(
            make_per_device(branch_bits),
            mesh=mesh,
            in_specs=(row_spec, row_spec, row_spec, row_spec, P()),
            out_specs=(row_spec, row_spec, row_spec, row_spec),
            check_vma=False,
        )(query_rows, key_rows, value_rows, output_grad, head_offsets)

    return run
```
